32 devices in a mesh: dp: 8 (over y, x, core), tensor: 4 (over z).
Axes of the slice: x: 2, y: 2, z: 4, core: 2. Of those that a mesh axis runs over, the one named last changes fastest.
Arguments:
- inputs: bfloat16 [4096, 2048], P('dp'), may hold values from -6 to 6
- active: int32 [4096], P('dp'), may hold values from 0 to 1, as said below
- block_table: int32 [16], replicated, may hold values from 0 to 15, as said below
- gain_one: bfloat16 [2048], replicated, may hold values from 0.099609375 to 1.8984375
- w_query: bfloat16 [2048, 2048], P(None, 'tensor'), may hold values from -0.125 to 0.125
- w_key: bfloat16 [2048, 1024], P(None, 'tensor'), may hold values from -0.125 to 0.125
- w_value: bfloat16 [2048, 1024], P(None, 'tensor'), may hold values from -0.125 to 0.125
- w_out: bfloat16 [2048, 2048], P('tensor'), may hold values from -4 to 4
- gain_two: bfloat16 [2048], replicated, may hold values from 0.099609375 to 1.8984375
- w_gate: bfloat16 [2048, 5632], P(None, 'tensor'), may hold values from -0.125 to 0.125
- w_up: bfloat16 [2048, 5632], P(None, 'tensor'), may hold values from -0.125 to 0.125
- w_down: bfloat16 [5632, 2048], P('tensor'), may hold values from -0.078125 to 0.078125
- cotangent: bfloat16 [4096, 2048], P('dp'), may hold values from -6 to 6
Outputs:
- output: bfloat16 [4096, 2048], P('dp')
- grad_input: float32 [4096, 2048], P('dp')
- grad_gain_one: float32 [2048], replicated
- grad_w_query: float32 [2048, 2048], P(None, 'tensor')
- grad_w_key: float32 [2048, 1024], P(None, 'tensor')
- grad_w_value: float32 [2048, 1024], P(None, 'tensor')
- grad_w_out: float32 [2048, 2048], P('tensor')
- grad_gain_two: float32 [2048], replicated
- grad_w_gate: float32 [2048, 5632], P(None, 'tensor')
- grad_w_up: float32 [2048, 5632], P(None, 'tensor')
- grad_w_down: float32 [5632, 2048], P('tensor')
The draws below stay inside these ranges and needn't reach their ends.
Inputs may be any that keep to these rules, and one draw needn't show every extreme that they name: `active`: 0 or 1 for every token; the share of 1s differs from one causal block to another. `block_table`: each causal block appears once; entries 2i and 2i+1 sum to 15.
All inputs are finite; a program needn't handle non-finite values.
Results may differ from the reference program's by a relative error of at most 0.014.
Values may be sent and summed in bfloat16 or wider, within the bound.
No kernel may reach another device: no remote copies, remote signals or barrier semaphores. Data moves between devices by JAX's collectives and lax.ppermute only.
A program may use at most 256 MiB of HBM per device.

```python
import jax
import jax.numpy as jnp
from jax import lax

D = 2048
HEADS = 16
KV_HEADS = 8
HEAD_DIM = 128
FF = 5632
GROUP = 2
LENGTH = 4096
BLOCK_ROWS = 256
BLOCKS = 16


def draw_active(key, part):
    rate_key = jax.random.fold_in(key, 11)
    cell_key = jax.random.fold_in(key, 12)
    rates = jax.random.randint(rate_key, (BLOCKS, 1), 30, 95, dtype=jnp.int32)
    draws = jax.random.randint(cell_key, (BLOCKS, BLOCK_ROWS), 0, 100, dtype=jnp.int32)
    return (draws < rates).astype(jnp.int32).reshape(LENGTH)


def draw_block_table(key, part):
    order = jax.random.permutation(jax.random.fold_in(key, 21), BLOCKS // 2).astype(jnp.int32)
    return jnp.stack([order, BLOCKS - 1 - order], axis=1).reshape(BLOCKS).astype(jnp.int32)


def block_levels(key, dims, pieces, low, high):
    def one(position, shards_of):
        steps = jax.random.uniform(jax.random.fold_in(jax.random.fold_in(key, 6), position), (shards_of,), jnp.float32, low / len(pieces), high / len(pieces))
        return jnp.repeat(jnp.exp(steps), dims[position] // shards_of).reshape((-1,) + (1,) * (len(dims) - position - 1))

    level = one(*pieces[0])
    for cut in pieces[1:]:
        level = level * one(*cut)
    return level


def centred(key, dims, scale, reach, cuts=(), kind=jnp.bfloat16):
    values = scale * jax.random.normal(key, dims, jnp.float32)
    if cuts:
        values = values * block_levels(key, dims, cuts, -0.22, 0.18)
    return jnp.clip(values, -reach, reach).astype(kind)


def setup_inputs(seed: int = 0) -> dict:
    key_of = jax.random.split(jax.random.key(seed), 14)
    return {
        "inputs": centred(key_of[0], (LENGTH, D), 1.0, 6.0, ((0, 8),)),
        "active": draw_active(jax.random.fold_in(key_of[13], 71), 0),
        "block_table": draw_block_table(jax.random.fold_in(key_of[13], 71), 0),
        "gain_one": jnp.clip(1.0 + 0.18 * jax.random.normal(key_of[3], (D,), jnp.float32), 0.099609375, 1.8984375).astype(jnp.bfloat16),
        "w_query": centred(key_of[4], (D, HEADS * HEAD_DIM), D ** -0.5, 0.125, ((1, 4),)),
        "w_key": centred(key_of[5], (D, KV_HEADS * HEAD_DIM), D ** -0.5, 0.125, ((1, 4),)),
        "w_value": centred(key_of[6], (D, KV_HEADS * HEAD_DIM), D ** -0.5, 0.125, ((1, 4),)),
        "w_out": centred(key_of[7], (HEADS * HEAD_DIM, D), (max(HEADS * HEAD_DIM * 4 // LENGTH, 1)) ** -0.5, 4.0, ((0, 4),)),
        "gain_two": jnp.clip(1.0 + 0.18 * jax.random.normal(key_of[8], (D,), jnp.float32), 0.099609375, 1.8984375).astype(jnp.bfloat16),
        "w_gate": centred(key_of[9], (D, FF), D ** -0.5, 0.125, ((1, 4),)),
        "w_up": centred(key_of[10], (D, FF), D ** -0.5, 0.125, ((1, 4),)),
        "w_down": centred(key_of[11], (FF, D), FF ** -0.5, 0.078125, ((0, 4),)),
        "cotangent": centred(key_of[12], (LENGTH, D), 1.0, 6.0, ((0, 8),)),
    }


EPS = 1e-05
MASKED_SCORE = -1e+30

@jax.custom_vjp
def low(v):
    return lax.optimization_barrier(v.astype(jnp.bfloat16)).astype(jnp.float32)

@jax.custom_vjp
def low_back(v):
    return v

def low_keep(v):
    return (low(v), None)

def low_pass(kept, grad):
    return (grad,)

def back_keep(v):
    return (v, None)

def back_low(kept, grad):
    return (low(grad),)
low.defvjp(low_keep, low_pass)
low_back.defvjp(back_keep, back_low)

def matmul(left, right):
    return jnp.dot(left, right, precision=lax.Precision.HIGHEST)

def rms_norm(values, scales):
    return values * lax.rsqrt(lax.optimization_barrier(jnp.mean(values * values, axis=-1, keepdims=True)) + EPS) * scales

def rotate(values, cos_table, sin_table):
    middle = values.shape[-1] // 2
    leading = values[..., :middle]
    trailing = values[..., middle:]
    return jnp.concatenate([leading * cos_table - trailing * sin_table, trailing * cos_table + leading * sin_table], axis=-1)

def angles_of(positions):
    frequency = 10000.0 ** (-jnp.arange(0, HEAD_DIM, 2, dtype=jnp.float32) / HEAD_DIM)
    angles = positions.astype(jnp.float32)[:, None] * frequency[None, :]
    return (jnp.cos(angles)[:, None, :], jnp.sin(angles)[:, None, :])

def reference(inputs, active, block_table, gain_one, w_query, w_key, w_value, w_out, gain_two, w_gate, w_up, w_down, cotangent):
    positions = (block_table[:, None] * BLOCK_ROWS + jnp.arange(BLOCK_ROWS, dtype=jnp.int32)[None, :]).reshape(LENGTH)
    keep_rows = active.astype(jnp.float32)[:, None]
    alive = active > 0
    cos_table, sin_table = angles_of(positions)
    query_block = min(512, LENGTH)
    score_scale = HEAD_DIM ** (-0.5)
    slot_ids = jnp.arange(LENGTH, dtype=jnp.int32)

    def forward_layer(source, gain_a, query_w, key_w, value_w, out_w, gain_b, gate_w, up_w, down_w):
        normed = low(rms_norm(source, gain_a))
        queries = low_back(matmul(normed, query_w)).reshape(LENGTH, HEADS, HEAD_DIM)
        keys = low_back(matmul(normed, key_w)).reshape(LENGTH, KV_HEADS, HEAD_DIM)
        values = low(low_back(matmul(normed, value_w))).reshape(LENGTH, KV_HEADS, HEAD_DIM)
        queries = low(rotate(queries, cos_table, sin_table))
        keys = low(rotate(keys, cos_table, sin_table))
        keys = jnp.repeat(keys, GROUP, axis=1)
        values = jnp.repeat(values, GROUP, axis=1)

        def attend(row_start):
            rows_q = lax.dynamic_slice_in_dim(queries, row_start, query_block, 0)
            rows_pos = lax.dynamic_slice_in_dim(positions, row_start, query_block, 0)
            own_ids = row_start + jnp.arange(query_block, dtype=jnp.int32)
            scores = low_back(jnp.einsum('qhd,khd->hqk', rows_q, keys, precision=lax.Precision.HIGHEST) * score_scale)
            allowed = (positions[None, :] <= rows_pos[:, None]) & (alive[None, :] | (slot_ids[None, :] == own_ids[:, None]))
            scores = jnp.where(allowed[None], scores, MASKED_SCORE)
            row_max = lax.optimization_barrier(jnp.max(scores, axis=-1, keepdims=True))
            shifted = jnp.exp(scores - row_max)
            probs = low(shifted / lax.optimization_barrier(jnp.sum(shifted, axis=-1, keepdims=True)))
            return jnp.einsum('hqk,khd->qhd', probs, values, precision=lax.Precision.HIGHEST)
        starts = jnp.arange(0, LENGTH, query_block, dtype=jnp.int32)
        mixed = lax.map(jax.checkpoint(attend), starts).reshape(LENGTH, HEADS * HEAD_DIM)
        attended = low(low_back(mixed))
        branch = low_back(matmul(attended, out_w))
        middle = source + keep_rows * branch
        normed_two = low(rms_norm(middle, gain_b))
        gate_value = low_back(matmul(normed_two, gate_w))
        up_value = low_back(matmul(normed_two, up_w))
        hidden = low(jax.nn.silu(gate_value) * up_value)
        return middle + keep_rows * low_back(matmul(hidden, down_w))
    result, pullback = jax.vjp(forward_layer, inputs.astype(jnp.float32), gain_one.astype(jnp.float32), w_query.astype(jnp.float32), w_key.astype(jnp.float32), w_value.astype(jnp.float32), w_out.astype(jnp.float32), gain_two.astype(jnp.float32), w_gate.astype(jnp.float32), w_up.astype(jnp.float32), w_down.astype(jnp.float32))
    grads = pullback(cotangent.astype(jnp.float32))
    return (result.astype(jnp.bfloat16), grads[0], grads[1], grads[2], grads[3], grads[4], grads[5], grads[6], grads[7], grads[8], grads[9])
```

```python
import jax
import jax.numpy as jnp
from jax import lax
from jax.sharding import PartitionSpec as P

HEAD_DIM = 128


EPS = 1e-05
MASKED_SCORE = -1e30


def rms_norm(values, scales):
    return values * lax.rsqrt(jnp.mean(values * values, axis=-1, keepdims=True) + EPS) * scales


def rotate(values, cos_table, sin_table):
    middle = values.shape[-1] // 2
    leading = values[..., :middle]
    trailing = values[..., middle:]
    return jnp.concatenate(
        [leading * cos_table - trailing * sin_table, trailing * cos_table + leading * sin_table],
        axis=-1,
    )


def angles_of(positions, head_size):
    frequency = 10000.0 ** (-jnp.arange(0, head_size, 2, dtype=jnp.float32) / head_size)
    angles = positions.astype(jnp.float32)[:, None] * frequency[None, :]
    return (jnp.cos(angles)[:, None, :], jnp.sin(angles)[:, None, :])


def swiglu(gate_value, up_value):
    return jax.nn.silu(gate_value) * up_value


def left_trans(left, right):
    return lax.dot_general(
        left, right, (((0,), (0,)), ((), ())), preferred_element_type=jnp.float32
    )


def right_trans(left, right):
    return lax.dot_general(
        left, right, (((1,), (1,)), ((), ())), preferred_element_type=jnp.float32
    )


def on_device(
    inputs,
    active,
    block_table,
    gain_one,
    w_query,
    w_key,
    w_value,
    w_out,
    gain_two,
    w_gate,
    w_up,
    w_down,
    cotangent,
):
    row_count = inputs.shape[0]
    local_heads = w_query.shape[1] // HEAD_DIM
    local_groups = w_key.shape[1] // HEAD_DIM
    group_size = local_heads // local_groups
    half_rows = row_count // 2
    length = row_count * lax.axis_size("dp")
    score_scale = HEAD_DIM ** (-0.5)
    key_pos = (
        block_table[:, None] * half_rows + jnp.arange(half_rows, dtype=jnp.int32)[None, :]
    ).reshape(length)
    row_start = lax.axis_index("dp") * row_count
    query_pos = lax.dynamic_slice_in_dim(key_pos, row_start, row_count)
    slot_ids = jnp.arange(length, dtype=jnp.int32)
    own_ids = row_start + jnp.arange(row_count, dtype=jnp.int32)
    cos_table, sin_table = angles_of(query_pos, HEAD_DIM)
    keep_rows = active.astype(jnp.float32)[:, None]
    source = inputs.astype(jnp.float32)
    normed_full, norm_one_back = jax.vjp(rms_norm, source, gain_one.astype(jnp.float32))
    normed = normed_full.astype(jnp.bfloat16)
    query_raw = jnp.dot(normed, w_query, preferred_element_type=jnp.float32).reshape(
        row_count, local_heads, HEAD_DIM
    )
    key_raw = jnp.dot(normed, w_key, preferred_element_type=jnp.float32).reshape(
        row_count, local_groups, HEAD_DIM
    )
    value_low = jnp.dot(normed, w_value, preferred_element_type=jnp.float32).astype(jnp.bfloat16)
    query_low = (
        rotate(query_raw, cos_table, sin_table)
        .reshape(row_count, local_heads * HEAD_DIM)
        .astype(jnp.bfloat16)
    )
    key_low = (
        rotate(key_raw, cos_table, sin_table)
        .reshape(row_count, local_groups * HEAD_DIM)
        .astype(jnp.bfloat16)
    )
    alive_low = active.astype(jnp.bfloat16)

    def allowed_of(alive_all):
        return (key_pos[None, :] <= query_pos[:, None]) & (
            (alive_all[None, :] > 0) | (slot_ids[None, :] == own_ids[:, None])
        )

    def head_scores(head_index, keys_all, allowed):
        query_part = query_low[:, head_index * HEAD_DIM : (head_index + 1) * HEAD_DIM]
        group_index = head_index // group_size
        key_part = keys_all[:, group_index * HEAD_DIM : (group_index + 1) * HEAD_DIM]
        raw_scores = right_trans(query_part, key_part) * score_scale
        return jnp.where(allowed, raw_scores, MASKED_SCORE)

    kv_width = local_groups * HEAD_DIM
    all_kv = lax.all_gather(
        jnp.concatenate([key_low, value_low], axis=1), "dp", axis=0, tiled=True
    )
    all_keys = all_kv[:, :kv_width]
    all_values = all_kv[:, kv_width:]
    all_alive = lax.all_gather(alive_low, "dp", axis=0, tiled=True)
    allowed_fwd = allowed_of(all_alive)
    mixed_parts = []
    lse_parts = []
    for head_index in range(local_heads):
        masked = head_scores(head_index, all_keys, allowed_fwd)
        row_max = jnp.max(masked, axis=1, keepdims=True)
        shifted = jnp.exp(masked - row_max)
        row_total = jnp.sum(shifted, axis=1, keepdims=True)
        probs_low = (shifted / row_total).astype(jnp.bfloat16)
        lse_parts.append(row_max + jnp.log(row_total))
        group_index = head_index // group_size
        value_part = all_values[:, group_index * HEAD_DIM : (group_index + 1) * HEAD_DIM]
        mixed_parts.append(jnp.dot(probs_low, value_part, preferred_element_type=jnp.float32))
    attended = jnp.concatenate(mixed_parts, axis=1).astype(jnp.bfloat16)
    branch = lax.psum(
        jnp.dot(attended, w_out, preferred_element_type=jnp.float32).astype(jnp.bfloat16), "tensor"
    ).astype(jnp.float32)
    middle = source + keep_rows * branch
    normed_two_full, norm_two_back = jax.vjp(rms_norm, middle, gain_two.astype(jnp.float32))
    normed_two = normed_two_full.astype(jnp.bfloat16)
    gate_value = jnp.dot(normed_two, w_gate, preferred_element_type=jnp.float32)
    up_value = jnp.dot(normed_two, w_up, preferred_element_type=jnp.float32)
    hidden_full, swiglu_back = jax.vjp(swiglu, gate_value, up_value)
    hidden = hidden_full.astype(jnp.bfloat16)
    down_sum = lax.psum(
        jnp.dot(hidden, w_down, preferred_element_type=jnp.float32).astype(jnp.bfloat16), "tensor"
    ).astype(jnp.float32)
    output = (middle + keep_rows * down_sum).astype(jnp.bfloat16)
    grad_out = cotangent.astype(jnp.float32)
    d_down = (keep_rows * grad_out).astype(jnp.bfloat16)
    grad_w_down = left_trans(hidden, d_down)
    d_hidden = right_trans(d_down, w_down)
    d_gate_full, d_up_full = swiglu_back(d_hidden)
    d_gate = d_gate_full.astype(jnp.bfloat16)
    d_up = d_up_full.astype(jnp.bfloat16)
    grad_w_gate = left_trans(normed_two, d_gate)
    grad_w_up = left_trans(normed_two, d_up)
    d_normed_two = lax.psum(
        (right_trans(d_gate, w_gate) + right_trans(d_up, w_up)).astype(jnp.bfloat16), "tensor"
    ).astype(jnp.float32)
    d_middle_norm, grad_gain_two = norm_two_back(d_normed_two)
    grad_middle = grad_out + d_middle_norm
    d_branch = (keep_rows * grad_middle).astype(jnp.bfloat16)
    grad_w_out = left_trans(attended, d_branch)
    d_attended = right_trans(d_branch, w_out).astype(jnp.bfloat16)
    back_keys, back_values = all_keys, all_values
    allowed_back = allowed_fwd
    d_query_parts = []
    d_key_parts = [
        jnp.zeros((length, HEAD_DIM), jnp.float32) for group_index in range(local_groups)
    ]
    d_value_parts = [
        jnp.zeros((length, HEAD_DIM), jnp.float32) for group_index in range(local_groups)
    ]
    for head_index in range(local_heads):
        group_index = head_index // group_size
        masked = head_scores(head_index, back_keys, allowed_back)
        probs = jnp.where(allowed_back, jnp.exp(masked - lse_parts[head_index]), 0.0)
        probs_low = probs.astype(jnp.bfloat16)
        d_out_part = d_attended[:, head_index * HEAD_DIM : (head_index + 1) * HEAD_DIM]
        key_part = back_keys[:, group_index * HEAD_DIM : (group_index + 1) * HEAD_DIM]
        value_part = back_values[:, group_index * HEAD_DIM : (group_index + 1) * HEAD_DIM]
        query_part = query_low[:, head_index * HEAD_DIM : (head_index + 1) * HEAD_DIM]
        d_probs = right_trans(d_out_part, value_part)
        row_delta = jnp.sum(probs * d_probs, axis=1, keepdims=True)
        d_scores = (probs * (d_probs - row_delta)).astype(jnp.bfloat16)
        d_query_parts.append(
            jnp.dot(d_scores, key_part, preferred_element_type=jnp.float32) * score_scale
        )
        d_key_parts[group_index] = (
            d_key_parts[group_index] + left_trans(d_scores, query_part) * score_scale
        )
        d_value_parts[group_index] = d_value_parts[group_index] + left_trans(probs_low, d_out_part)
    d_key_all = jnp.concatenate(d_key_parts, axis=1)
    d_value_all = jnp.concatenate(d_value_parts, axis=1)
    d_kv_own = lax.psum_scatter(
        jnp.concatenate([d_key_all, d_value_all], axis=1).astype(jnp.bfloat16),
        "dp",
        scatter_dimension=0,
        tiled=True,
    ).astype(jnp.float32)
    d_key_own = d_kv_own[:, :kv_width]
    d_value_own = d_kv_own[:, kv_width:]
    d_queries = jnp.concatenate(d_query_parts, axis=1).reshape(row_count, local_heads, HEAD_DIM)
    d_query_low = (
        rotate(d_queries, cos_table, -sin_table)
        .reshape(row_count, local_heads * HEAD_DIM)
        .astype(jnp.bfloat16)
    )
    d_key_low = (
        rotate(d_key_own.reshape(row_count, local_groups, HEAD_DIM), cos_table, -sin_table)
        .reshape(row_count, local_groups * HEAD_DIM)
        .astype(jnp.bfloat16)
    )
    d_value_low = d_value_own.astype(jnp.bfloat16)
    grad_w_query = left_trans(normed, d_query_low)
    grad_w_key = left_trans(normed, d_key_low)
    grad_w_value = left_trans(normed, d_value_low)
    d_normed_part = (
        right_trans(d_query_low, w_query)
        + right_trans(d_key_low, w_key)
        + right_trans(d_value_low, w_value)
    )
    d_normed = lax.psum(d_normed_part.astype(jnp.bfloat16), "tensor").astype(jnp.float32)
    d_source_norm, grad_gain_one = norm_one_back(d_normed)
    grad_input = grad_middle + d_source_norm
    grad_gain_one, grad_gain_two = lax.psum((grad_gain_one, grad_gain_two), "dp")
    (
        grad_w_query,
        grad_w_key,
        grad_w_value,
        grad_w_out,
        grad_w_gate,
        grad_w_up,
        grad_w_down,
    ) = [
        lax.psum(grad.astype(jnp.bfloat16), "dp").astype(jnp.float32)
        for grad in (
            grad_w_query,
            grad_w_key,
            grad_w_value,
            grad_w_out,
            grad_w_gate,
            grad_w_up,
            grad_w_down,
        )
    ]
    return (
        output,
        grad_input,
        grad_gain_one,
        grad_w_query,
        grad_w_key,
        grad_w_value,
        grad_w_out,
        grad_gain_two,
        grad_w_gate,
        grad_w_up,
        grad_w_down,
    )


def solution(mesh):
    placed = (
        P("dp", None),
        P("dp"),
        P(),
        P(),
        P(None, "tensor"),
        P(None, "tensor"),
        P(None, "tensor"),
        P("tensor", None),
        P(),
        P(None, "tensor"),
        P(None, "tensor"),
        P("tensor", None),
        P("dp", None),
    )
    return jax.shard_map(
        on_device,
        mesh=mesh,
        in_specs=placed,
        out_specs=(
            P("dp", None),
            P("dp", None),
            P(),
            P(None, "tensor"),
            P(None, "tensor"),
            P(None, "tensor"),
            P("tensor", None),
            P(),
            P(None, "tensor"),
            P(None, "tensor"),
            P("tensor", None),
        ),
        check_vma=False,
    )
```

```python
import jax
import jax.numpy as jnp
from jax import lax
from jax.sharding import PartitionSpec as P

HEAD_DIM = 128


EPS = 1e-05
MASKED_SCORE = -1e30


def rms_norm(values, scales):
    return values * lax.rsqrt(jnp.mean(values * values, axis=-1, keepdims=True) + EPS) * scales


def rotate(values, cos_table, sin_table):
    middle = values.shape[-1] // 2
    leading = values[..., :middle]
    trailing = values[..., middle:]
    return jnp.concatenate(
        [leading * cos_table - trailing * sin_table, trailing * cos_table + leading * sin_table],
        axis=-1,
    )


def angles_of(positions, head_size):
    frequency = 10000.0 ** (-jnp.arange(0, head_size, 2, dtype=jnp.float32) / head_size)
    angles = positions.astype(jnp.float32)[:, None] * frequency[None, :]
    return (jnp.cos(angles)[:, None, :], jnp.sin(angles)[:, None, :])


def swiglu(gate_value, up_value):
    return jax.nn.silu(gate_value) * up_value


def left_trans(left, right):
    return lax.dot_general(
        left, right, (((0,), (0,)), ((), ())), preferred_element_type=jnp.float32
    )


def right_trans(left, right):
    return lax.dot_general(
        left, right, (((1,), (1,)), ((), ())), preferred_element_type=jnp.float32
    )


def partner_perm(axis_size, mask):
    return [(index, index ^ mask) for index in range(axis_size)]


def permute_sum(parts, dims, axis):
    size = lax.axis_size(axis)
    steps = size.bit_length() - 1
    assert 1 << steps == size
    me = lax.axis_index(axis)
    pieces = list(parts)
    for step in range(steps):
        bit = (me >> step) & 1
        keep, send = [], []
        for piece, dim in zip(pieces, dims):
            half = piece.shape[dim] // 2
            keep.append(lax.dynamic_slice_in_dim(piece, bit * half, half, axis=dim))
            send.append(
                lax.dynamic_slice_in_dim(piece, (1 - bit) * half, half, axis=dim).astype(jnp.bfloat16)
            )
        got = lax.ppermute(send, axis, partner_perm(size, 1 << step))
        pieces = [mine + theirs.astype(jnp.float32) for mine, theirs in zip(keep, got)]
    pieces = [piece.astype(jnp.bfloat16) for piece in pieces]
    for step in reversed(range(steps)):
        first = ((me >> step) & 1) == 0
        got = lax.ppermute(pieces, axis, partner_perm(size, 1 << step))
        pieces = [
            jnp.concatenate(
                [jnp.where(first, mine, theirs), jnp.where(first, theirs, mine)], axis=dim
            )
            for mine, theirs, dim in zip(pieces, got, dims)
        ]
    return [piece.astype(jnp.float32) for piece in pieces]


def permute_allsum(value, axis):
    size = lax.axis_size(axis)
    steps = size.bit_length() - 1
    for step in range(steps):
        value = value + lax.ppermute(value, axis, partner_perm(size, 1 << step))
    return value


def on_device(
    inputs,
    active,
    block_table,
    gain_one,
    w_query,
    w_key,
    w_value,
    w_out,
    gain_two,
    w_gate,
    w_up,
    w_down,
    cotangent,
):
    row_count = inputs.shape[0]
    local_heads = w_query.shape[1] // HEAD_DIM
    local_groups = w_key.shape[1] // HEAD_DIM
    group_size = local_heads // local_groups
    half_rows = row_count // 2
    length = row_count * lax.axis_size("dp")
    score_scale = HEAD_DIM ** (-0.5)
    key_pos = (
        block_table[:, None] * half_rows + jnp.arange(half_rows, dtype=jnp.int32)[None, :]
    ).reshape(length)
    row_start = lax.axis_index("dp") * row_count
    query_pos = lax.dynamic_slice_in_dim(key_pos, row_start, row_count)
    slot_ids = jnp.arange(length, dtype=jnp.int32)
    own_ids = row_start + jnp.arange(row_count, dtype=jnp.int32)
    cos_table, sin_table = angles_of(query_pos, HEAD_DIM)
    keep_rows = active.astype(jnp.float32)[:, None]
    source = inputs.astype(jnp.float32)
    normed_full, norm_one_back = jax.vjp(rms_norm, source, gain_one.astype(jnp.float32))
    normed = normed_full.astype(jnp.bfloat16)
    query_raw = jnp.dot(normed, w_query, preferred_element_type=jnp.float32).reshape(
        row_count, local_heads, HEAD_DIM
    )
    key_raw = jnp.dot(normed, w_key, preferred_element_type=jnp.float32).reshape(
        row_count, local_groups, HEAD_DIM
    )
    value_low = jnp.dot(normed, w_value, preferred_element_type=jnp.float32).astype(jnp.bfloat16)
    query_low = (
        rotate(query_raw, cos_table, sin_table)
        .reshape(row_count, local_heads * HEAD_DIM)
        .astype(jnp.bfloat16)
    )
    key_low = (
        rotate(key_raw, cos_table, sin_table)
        .reshape(row_count, local_groups * HEAD_DIM)
        .astype(jnp.bfloat16)
    )
    alive_low = active.astype(jnp.bfloat16)

    def allowed_of(alive_all):
        return (key_pos[None, :] <= query_pos[:, None]) & (
            (alive_all[None, :] > 0) | (slot_ids[None, :] == own_ids[:, None])
        )

    def head_scores(head_index, keys_all, allowed):
        query_part = query_low[:, head_index * HEAD_DIM : (head_index + 1) * HEAD_DIM]
        group_index = head_index // group_size
        key_part = keys_all[:, group_index * HEAD_DIM : (group_index + 1) * HEAD_DIM]
        raw_scores = right_trans(query_part, key_part) * score_scale
        return jnp.where(allowed, raw_scores, MASKED_SCORE)

    kv_width = local_groups * HEAD_DIM
    all_kv = lax.all_gather(
        jnp.concatenate([key_low, value_low], axis=1), "dp", axis=0, tiled=True
    )
    all_keys = all_kv[:, :kv_width]
    all_values = all_kv[:, kv_width:]
    all_alive = lax.all_gather(alive_low, "dp", axis=0, tiled=True)
    allowed_fwd = allowed_of(all_alive)
    mixed_parts = []
    lse_parts = []
    for head_index in range(local_heads):
        masked = head_scores(head_index, all_keys, allowed_fwd)
        row_max = jnp.max(masked, axis=1, keepdims=True)
        shifted = jnp.exp(masked - row_max)
        row_total = jnp.sum(shifted, axis=1, keepdims=True)
        probs_low = (shifted / row_total).astype(jnp.bfloat16)
        lse_parts.append(row_max + jnp.log(row_total))
        group_index = head_index // group_size
        value_part = all_values[:, group_index * HEAD_DIM : (group_index + 1) * HEAD_DIM]
        mixed_parts.append(jnp.dot(probs_low, value_part, preferred_element_type=jnp.float32))
    attended = jnp.concatenate(mixed_parts, axis=1).astype(jnp.bfloat16)
    branch = lax.psum(
        jnp.dot(attended, w_out, preferred_element_type=jnp.float32).astype(jnp.bfloat16), "tensor"
    ).astype(jnp.float32)
    middle = source + keep_rows * branch
    normed_two_full, norm_two_back = jax.vjp(rms_norm, middle, gain_two.astype(jnp.float32))
    normed_two = normed_two_full.astype(jnp.bfloat16)
    gate_value = jnp.dot(normed_two, w_gate, preferred_element_type=jnp.float32)
    up_value = jnp.dot(normed_two, w_up, preferred_element_type=jnp.float32)
    hidden_full, swiglu_back = jax.vjp(swiglu, gate_value, up_value)
    hidden = hidden_full.astype(jnp.bfloat16)
    down_sum = lax.psum(
        jnp.dot(hidden, w_down, preferred_element_type=jnp.float32).astype(jnp.bfloat16), "tensor"
    ).astype(jnp.float32)
    output = (middle + keep_rows * down_sum).astype(jnp.bfloat16)
    grad_out = cotangent.astype(jnp.float32)
    d_down = (keep_rows * grad_out).astype(jnp.bfloat16)
    grad_w_down = left_trans(hidden, d_down)
    d_hidden = right_trans(d_down, w_down)
    d_gate_full, d_up_full = swiglu_back(d_hidden)
    d_gate = d_gate_full.astype(jnp.bfloat16)
    d_up = d_up_full.astype(jnp.bfloat16)
    grad_w_gate = left_trans(normed_two, d_gate)
    grad_w_up = left_trans(normed_two, d_up)
    d_normed_two = lax.psum(
        (right_trans(d_gate, w_gate) + right_trans(d_up, w_up)).astype(jnp.bfloat16), "tensor"
    ).astype(jnp.float32)
    d_middle_norm, grad_gain_two = norm_two_back(d_normed_two)
    grad_middle = grad_out + d_middle_norm
    d_branch = (keep_rows * grad_middle).astype(jnp.bfloat16)
    grad_w_out = left_trans(attended, d_branch)
    d_attended = right_trans(d_branch, w_out).astype(jnp.bfloat16)
    back_keys, back_values = all_keys, all_values
    allowed_back = allowed_fwd
    d_query_parts = []
    d_key_parts = [
        jnp.zeros((length, HEAD_DIM), jnp.float32) for group_index in range(local_groups)
    ]
    d_value_parts = [
        jnp.zeros((length, HEAD_DIM), jnp.float32) for group_index in range(local_groups)
    ]
    for head_index in range(local_heads):
        group_index = head_index // group_size
        masked = head_scores(head_index, back_keys, allowed_back)
        probs = jnp.where(allowed_back, jnp.exp(masked - lse_parts[head_index]), 0.0)
        probs_low = probs.astype(jnp.bfloat16)
        d_out_part = d_attended[:, head_index * HEAD_DIM : (head_index + 1) * HEAD_DIM]
        key_part = back_keys[:, group_index * HEAD_DIM : (group_index + 1) * HEAD_DIM]
        value_part = back_values[:, group_index * HEAD_DIM : (group_index + 1) * HEAD_DIM]
        query_part = query_low[:, head_index * HEAD_DIM : (head_index + 1) * HEAD_DIM]
        d_probs = right_trans(d_out_part, value_part)
        row_delta = jnp.sum(probs * d_probs, axis=1, keepdims=True)
        d_scores = (probs * (d_probs - row_delta)).astype(jnp.bfloat16)
        d_query_parts.append(
            jnp.dot(d_scores, key_part, preferred_element_type=jnp.float32) * score_scale
        )
        d_key_parts[group_index] = (
            d_key_parts[group_index] + left_trans(d_scores, query_part) * score_scale
        )
        d_value_parts[group_index] = d_value_parts[group_index] + left_trans(probs_low, d_out_part)
    d_key_all = jnp.concatenate(d_key_parts, axis=1)
    d_value_all = jnp.concatenate(d_value_parts, axis=1)
    d_kv_own = lax.psum_scatter(
        jnp.concatenate([d_key_all, d_value_all], axis=1).astype(jnp.bfloat16),
        "dp",
        scatter_dimension=0,
        tiled=True,
    ).astype(jnp.float32)
    d_key_own = d_kv_own[:, :kv_width]
    d_value_own = d_kv_own[:, kv_width:]
    d_queries = jnp.concatenate(d_query_parts, axis=1).reshape(row_count, local_heads, HEAD_DIM)
    d_query_low = (
        rotate(d_queries, cos_table, -sin_table)
        .reshape(row_count, local_heads * HEAD_DIM)
        .astype(jnp.bfloat16)
    )
    d_key_low = (
        rotate(d_key_own.reshape(row_count, local_groups, HEAD_DIM), cos_table, -sin_table)
        .reshape(row_count, local_groups * HEAD_DIM)
        .astype(jnp.bfloat16)
    )
    d_value_low = d_value_own.astype(jnp.bfloat16)
    grad_w_query = left_trans(normed, d_query_low)
    grad_w_key = left_trans(normed, d_key_low)
    grad_w_value = left_trans(normed, d_value_low)
    d_normed_part = (
        right_trans(d_query_low, w_query)
        + right_trans(d_key_low, w_key)
        + right_trans(d_value_low, w_value)
    )
    d_normed = lax.psum(d_normed_part.astype(jnp.bfloat16), "tensor").astype(jnp.float32)
    d_source_norm, grad_gain_one = norm_one_back(d_normed)
    grad_input = grad_middle + d_source_norm
    grad_gain_one = permute_allsum(grad_gain_one, "dp")
    grad_gain_two = permute_allsum(grad_gain_two, "dp")
    grad_w_gate, grad_w_up, grad_w_down = permute_sum(
        [grad_w_gate, grad_w_up, grad_w_down], [0, 0, 1], "dp"
    )
    (grad_w_out,) = permute_sum([grad_w_out], [1], "dp")
    grad_w_query, grad_w_key, grad_w_value = permute_sum(
        [grad_w_query, grad_w_key, grad_w_value], [0, 0, 0], "dp"
    )
    return (
        output,
        grad_input,
        grad_gain_one,
        grad_w_query,
        grad_w_key,
        grad_w_value,
        grad_w_out,
        grad_gain_two,
        grad_w_gate,
        grad_w_up,
        grad_w_down,
    )


def solution(mesh):
    placed = (
        P("dp", None),
        P("dp"),
        P(),
        P(),
        P(None, "tensor"),
        P(None, "tensor"),
        P(None, "tensor"),
        P("tensor", None),
        P(),
        P(None, "tensor"),
        P(None, "tensor"),
        P("tensor", None),
        P("dp", None),
    )
    return jax.shard_map(
        on_device,
        mesh=mesh,
        in_specs=placed,
        out_specs=(
            P("dp", None),
            P("dp", None),
            P(),
            P(None, "tensor"),
            P(None, "tensor"),
            P(None, "tensor"),
            P("tensor", None),
            P(),
            P(None, "tensor"),
            P(None, "tensor"),
            P("tensor", None),
        ),
        check_vma=False,
    )
```

```python
import jax
import jax.numpy as jnp
from jax import lax
from jax.sharding import PartitionSpec as P

HEAD_DIM = 128


EPS = 1e-05
MASKED_SCORE = -1e30


def rms_norm(values, scales):
    return values * lax.rsqrt(jnp.mean(values * values, axis=-1, keepdims=True) + EPS) * scales


def rotate(values, cos_table, sin_table):
    middle = values.shape[-1] // 2
    leading = values[..., :middle]
    trailing = values[..., middle:]
    return jnp.concatenate(
        [leading * cos_table - trailing * sin_table, trailing * cos_table + leading * sin_table],
        axis=-1,
    )


def angles_of(positions, head_size):
    frequency = 10000.0 ** (-jnp.arange(0, head_size, 2, dtype=jnp.float32) / head_size)
    angles = positions.astype(jnp.float32)[:, None] * frequency[None, :]
    return (jnp.cos(angles)[:, None, :], jnp.sin(angles)[:, None, :])


def swiglu(gate_value, up_value):
    return jax.nn.silu(gate_value) * up_value


def left_trans(left, right):
    return lax.dot_general(
        left, right, (((0,), (0,)), ((), ())), preferred_element_type=jnp.float32
    )


def right_trans(left, right):
    return lax.dot_general(
        left, right, (((1,), (1,)), ((), ())), preferred_element_type=jnp.float32
    )


def partner_perm(axis_size, mask):
    return [(index, index ^ mask) for index in range(axis_size)]


def permute_sum(parts, dims, axis):
    size = lax.axis_size(axis)
    steps = size.bit_length() - 1
    assert 1 << steps == size
    me = lax.axis_index(axis)
    pieces = list(parts)
    for step in range(steps):
        bit = (me >> step) & 1
        keep, send = [], []
        for piece, dim in zip(pieces, dims):
            half = piece.shape[dim] // 2
            keep.append(lax.dynamic_slice_in_dim(piece, bit * half, half, axis=dim))
            send.append(
                lax.dynamic_slice_in_dim(piece, (1 - bit) * half, half, axis=dim).astype(jnp.bfloat16)
            )
        got = lax.ppermute(send, axis, partner_perm(size, 1 << step))
        pieces = [mine + theirs.astype(jnp.float32) for mine, theirs in zip(keep, got)]
    pieces = [piece.astype(jnp.bfloat16) for piece in pieces]
    for step in reversed(range(steps)):
        first = ((me >> step) & 1) == 0
        got = lax.ppermute(pieces, axis, partner_perm(size, 1 << step))
        pieces = [
            jnp.concatenate(
                [jnp.where(first, mine, theirs), jnp.where(first, theirs, mine)], axis=dim
            )
            for mine, theirs, dim in zip(pieces, got, dims)
        ]
    return [piece.astype(jnp.float32) for piece in pieces]


def permute_allsum(value, axis):
    size = lax.axis_size(axis)
    steps = size.bit_length() - 1
    for step in range(steps):
        value = value + lax.ppermute(value, axis, partner_perm(size, 1 << step))
    return value


def on_device(
    inputs,
    active,
    block_table,
    gain_one,
    w_query,
    w_key,
    w_value,
    w_out,
    gain_two,
    w_gate,
    w_up,
    w_down,
    cotangent,
):
    row_count = inputs.shape[0]
    local_heads = w_query.shape[1] // HEAD_DIM
    local_groups = w_key.shape[1] // HEAD_DIM
    group_size = local_heads // local_groups
    half_rows = row_count // 2
    length = row_count * lax.axis_size("dp")
    score_scale = HEAD_DIM ** (-0.5)
    key_pos = (
        block_table[:, None] * half_rows + jnp.arange(half_rows, dtype=jnp.int32)[None, :]
    ).reshape(length)
    row_start = lax.axis_index("dp") * row_count
    query_pos = lax.dynamic_slice_in_dim(key_pos, row_start, row_count)
    slot_ids = jnp.arange(length, dtype=jnp.int32)
    own_ids = row_start + jnp.arange(row_count, dtype=jnp.int32)
    cos_table, sin_table = angles_of(query_pos, HEAD_DIM)
    keep_rows = active.astype(jnp.float32)[:, None]
    source = inputs.astype(jnp.float32)
    normed_full, norm_one_back = jax.vjp(rms_norm, source, gain_one.astype(jnp.float32))
    normed = normed_full.astype(jnp.bfloat16)
    query_raw = jnp.dot(normed, w_query, preferred_element_type=jnp.float32).reshape(
        row_count, local_heads, HEAD_DIM
    )
    key_raw = jnp.dot(normed, w_key, preferred_element_type=jnp.float32).reshape(
        row_count, local_groups, HEAD_DIM
    )
    value_low = jnp.dot(normed, w_value, preferred_element_type=jnp.float32).astype(jnp.bfloat16)
    query_low = (
        rotate(query_raw, cos_table, sin_table)
        .reshape(row_count, local_heads * HEAD_DIM)
        .astype(jnp.bfloat16)
    )
    key_low = (
        rotate(key_raw, cos_table, sin_table)
        .reshape(row_count, local_groups * HEAD_DIM)
        .astype(jnp.bfloat16)
    )
    alive_low = active.astype(jnp.bfloat16)

    def allowed_of(alive_all):
        return (key_pos[None, :] <= query_pos[:, None]) & (
            (alive_all[None, :] > 0) | (slot_ids[None, :] == own_ids[:, None])
        )

    def head_scores(head_index, keys_all, allowed):
        query_part = query_low[:, head_index * HEAD_DIM : (head_index + 1) * HEAD_DIM]
        group_index = head_index // group_size
        key_part = keys_all[:, group_index * HEAD_DIM : (group_index + 1) * HEAD_DIM]
        raw_scores = right_trans(query_part, key_part) * score_scale
        return jnp.where(allowed, raw_scores, MASKED_SCORE)

    kv_width = local_groups * HEAD_DIM
    all_kv = lax.all_gather(
        jnp.concatenate([key_low, value_low], axis=1), "dp", axis=0, tiled=True
    )
    all_keys = all_kv[:, :kv_width]
    all_values = all_kv[:, kv_width:]
    all_alive = lax.all_gather(alive_low, "dp", axis=0, tiled=True)
    allowed_fwd = allowed_of(all_alive)
    mixed_parts = []
    lse_parts = []
    for head_index in range(local_heads):
        masked = head_scores(head_index, all_keys, allowed_fwd)
        row_max = jnp.max(masked, axis=1, keepdims=True)
        shifted = jnp.exp(masked - row_max)
        row_total = jnp.sum(shifted, axis=1, keepdims=True)
        probs_low = (shifted / row_total).astype(jnp.bfloat16)
        lse_parts.append(row_max + jnp.log(row_total))
        group_index = head_index // group_size
        value_part = all_values[:, group_index * HEAD_DIM : (group_index + 1) * HEAD_DIM]
        mixed_parts.append(jnp.dot(probs_low, value_part, preferred_element_type=jnp.float32))
    attended = jnp.concatenate(mixed_parts, axis=1).astype(jnp.bfloat16)
    (branch,) = permute_sum(
        [jnp.dot(attended, w_out, preferred_element_type=jnp.float32)], [0], "tensor"
    )
    middle = source + keep_rows * branch
    normed_two_full, norm_two_back = jax.vjp(rms_norm, middle, gain_two.astype(jnp.float32))
    normed_two = normed_two_full.astype(jnp.bfloat16)
    gate_value = jnp.dot(normed_two, w_gate, preferred_element_type=jnp.float32)
    up_value = jnp.dot(normed_two, w_up, preferred_element_type=jnp.float32)
    hidden_full, swiglu_back = jax.vjp(swiglu, gate_value, up_value)
    hidden = hidden_full.astype(jnp.bfloat16)
    (down_sum,) = permute_sum(
        [jnp.dot(hidden, w_down, preferred_element_type=jnp.float32)], [0], "tensor"
    )
    output = (middle + keep_rows * down_sum).astype(jnp.bfloat16)
    grad_out = cotangent.astype(jnp.float32)
    d_down = (keep_rows * grad_out).astype(jnp.bfloat16)
    grad_w_down = left_trans(hidden, d_down)
    d_hidden = right_trans(d_down, w_down)
    d_gate_full, d_up_full = swiglu_back(d_hidden)
    d_gate = d_gate_full.astype(jnp.bfloat16)
    d_up = d_up_full.astype(jnp.bfloat16)
    grad_w_gate = left_trans(normed_two, d_gate)
    grad_w_up = left_trans(normed_two, d_up)
    (d_normed_two,) = permute_sum(
        [right_trans(d_gate, w_gate) + right_trans(d_up, w_up)], [0], "tensor"
    )
    d_middle_norm, grad_gain_two = norm_two_back(d_normed_two)
    grad_middle = grad_out + d_middle_norm
    d_branch = (keep_rows * grad_middle).astype(jnp.bfloat16)
    grad_w_out = left_trans(attended, d_branch)
    d_attended = right_trans(d_branch, w_out).astype(jnp.bfloat16)
    back_keys, back_values = all_keys, all_values
    allowed_back = allowed_fwd
    d_query_parts = []
    d_key_parts = [
        jnp.zeros((length, HEAD_DIM), jnp.float32) for group_index in range(local_groups)
    ]
    d_value_parts = [
        jnp.zeros((length, HEAD_DIM), jnp.float32) for group_index in range(local_groups)
    ]
    for head_index in range(local_heads):
        group_index = head_index // group_size
        masked = head_scores(head_index, back_keys, allowed_back)
        probs = jnp.where(allowed_back, jnp.exp(masked - lse_parts[head_index]), 0.0)
        probs_low = probs.astype(jnp.bfloat16)
        d_out_part = d_attended[:, head_index * HEAD_DIM : (head_index + 1) * HEAD_DIM]
        key_part = back_keys[:, group_index * HEAD_DIM : (group_index + 1) * HEAD_DIM]
        value_part = back_values[:, group_index * HEAD_DIM : (group_index + 1) * HEAD_DIM]
        query_part = query_low[:, head_index * HEAD_DIM : (head_index + 1) * HEAD_DIM]
        d_probs = right_trans(d_out_part, value_part)
        row_delta = jnp.sum(probs * d_probs, axis=1, keepdims=True)
        d_scores = (probs * (d_probs - row_delta)).astype(jnp.bfloat16)
        d_query_parts.append(
            jnp.dot(d_scores, key_part, preferred_element_type=jnp.float32) * score_scale
        )
        d_key_parts[group_index] = (
            d_key_parts[group_index] + left_trans(d_scores, query_part) * score_scale
        )
        d_value_parts[group_index] = d_value_parts[group_index] + left_trans(probs_low, d_out_part)
    d_key_all = jnp.concatenate(d_key_parts, axis=1)
    d_value_all = jnp.concatenate(d_value_parts, axis=1)
    d_kv_own = lax.psum_scatter(
        jnp.concatenate([d_key_all, d_value_all], axis=1).astype(jnp.bfloat16),
        "dp",
        scatter_dimension=0,
        tiled=True,
    ).astype(jnp.float32)
    d_key_own = d_kv_own[:, :kv_width]
    d_value_own = d_kv_own[:, kv_width:]
    d_queries = jnp.concatenate(d_query_parts, axis=1).reshape(row_count, local_heads, HEAD_DIM)
    d_query_low = (
        rotate(d_queries, cos_table, -sin_table)
        .reshape(row_count, local_heads * HEAD_DIM)
        .astype(jnp.bfloat16)
    )
    d_key_low = (
        rotate(d_key_own.reshape(row_count, local_groups, HEAD_DIM), cos_table, -sin_table)
        .reshape(row_count, local_groups * HEAD_DIM)
        .astype(jnp.bfloat16)
    )
    d_value_low = d_value_own.astype(jnp.bfloat16)
    grad_w_query = left_trans(normed, d_query_low)
    grad_w_key = left_trans(normed, d_key_low)
    grad_w_value = left_trans(normed, d_value_low)
    d_normed_part = (
        right_trans(d_query_low, w_query)
        + right_trans(d_key_low, w_key)
        + right_trans(d_value_low, w_value)
    )
    (d_normed,) = permute_sum([d_normed_part], [0], "tensor")
    d_source_norm, grad_gain_one = norm_one_back(d_normed)
    grad_input = grad_middle + d_source_norm
    grad_gain_one = permute_allsum(grad_gain_one, "dp")
    grad_gain_two = permute_allsum(grad_gain_two, "dp")
    def dp_sum(grads):
        return [lax.psum(grad.astype(jnp.bfloat16), "dp").astype(jnp.float32) for grad in grads]

    grad_w_gate, grad_w_up, grad_w_down = dp_sum([grad_w_gate, grad_w_up, grad_w_down])
    grad_w_gate, grad_w_up, grad_w_down, grad_w_out = lax.optimization_barrier(
        (grad_w_gate, grad_w_up, grad_w_down, grad_w_out)
    )
    (grad_w_out,) = dp_sum([grad_w_out])
    grad_w_out, grad_w_query, grad_w_key, grad_w_value = lax.optimization_barrier(
        (grad_w_out, grad_w_query, grad_w_key, grad_w_value)
    )
    grad_w_query, grad_w_key, grad_w_value = dp_sum([grad_w_query, grad_w_key, grad_w_value])
    return (
        output,
        grad_input,
        grad_gain_one,
        grad_w_query,
        grad_w_key,
        grad_w_value,
        grad_w_out,
        grad_gain_two,
        grad_w_gate,
        grad_w_up,
        grad_w_down,
    )


def solution(mesh):
    placed = (
        P("dp", None),
        P("dp"),
        P(),
        P(),
        P(None, "tensor"),
        P(None, "tensor"),
        P(None, "tensor"),
        P("tensor", None),
        P(),
        P(None, "tensor"),
        P(None, "tensor"),
        P("tensor", None),
        P("dp", None),
    )
    return jax.shard_map(
        on_device,
        mesh=mesh,
        in_specs=placed,
        out_specs=(
            P("dp", None),
            P("dp", None),
            P(),
            P(None, "tensor"),
            P(None, "tensor"),
            P(None, "tensor"),
            P("tensor", None),
            P(),
            P(None, "tensor"),
            P(None, "tensor"),
            P("tensor", None),
        ),
        check_vma=False,
    )
```

```python
import jax
import jax.numpy as jnp
from jax import lax
from jax.sharding import PartitionSpec as P


HEAD_DIM = 128


EPS = 1e-05
MASKED_SCORE = -1e30


def rms_norm(values, scales):
    return values * lax.rsqrt(jnp.mean(values * values, axis=-1, keepdims=True) + EPS) * scales


def rotate(values, cos_table, sin_table):
    middle = values.shape[-1] // 2
    leading = values[..., :middle]
    trailing = values[..., middle:]
    return jnp.concatenate(
        [leading * cos_table - trailing * sin_table, trailing * cos_table + leading * sin_table],
        axis=-1,
    )


def angles_of(positions, head_size):
    frequency = 10000.0 ** (-jnp.arange(0, head_size, 2, dtype=jnp.float32) / head_size)
    angles = positions.astype(jnp.float32)[:, None] * frequency[None, :]
    return (jnp.cos(angles)[:, None, :], jnp.sin(angles)[:, None, :])


def swiglu(gate_value, up_value):
    return jax.nn.silu(gate_value) * up_value


def left_trans(left, right):
    return lax.dot_general(
        left, right, (((0,), (0,)), ((), ())), preferred_element_type=jnp.float32
    )


def right_trans(left, right):
    return lax.dot_general(
        left, right, (((1,), (1,)), ((), ())), preferred_element_type=jnp.float32
    )


def partner_perm(axis_size, mask):
    return [(index, index ^ mask) for index in range(axis_size)]


def permute_sum(parts, dims, axis):
    size = lax.axis_size(axis)
    steps = size.bit_length() - 1
    assert 1 << steps == size
    me = lax.axis_index(axis)
    pieces = list(parts)
    for step in range(steps):
        bit = (me >> step) & 1
        keep, send = [], []
        for piece, dim in zip(pieces, dims):
            half = piece.shape[dim] // 2
            keep.append(lax.dynamic_slice_in_dim(piece, bit * half, half, axis=dim))
            send.append(
                lax.dynamic_slice_in_dim(piece, (1 - bit) * half, half, axis=dim).astype(jnp.bfloat16)
            )
        got = lax.ppermute(send, axis, partner_perm(size, 1 << step))
        pieces = [mine + theirs.astype(jnp.float32) for mine, theirs in zip(keep, got)]
    pieces = [piece.astype(jnp.bfloat16) for piece in pieces]
    for step in reversed(range(steps)):
        first = ((me >> step) & 1) == 0
        got = lax.ppermute(pieces, axis, partner_perm(size, 1 << step))
        pieces = [
            jnp.concatenate(
                [jnp.where(first, mine, theirs), jnp.where(first, theirs, mine)], axis=dim
            )
            for mine, theirs, dim in zip(pieces, got, dims)
        ]
    return [piece.astype(jnp.float32) for piece in pieces]


def permute_allsum(value, axis):
    size = lax.axis_size(axis)
    steps = size.bit_length() - 1
    for step in range(steps):
        value = value + lax.ppermute(value, axis, partner_perm(size, 1 << step))
    return value


def on_device(
    inputs,
    active,
    block_table,
    gain_one,
    w_query,
    w_key,
    w_value,
    w_out,
    gain_two,
    w_gate,
    w_up,
    w_down,
    cotangent,
):
    row_count = inputs.shape[0]
    local_heads = w_query.shape[1] // HEAD_DIM
    local_groups = w_key.shape[1] // HEAD_DIM
    group_size = local_heads // local_groups
    half_rows = row_count // 2
    length = row_count * lax.axis_size("dp")
    score_scale = HEAD_DIM ** (-0.5)
    key_pos = (
        block_table[:, None] * half_rows + jnp.arange(half_rows, dtype=jnp.int32)[None, :]
    ).reshape(length)
    row_start = lax.axis_index("dp") * row_count
    query_pos = lax.dynamic_slice_in_dim(key_pos, row_start, row_count)
    slot_ids = jnp.arange(length, dtype=jnp.int32)
    own_ids = row_start + jnp.arange(row_count, dtype=jnp.int32)
    cos_table, sin_table = angles_of(query_pos, HEAD_DIM)
    keep_rows = active.astype(jnp.float32)[:, None]
    source = inputs.astype(jnp.float32)
    normed_full, norm_one_back = jax.vjp(rms_norm, source, gain_one.astype(jnp.float32))
    normed = normed_full.astype(jnp.bfloat16)
    query_raw = jnp.dot(normed, w_query, preferred_element_type=jnp.float32).reshape(
        row_count, local_heads, HEAD_DIM
    )
    key_raw = jnp.dot(normed, w_key, preferred_element_type=jnp.float32).reshape(
        row_count, local_groups, HEAD_DIM
    )
    value_low = jnp.dot(normed, w_value, preferred_element_type=jnp.float32).astype(jnp.bfloat16)
    query_low = (
        rotate(query_raw, cos_table, sin_table)
        .reshape(row_count, local_heads * HEAD_DIM)
        .astype(jnp.bfloat16)
    )
    key_low = (
        rotate(key_raw, cos_table, sin_table)
        .reshape(row_count, local_groups * HEAD_DIM)
        .astype(jnp.bfloat16)
    )
    alive_low = active.astype(jnp.bfloat16)

    def allowed_of(alive_all):
        return (key_pos[None, :] <= query_pos[:, None]) & (
            (alive_all[None, :] > 0) | (slot_ids[None, :] == own_ids[:, None])
        )

    def head_scores(head_index, keys_all, allowed):
        query_part = query_low[:, head_index * HEAD_DIM : (head_index + 1) * HEAD_DIM]
        group_index = head_index // group_size
        key_part = keys_all[:, group_index * HEAD_DIM : (group_index + 1) * HEAD_DIM]
        raw_scores = right_trans(query_part, key_part) * score_scale
        return jnp.where(allowed, raw_scores, MASKED_SCORE)

    kv_width = local_groups * HEAD_DIM
    all_kv = lax.all_gather(
        jnp.concatenate([key_low, value_low], axis=1), "dp", axis=0, tiled=True
    )
    all_keys = all_kv[:, :kv_width]
    all_values = all_kv[:, kv_width:]
    all_alive = lax.all_gather(alive_low, "dp", axis=0, tiled=True)
    allowed_fwd = allowed_of(all_alive)
    mixed_parts = []
    lse_parts = []
    for head_index in range(local_heads):
        masked = head_scores(head_index, all_keys, allowed_fwd)
        row_max = jnp.max(masked, axis=1, keepdims=True)
        shifted = jnp.exp(masked - row_max)
        row_total = jnp.sum(shifted, axis=1, keepdims=True)
        probs_low = (shifted / row_total).astype(jnp.bfloat16)
        lse_parts.append(row_max + jnp.log(row_total))
        group_index = head_index // group_size
        value_part = all_values[:, group_index * HEAD_DIM : (group_index + 1) * HEAD_DIM]
        mixed_parts.append(jnp.dot(probs_low, value_part, preferred_element_type=jnp.float32))
    attended = jnp.concatenate(mixed_parts, axis=1).astype(jnp.bfloat16)
    (branch,) = permute_sum(
        [jnp.dot(attended, w_out, preferred_element_type=jnp.float32)], [0], "tensor"
    )
    middle = source + keep_rows * branch
    normed_two_full, norm_two_back = jax.vjp(rms_norm, middle, gain_two.astype(jnp.float32))
    normed_two = normed_two_full.astype(jnp.bfloat16)
    gate_value = jnp.dot(normed_two, w_gate, preferred_element_type=jnp.float32)
    up_value = jnp.dot(normed_two, w_up, preferred_element_type=jnp.float32)
    hidden_full, swiglu_back = jax.vjp(swiglu, gate_value, up_value)
    hidden = hidden_full.astype(jnp.bfloat16)
    down_part = jnp.dot(hidden, w_down, preferred_element_type=jnp.float32)
    grad_out = cotangent.astype(jnp.float32)

    def dp_sum(grads):
        return [lax.psum(grad.astype(jnp.bfloat16), "dp").astype(jnp.float32) for grad in grads]

    d_down = (keep_rows * grad_out).astype(jnp.bfloat16)
    grad_w_down = left_trans(hidden, d_down)
    d_hidden = right_trans(d_down, w_down)
    d_gate_full, d_up_full = swiglu_back(d_hidden)
    d_gate = d_gate_full.astype(jnp.bfloat16)
    d_up = d_up_full.astype(jnp.bfloat16)
    grad_w_gate = left_trans(normed_two, d_gate)
    grad_w_up = left_trans(normed_two, d_up)
    d_normed_two_part = right_trans(d_gate, w_gate) + right_trans(d_up, w_up)
    grad_w_gate, grad_w_up, grad_w_down, d_normed_two_part = lax.optimization_barrier(
        (grad_w_gate, grad_w_up, grad_w_down, d_normed_two_part)
    )
    grad_w_gate, grad_w_up, grad_w_down = dp_sum([grad_w_gate, grad_w_up, grad_w_down])
    (d_normed_two,) = permute_sum([d_normed_two_part], [0], "tensor")
    down_part, d_normed_two = lax.optimization_barrier((down_part, d_normed_two))
    (down_sum,) = permute_sum([down_part], [0], "tensor")
    d_middle_norm, grad_gain_two = norm_two_back(d_normed_two)
    grad_middle = grad_out + d_middle_norm
    d_branch = (keep_rows * grad_middle).astype(jnp.bfloat16)
    grad_w_out = left_trans(attended, d_branch)
    grad_w_gate, grad_w_up, grad_w_down, grad_w_out = lax.optimization_barrier(
        (grad_w_gate, grad_w_up, grad_w_down, grad_w_out)
    )
    d_attended = right_trans(d_branch, w_out).astype(jnp.bfloat16)
    back_keys, back_values = all_keys, all_values
    allowed_back = allowed_fwd
    d_query_parts = []
    d_key_parts = [jnp.zeros((length, HEAD_DIM), jnp.float32) for _ in range(local_groups)]
    d_value_parts = [jnp.zeros((length, HEAD_DIM), jnp.float32) for _ in range(local_groups)]
    for head_index in range(local_heads):
        group_index = head_index // group_size
        masked = head_scores(head_index, back_keys, allowed_back)
        probs = jnp.where(allowed_back, jnp.exp(masked - lse_parts[head_index]), 0.0)
        probs_low = probs.astype(jnp.bfloat16)
        d_out_part = d_attended[:, head_index * HEAD_DIM : (head_index + 1) * HEAD_DIM]
        key_part = back_keys[:, group_index * HEAD_DIM : (group_index + 1) * HEAD_DIM]
        value_part = back_values[:, group_index * HEAD_DIM : (group_index + 1) * HEAD_DIM]
        query_part = query_low[:, head_index * HEAD_DIM : (head_index + 1) * HEAD_DIM]
        d_probs = right_trans(d_out_part, value_part)
        row_delta = jnp.sum(probs * d_probs, axis=1, keepdims=True)
        d_scores = (probs * (d_probs - row_delta)).astype(jnp.bfloat16)
        d_query_parts.append(
            jnp.dot(d_scores, key_part, preferred_element_type=jnp.float32) * score_scale
        )
        d_key_parts[group_index] = (
            d_key_parts[group_index] + left_trans(d_scores, query_part) * score_scale
        )
        d_value_parts[group_index] = d_value_parts[group_index] + left_trans(probs_low, d_out_part)
    d_key_all = jnp.concatenate(d_key_parts, axis=1)
    d_value_all = jnp.concatenate(d_value_parts, axis=1)
    d_kv_cat = jnp.concatenate([d_key_all, d_value_all], axis=1).astype(jnp.bfloat16)
    d_kv_own = lax.psum_scatter(
        d_kv_cat,
        "dp",
        scatter_dimension=0,
        tiled=True,
    ).astype(jnp.float32)
    d_kv_own, grad_w_out = lax.optimization_barrier((d_kv_own, grad_w_out))
    (grad_w_out,) = dp_sum([grad_w_out])
    d_key_own = d_kv_own[:, :kv_width]
    d_value_own = d_kv_own[:, kv_width:]
    d_queries = jnp.concatenate(d_query_parts, axis=1).reshape(row_count, local_heads, HEAD_DIM)
    d_query_low = (
        rotate(d_queries, cos_table, -sin_table)
        .reshape(row_count, local_heads * HEAD_DIM)
        .astype(jnp.bfloat16)
    )
    d_key_low = (
        rotate(d_key_own.reshape(row_count, local_groups, HEAD_DIM), cos_table, -sin_table)
        .reshape(row_count, local_groups * HEAD_DIM)
        .astype(jnp.bfloat16)
    )
    d_value_low = d_value_own.astype(jnp.bfloat16)
    grad_w_query = left_trans(normed, d_query_low)
    grad_w_key = left_trans(normed, d_key_low)
    grad_w_value = left_trans(normed, d_value_low)
    d_normed_part = (
        right_trans(d_query_low, w_query)
        + right_trans(d_key_low, w_key)
        + right_trans(d_value_low, w_value)
    )
    down_sum, d_normed_part = lax.optimization_barrier((down_sum, d_normed_part))
    output = (middle + keep_rows * down_sum).astype(jnp.bfloat16)
    (d_normed,) = permute_sum([d_normed_part], [0], "tensor")
    d_source_norm, grad_gain_one = norm_one_back(d_normed)
    grad_input = grad_middle + d_source_norm
    grad_gain_one = permute_allsum(grad_gain_one, "dp")
    grad_gain_two = permute_allsum(grad_gain_two, "dp")
    grad_w_query, grad_w_key, grad_w_value = dp_sum([grad_w_query, grad_w_key, grad_w_value])
    return (
        output,
        grad_input,
        grad_gain_one,
        grad_w_query,
        grad_w_key,
        grad_w_value,
        grad_w_out,
        grad_gain_two,
        grad_w_gate,
        grad_w_up,
        grad_w_down,
    )


def solution(mesh):
    placed = (
        P("dp", None),
        P("dp"),
        P(),
        P(),
        P(None, "tensor"),
        P(None, "tensor"),
        P(None, "tensor"),
        P("tensor", None),
        P(),
        P(None, "tensor"),
        P(None, "tensor"),
        P("tensor", None),
        P("dp", None),
    )
    return jax.shard_map(
        on_device,
        mesh=mesh,
        in_specs=placed,
        out_specs=(
            P("dp", None),
            P("dp", None),
            P(),
            P(None, "tensor"),
            P(None, "tensor"),
            P(None, "tensor"),
            P("tensor", None),
            P(),
            P(None, "tensor"),
            P(None, "tensor"),
            P("tensor", None),
        ),
        check_vma=False,
    )
```

```python
import jax
import jax.numpy as jnp
from jax import lax
from jax.sharding import PartitionSpec as P


HEAD_DIM = 128


EPS = 1e-05
MASKED_SCORE = -1e30


def rms_norm(values, scales):
    return values * lax.rsqrt(jnp.mean(values * values, axis=-1, keepdims=True) + EPS) * scales


def rotate(values, cos_table, sin_table):
    middle = values.shape[-1] // 2
    leading = values[..., :middle]
    trailing = values[..., middle:]
    return jnp.concatenate(
        [leading * cos_table - trailing * sin_table, trailing * cos_table + leading * sin_table],
        axis=-1,
    )


def angles_of(positions, head_size):
    frequency = 10000.0 ** (-jnp.arange(0, head_size, 2, dtype=jnp.float32) / head_size)
    angles = positions.astype(jnp.float32)[:, None] * frequency[None, :]
    return (jnp.cos(angles)[:, None, :], jnp.sin(angles)[:, None, :])


def swiglu(gate_value, up_value):
    return jax.nn.silu(gate_value) * up_value


def left_trans(left, right):
    return lax.dot_general(
        left, right, (((0,), (0,)), ((), ())), preferred_element_type=jnp.float32
    )


def right_trans(left, right):
    return lax.dot_general(
        left, right, (((1,), (1,)), ((), ())), preferred_element_type=jnp.float32
    )


def partner_perm(axis_size, mask):
    return [(index, index ^ mask) for index in range(axis_size)]


def permute_sum(parts, dims, axis):
    size = lax.axis_size(axis)
    steps = size.bit_length() - 1
    assert 1 << steps == size
    me = lax.axis_index(axis)
    pieces = list(parts)
    for step in range(steps):
        bit = (me >> step) & 1
        keep, send = [], []
        for piece, dim in zip(pieces, dims):
            half = piece.shape[dim] // 2
            keep.append(lax.dynamic_slice_in_dim(piece, bit * half, half, axis=dim))
            send.append(
                lax.dynamic_slice_in_dim(piece, (1 - bit) * half, half, axis=dim).astype(jnp.bfloat16)
            )
        got = lax.ppermute(send, axis, partner_perm(size, 1 << step))
        pieces = [mine + theirs.astype(jnp.float32) for mine, theirs in zip(keep, got)]
    pieces = [piece.astype(jnp.bfloat16) for piece in pieces]
    for step in reversed(range(steps)):
        first = ((me >> step) & 1) == 0
        got = lax.ppermute(pieces, axis, partner_perm(size, 1 << step))
        pieces = [
            jnp.concatenate(
                [jnp.where(first, mine, theirs), jnp.where(first, theirs, mine)], axis=dim
            )
            for mine, theirs, dim in zip(pieces, got, dims)
        ]
    return [piece.astype(jnp.float32) for piece in pieces]


def permute_allsum(value, axis):
    size = lax.axis_size(axis)
    steps = size.bit_length() - 1
    for step in range(steps):
        value = value + lax.ppermute(value, axis, partner_perm(size, 1 << step))
    return value


def on_device(
    inputs,
    active,
    block_table,
    gain_one,
    w_query,
    w_key,
    w_value,
    w_out,
    gain_two,
    w_gate,
    w_up,
    w_down,
    cotangent,
):
    row_count = inputs.shape[0]
    local_heads = w_query.shape[1] // HEAD_DIM
    local_groups = w_key.shape[1] // HEAD_DIM
    group_size = local_heads // local_groups
    half_rows = row_count // 2
    length = row_count * lax.axis_size("dp")
    score_scale = HEAD_DIM ** (-0.5)
    key_pos = (
        block_table[:, None] * half_rows + jnp.arange(half_rows, dtype=jnp.int32)[None, :]
    ).reshape(length)
    row_start = lax.axis_index("dp") * row_count
    query_pos = lax.dynamic_slice_in_dim(key_pos, row_start, row_count)
    slot_ids = jnp.arange(length, dtype=jnp.int32)
    own_ids = row_start + jnp.arange(row_count, dtype=jnp.int32)
    cos_table, sin_table = angles_of(query_pos, HEAD_DIM)
    keep_rows = active.astype(jnp.float32)[:, None]
    source = inputs.astype(jnp.float32)
    normed_full, norm_one_back = jax.vjp(rms_norm, source, gain_one.astype(jnp.float32))
    normed = normed_full.astype(jnp.bfloat16)
    query_raw = jnp.dot(normed, w_query, preferred_element_type=jnp.float32).reshape(
        row_count, local_heads, HEAD_DIM
    )
    key_raw = jnp.dot(normed, w_key, preferred_element_type=jnp.float32).reshape(
        row_count, local_groups, HEAD_DIM
    )
    value_low = jnp.dot(normed, w_value, preferred_element_type=jnp.float32).astype(jnp.bfloat16)
    query_low = (
        rotate(query_raw, cos_table, sin_table)
        .reshape(row_count, local_heads * HEAD_DIM)
        .astype(jnp.bfloat16)
    )
    key_low = (
        rotate(key_raw, cos_table, sin_table)
        .reshape(row_count, local_groups * HEAD_DIM)
        .astype(jnp.bfloat16)
    )
    alive_low = active.astype(jnp.bfloat16)

    def allowed_of(alive_all):
        return (key_pos[None, :] <= query_pos[:, None]) & (
            (alive_all[None, :] > 0) | (slot_ids[None, :] == own_ids[:, None])
        )

    def head_scores(head_index, keys_all, allowed):
        query_part = query_low[:, head_index * HEAD_DIM : (head_index + 1) * HEAD_DIM]
        group_index = head_index // group_size
        key_part = keys_all[:, group_index * HEAD_DIM : (group_index + 1) * HEAD_DIM]
        raw_scores = right_trans(query_part, key_part) * score_scale
        return jnp.where(allowed, raw_scores, MASKED_SCORE)

    kv_width = local_groups * HEAD_DIM
    all_kv = lax.all_gather(
        jnp.concatenate([key_low, value_low], axis=1), "dp", axis=0, tiled=True
    )
    all_keys = all_kv[:, :kv_width]
    all_values = all_kv[:, kv_width:]
    all_alive = lax.all_gather(alive_low, "dp", axis=0, tiled=True)
    allowed_fwd = allowed_of(all_alive)
    mixed_parts = []
    lse_parts = []
    for head_index in range(local_heads):
        masked = head_scores(head_index, all_keys, allowed_fwd)
        row_max = jnp.max(masked, axis=1, keepdims=True)
        shifted = jnp.exp(masked - row_max)
        row_total = jnp.sum(shifted, axis=1, keepdims=True)
        probs_low = (shifted / row_total).astype(jnp.bfloat16)
        lse_parts.append(row_max + jnp.log(row_total))
        group_index = head_index // group_size
        value_part = all_values[:, group_index * HEAD_DIM : (group_index + 1) * HEAD_DIM]
        mixed_parts.append(jnp.dot(probs_low, value_part, preferred_element_type=jnp.float32))
    attended = jnp.concatenate(mixed_parts, axis=1).astype(jnp.bfloat16)
    (branch,) = permute_sum(
        [jnp.dot(attended, w_out, preferred_element_type=jnp.float32)], [0], "tensor"
    )
    middle = source + keep_rows * branch
    normed_two_full, norm_two_back = jax.vjp(rms_norm, middle, gain_two.astype(jnp.float32))
    normed_two = normed_two_full.astype(jnp.bfloat16)
    gate_value = jnp.dot(normed_two, w_gate, preferred_element_type=jnp.float32)
    up_value = jnp.dot(normed_two, w_up, preferred_element_type=jnp.float32)
    hidden_full, swiglu_back = jax.vjp(swiglu, gate_value, up_value)
    hidden = hidden_full.astype(jnp.bfloat16)
    down_part = jnp.dot(hidden, w_down, preferred_element_type=jnp.float32)
    grad_out = cotangent.astype(jnp.float32)

    def dp_sum(grads):
        return [lax.psum(grad.astype(jnp.bfloat16), "dp") for grad in grads]

    d_down = (keep_rows * grad_out).astype(jnp.bfloat16)
    grad_w_down = left_trans(hidden, d_down)
    d_hidden = right_trans(d_down, w_down)
    d_gate_full, d_up_full = swiglu_back(d_hidden)
    d_gate = d_gate_full.astype(jnp.bfloat16)
    d_up = d_up_full.astype(jnp.bfloat16)
    grad_w_gate = left_trans(normed_two, d_gate)
    grad_w_up = left_trans(normed_two, d_up)
    d_normed_two_part = right_trans(d_gate, w_gate) + right_trans(d_up, w_up)
    grad_w_gate, grad_w_up, grad_w_down, d_normed_two_part = lax.optimization_barrier(
        (grad_w_gate, grad_w_up, grad_w_down, d_normed_two_part)
    )
    mlp_grads = dp_sum([grad_w_gate, grad_w_up, grad_w_down])
    grad_w_gate, grad_w_up, grad_w_down = mlp_grads
    (d_normed_two,) = permute_sum([d_normed_two_part], [0], "tensor")
    down_part, d_normed_two = lax.optimization_barrier((down_part, d_normed_two))
    (down_sum,) = permute_sum([down_part], [0], "tensor")
    d_middle_norm, grad_gain_two = norm_two_back(d_normed_two)
    grad_middle = grad_out + d_middle_norm
    d_branch = (keep_rows * grad_middle).astype(jnp.bfloat16)
    grad_w_out = left_trans(attended, d_branch)
    grad_w_gate, grad_w_up, grad_w_down, grad_w_out = lax.optimization_barrier(
        (grad_w_gate, grad_w_up, grad_w_down, grad_w_out)
    )
    d_attended = right_trans(d_branch, w_out).astype(jnp.bfloat16)
    back_keys, back_values = all_keys, all_values
    allowed_back = allowed_fwd
    d_query_parts = []
    d_key_parts = [jnp.zeros((length, HEAD_DIM), jnp.float32) for _ in range(local_groups)]
    d_value_parts = [jnp.zeros((length, HEAD_DIM), jnp.float32) for _ in range(local_groups)]
    for head_index in range(local_heads):
        group_index = head_index // group_size
        masked = head_scores(head_index, back_keys, allowed_back)
        probs = jnp.where(allowed_back, jnp.exp(masked - lse_parts[head_index]), 0.0)
        probs_low = probs.astype(jnp.bfloat16)
        d_out_part = d_attended[:, head_index * HEAD_DIM : (head_index + 1) * HEAD_DIM]
        key_part = back_keys[:, group_index * HEAD_DIM : (group_index + 1) * HEAD_DIM]
        value_part = back_values[:, group_index * HEAD_DIM : (group_index + 1) * HEAD_DIM]
        query_part = query_low[:, head_index * HEAD_DIM : (head_index + 1) * HEAD_DIM]
        d_probs = right_trans(d_out_part, value_part)
        row_delta = jnp.sum(probs * d_probs, axis=1, keepdims=True)
        d_scores = (probs * (d_probs - row_delta)).astype(jnp.bfloat16)
        d_query_parts.append(
            jnp.dot(d_scores, key_part, preferred_element_type=jnp.float32) * score_scale
        )
        d_key_parts[group_index] = (
            d_key_parts[group_index] + left_trans(d_scores, query_part) * score_scale
        )
        d_value_parts[group_index] = d_value_parts[group_index] + left_trans(probs_low, d_out_part)
    d_key_all = jnp.concatenate(d_key_parts, axis=1)
    d_value_all = jnp.concatenate(d_value_parts, axis=1)
    d_kv_cat = jnp.concatenate([d_key_all, d_value_all], axis=1).astype(jnp.bfloat16)
    d_kv_own = lax.psum_scatter(
        d_kv_cat,
        "dp",
        scatter_dimension=0,
        tiled=True,
    ).astype(jnp.float32)
    d_kv_own, grad_w_out = lax.optimization_barrier((d_kv_own, grad_w_out))
    d_key_own = d_kv_own[:, :kv_width]
    d_value_own = d_kv_own[:, kv_width:]
    d_queries = jnp.concatenate(d_query_parts, axis=1).reshape(row_count, local_heads, HEAD_DIM)
    d_query_low = (
        rotate(d_queries, cos_table, -sin_table)
        .reshape(row_count, local_heads * HEAD_DIM)
        .astype(jnp.bfloat16)
    )
    d_key_low = (
        rotate(d_key_own.reshape(row_count, local_groups, HEAD_DIM), cos_table, -sin_table)
        .reshape(row_count, local_groups * HEAD_DIM)
        .astype(jnp.bfloat16)
    )
    d_value_low = d_value_own.astype(jnp.bfloat16)
    grad_w_query = left_trans(normed, d_query_low)
    grad_w_key = left_trans(normed, d_key_low)
    grad_w_value = left_trans(normed, d_value_low)
    d_normed_part = (
        right_trans(d_query_low, w_query)
        + right_trans(d_key_low, w_key)
        + right_trans(d_value_low, w_value)
    )
    (
        down_sum,
        d_normed_part,
        grad_w_out,
        grad_w_query,
        grad_w_key,
        grad_w_value,
    ) = lax.optimization_barrier(
        (down_sum, d_normed_part, grad_w_out, grad_w_query, grad_w_key, grad_w_value)
    )
    grad_w_out, grad_w_query, grad_w_key, grad_w_value = dp_sum(
        [grad_w_out, grad_w_query, grad_w_key, grad_w_value]
    )
    grad_w_gate, grad_w_up, grad_w_down = [
        grad.astype(jnp.float32) for grad in (grad_w_gate, grad_w_up, grad_w_down)
    ]
    output = (middle + keep_rows * down_sum).astype(jnp.bfloat16)
    (d_normed,) = permute_sum([d_normed_part], [0], "tensor")
    d_source_norm, grad_gain_one = norm_one_back(d_normed)
    grad_input = grad_middle + d_source_norm
    grad_gain_one = permute_allsum(grad_gain_one, "dp")
    grad_gain_two = permute_allsum(grad_gain_two, "dp")
    grad_w_out, grad_w_query, grad_w_key, grad_w_value = [
        grad.astype(jnp.float32) for grad in (grad_w_out, grad_w_query, grad_w_key, grad_w_value)
    ]
    return (
        output,
        grad_input,
        grad_gain_one,
        grad_w_query,
        grad_w_key,
        grad_w_value,
        grad_w_out,
        grad_gain_two,
        grad_w_gate,
        grad_w_up,
        grad_w_down,
    )


def solution(mesh):
    placed = (
        P("dp", None),
        P("dp"),
        P(),
        P(),
        P(None, "tensor"),
        P(None, "tensor"),
        P(None, "tensor"),
        P("tensor", None),
        P(),
        P(None, "tensor"),
        P(None, "tensor"),
        P("tensor", None),
        P("dp", None),
    )
    return jax.shard_map(
        on_device,
        mesh=mesh,
        in_specs=placed,
        out_specs=(
            P("dp", None),
            P("dp", None),
            P(),
            P(None, "tensor"),
            P(None, "tensor"),
            P(None, "tensor"),
            P("tensor", None),
            P(),
            P(None, "tensor"),
            P(None, "tensor"),
            P("tensor", None),
        ),
        check_vma=False,
    )
```

```python
import jax
import jax.numpy as jnp
from jax import lax
from jax.sharding import PartitionSpec as P


HEAD_DIM = 128


EPS = 1e-05
MASKED_SCORE = -1e30


def rms_norm(values, scales):
    return values * lax.rsqrt(jnp.mean(values * values, axis=-1, keepdims=True) + EPS) * scales


def rotate(values, cos_table, sin_table):
    middle = values.shape[-1] // 2
    leading = values[..., :middle]
    trailing = values[..., middle:]
    return jnp.concatenate(
        [leading * cos_table - trailing * sin_table, trailing * cos_table + leading * sin_table],
        axis=-1,
    )


def angles_of(positions, head_size):
    frequency = 10000.0 ** (-jnp.arange(0, head_size, 2, dtype=jnp.float32) / head_size)
    angles = positions.astype(jnp.float32)[:, None] * frequency[None, :]
    return (jnp.cos(angles)[:, None, :], jnp.sin(angles)[:, None, :])


def swiglu(gate_value, up_value):
    return jax.nn.silu(gate_value) * up_value


def left_trans(left, right):
    return lax.dot_general(
        left, right, (((0,), (0,)), ((), ())), preferred_element_type=jnp.float32
    )


def right_trans(left, right):
    return lax.dot_general(
        left, right, (((1,), (1,)), ((), ())), preferred_element_type=jnp.float32
    )


def partner_perm(axis_size, mask):
    return [(index, index ^ mask) for index in range(axis_size)]


def permute_sum(parts, dims, axis):
    size = lax.axis_size(axis)
    steps = size.bit_length() - 1
    assert 1 << steps == size
    me = lax.axis_index(axis)
    pieces = list(parts)
    for step in range(steps):
        bit = (me >> step) & 1
        keep, send = [], []
        for piece, dim in zip(pieces, dims):
            half = piece.shape[dim] // 2
            keep.append(lax.dynamic_slice_in_dim(piece, bit * half, half, axis=dim))
            send.append(
                lax.dynamic_slice_in_dim(piece, (1 - bit) * half, half, axis=dim).astype(jnp.bfloat16)
            )
        got = lax.ppermute(send, axis, partner_perm(size, 1 << step))
        pieces = [mine + theirs.astype(jnp.float32) for mine, theirs in zip(keep, got)]
    pieces = [piece.astype(jnp.bfloat16) for piece in pieces]
    for step in reversed(range(steps)):
        first = ((me >> step) & 1) == 0
        got = lax.ppermute(pieces, axis, partner_perm(size, 1 << step))
        pieces = [
            jnp.concatenate(
                [jnp.where(first, mine, theirs), jnp.where(first, theirs, mine)], axis=dim
            )
            for mine, theirs, dim in zip(pieces, got, dims)
        ]
    return [piece.astype(jnp.float32) for piece in pieces]


def permute_allsum(value, axis):
    size = lax.axis_size(axis)
    steps = size.bit_length() - 1
    for step in range(steps):
        value = value + lax.ppermute(value, axis, partner_perm(size, 1 << step))
    return value


def on_device(
    inputs,
    active,
    block_table,
    gain_one,
    w_query,
    w_key,
    w_value,
    w_out,
    gain_two,
    w_gate,
    w_up,
    w_down,
    cotangent,
):
    row_count = inputs.shape[0]
    local_heads = w_query.shape[1] // HEAD_DIM
    local_groups = w_key.shape[1] // HEAD_DIM
    group_size = local_heads // local_groups
    half_rows = row_count // 2
    length = row_count * lax.axis_size("dp")
    score_scale = HEAD_DIM ** (-0.5)
    key_pos = (
        block_table[:, None] * half_rows + jnp.arange(half_rows, dtype=jnp.int32)[None, :]
    ).reshape(length)
    row_start = lax.axis_index("dp") * row_count
    query_pos = lax.dynamic_slice_in_dim(key_pos, row_start, row_count)
    slot_ids = jnp.arange(length, dtype=jnp.int32)
    own_ids = row_start + jnp.arange(row_count, dtype=jnp.int32)
    cos_table, sin_table = angles_of(query_pos, HEAD_DIM)
    keep_rows = active.astype(jnp.float32)[:, None]
    source = inputs.astype(jnp.float32)
    normed_full, norm_one_back = jax.vjp(rms_norm, source, gain_one.astype(jnp.float32))
    normed = normed_full.astype(jnp.bfloat16)
    query_raw = jnp.dot(normed, w_query, preferred_element_type=jnp.float32).reshape(
        row_count, local_heads, HEAD_DIM
    )
    key_raw = jnp.dot(normed, w_key, preferred_element_type=jnp.float32).reshape(
        row_count, local_groups, HEAD_DIM
    )
    value_low = jnp.dot(normed, w_value, preferred_element_type=jnp.float32).astype(jnp.bfloat16)
    query_low = (
        rotate(query_raw, cos_table, sin_table)
        .reshape(row_count, local_heads * HEAD_DIM)
        .astype(jnp.bfloat16)
    )
    key_low = (
        rotate(key_raw, cos_table, sin_table)
        .reshape(row_count, local_groups * HEAD_DIM)
        .astype(jnp.bfloat16)
    )
    alive_low = active.astype(jnp.bfloat16)

    def allowed_of(alive_all):
        return (key_pos[None, :] <= query_pos[:, None]) & (
            (alive_all[None, :] > 0) | (slot_ids[None, :] == own_ids[:, None])
        )

    def head_scores(head_index, keys_all, allowed):
        query_part = query_low[:, head_index * HEAD_DIM : (head_index + 1) * HEAD_DIM]
        group_index = head_index // group_size
        key_part = keys_all[:, group_index * HEAD_DIM : (group_index + 1) * HEAD_DIM]
        raw_scores = right_trans(query_part, key_part) * score_scale
        return jnp.where(allowed, raw_scores, MASKED_SCORE)

    kv_width = local_groups * HEAD_DIM
    all_kv = lax.all_gather(
        jnp.concatenate([key_low, value_low], axis=1), "dp", axis=0, tiled=True
    )
    all_keys = all_kv[:, :kv_width]
    all_values = all_kv[:, kv_width:]
    all_alive = lax.all_gather(alive_low, "dp", axis=0, tiled=True)
    allowed_fwd = allowed_of(all_alive)
    mixed_parts = []
    lse_parts = []
    for head_index in range(local_heads):
        masked = head_scores(head_index, all_keys, allowed_fwd)
        row_max = jnp.max(masked, axis=1, keepdims=True)
        shifted = jnp.exp(masked - row_max)
        row_total = jnp.sum(shifted, axis=1, keepdims=True)
        probs_low = (shifted / row_total).astype(jnp.bfloat16)
        lse_parts.append(row_max + jnp.log(row_total))
        group_index = head_index // group_size
        value_part = all_values[:, group_index * HEAD_DIM : (group_index + 1) * HEAD_DIM]
        mixed_parts.append(jnp.dot(probs_low, value_part, preferred_element_type=jnp.float32))
    attended = jnp.concatenate(mixed_parts, axis=1).astype(jnp.bfloat16)
    branch_part = jnp.dot(attended, w_out, preferred_element_type=jnp.float32)
    branch_top = lax.psum(branch_part[:half_rows].astype(jnp.bfloat16), "tensor")
    (branch_bottom,) = permute_sum([branch_part[half_rows:]], [0], "tensor")
    branch = jnp.concatenate([branch_top.astype(jnp.float32), branch_bottom], axis=0)
    middle = source + keep_rows * branch
    normed_two_full, norm_two_back = jax.vjp(rms_norm, middle, gain_two.astype(jnp.float32))
    normed_two = normed_two_full.astype(jnp.bfloat16)
    gate_value = jnp.dot(normed_two, w_gate, preferred_element_type=jnp.float32)
    up_value = jnp.dot(normed_two, w_up, preferred_element_type=jnp.float32)
    hidden_full, swiglu_back = jax.vjp(swiglu, gate_value, up_value)
    hidden = hidden_full.astype(jnp.bfloat16)
    down_part = jnp.dot(hidden, w_down, preferred_element_type=jnp.float32)
    grad_out = cotangent.astype(jnp.float32)

    def dp_sum(grads):
        return [lax.psum(grad.astype(jnp.bfloat16), "dp") for grad in grads]

    d_down = (keep_rows * grad_out).astype(jnp.bfloat16)
    grad_w_down = left_trans(hidden, d_down)
    d_hidden = right_trans(d_down, w_down)
    d_gate_full, d_up_full = swiglu_back(d_hidden)
    d_gate = d_gate_full.astype(jnp.bfloat16)
    d_up = d_up_full.astype(jnp.bfloat16)
    grad_w_gate = left_trans(normed_two, d_gate)
    grad_w_up = left_trans(normed_two, d_up)
    d_normed_two_part = right_trans(d_gate, w_gate) + right_trans(d_up, w_up)
    grad_w_gate, grad_w_up, grad_w_down, d_normed_two_part = lax.optimization_barrier(
        (grad_w_gate, grad_w_up, grad_w_down, d_normed_two_part)
    )
    mlp_grads = dp_sum([grad_w_gate, grad_w_up, grad_w_down])
    grad_w_gate, grad_w_up, grad_w_down = mlp_grads
    (d_normed_two,) = permute_sum([d_normed_two_part], [0], "tensor")
    down_part, d_normed_two = lax.optimization_barrier((down_part, d_normed_two))
    (down_sum,) = permute_sum([down_part], [0], "tensor")
    d_middle_norm, grad_gain_two = norm_two_back(d_normed_two)
    grad_middle = grad_out + d_middle_norm
    d_branch = (keep_rows * grad_middle).astype(jnp.bfloat16)
    grad_w_out = left_trans(attended, d_branch)
    grad_w_gate, grad_w_up, grad_w_down, grad_w_out = lax.optimization_barrier(
        (grad_w_gate, grad_w_up, grad_w_down, grad_w_out)
    )
    d_attended = right_trans(d_branch, w_out).astype(jnp.bfloat16)
    back_keys, back_values = all_keys, all_values
    allowed_back = allowed_fwd
    d_query_parts = []
    d_key_parts = [jnp.zeros((length, HEAD_DIM), jnp.float32) for _ in range(local_groups)]
    d_value_parts = [jnp.zeros((length, HEAD_DIM), jnp.float32) for _ in range(local_groups)]
    for head_index in range(local_heads):
        group_index = head_index // group_size
        masked = head_scores(head_index, back_keys, allowed_back)
        probs = jnp.where(allowed_back, jnp.exp(masked - lse_parts[head_index]), 0.0)
        probs_low = probs.astype(jnp.bfloat16)
        d_out_part = d_attended[:, head_index * HEAD_DIM : (head_index + 1) * HEAD_DIM]
        key_part = back_keys[:, group_index * HEAD_DIM : (group_index + 1) * HEAD_DIM]
        value_part = back_values[:, group_index * HEAD_DIM : (group_index + 1) * HEAD_DIM]
        query_part = query_low[:, head_index * HEAD_DIM : (head_index + 1) * HEAD_DIM]
        d_probs = right_trans(d_out_part, value_part)
        row_delta = jnp.sum(probs * d_probs, axis=1, keepdims=True)
        d_scores = (probs * (d_probs - row_delta)).astype(jnp.bfloat16)
        d_query_parts.append(
            jnp.dot(d_scores, key_part, preferred_element_type=jnp.float32) * score_scale
        )
        d_key_parts[group_index] = (
            d_key_parts[group_index] + left_trans(d_scores, query_part) * score_scale
        )
        d_value_parts[group_index] = d_value_parts[group_index] + left_trans(probs_low, d_out_part)
    d_key_all = jnp.concatenate(d_key_parts, axis=1)
    d_value_all = jnp.concatenate(d_value_parts, axis=1)
    d_kv_cat = jnp.concatenate([d_key_all, d_value_all], axis=1).astype(jnp.bfloat16)
    d_kv_own = lax.psum_scatter(
        d_kv_cat,
        "dp",
        scatter_dimension=0,
        tiled=True,
    ).astype(jnp.float32)
    d_kv_own, grad_w_out = lax.optimization_barrier((d_kv_own, grad_w_out))
    d_key_own = d_kv_own[:, :kv_width]
    d_value_own = d_kv_own[:, kv_width:]
    d_queries = jnp.concatenate(d_query_parts, axis=1).reshape(row_count, local_heads, HEAD_DIM)
    d_query_low = (
        rotate(d_queries, cos_table, -sin_table)
        .reshape(row_count, local_heads * HEAD_DIM)
        .astype(jnp.bfloat16)
    )
    d_key_low = (
        rotate(d_key_own.reshape(row_count, local_groups, HEAD_DIM), cos_table, -sin_table)
        .reshape(row_count, local_groups * HEAD_DIM)
        .astype(jnp.bfloat16)
    )
    d_value_low = d_value_own.astype(jnp.bfloat16)
    grad_w_query = left_trans(normed, d_query_low)
    grad_w_key = left_trans(normed, d_key_low)
    grad_w_value = left_trans(normed, d_value_low)
    d_normed_part = (
        right_trans(d_query_low, w_query)
        + right_trans(d_key_low, w_key)
        + right_trans(d_value_low, w_value)
    )
    (
        down_sum,
        d_normed_part,
        grad_w_out,
        grad_w_query,
        grad_w_key,
        grad_w_value,
    ) = lax.optimization_barrier(
        (down_sum, d_normed_part, grad_w_out, grad_w_query, grad_w_key, grad_w_value)
    )
    grad_w_out, grad_w_query, grad_w_key, grad_w_value = dp_sum(
        [grad_w_out, grad_w_query, grad_w_key, grad_w_value]
    )
    grad_w_gate, grad_w_up, grad_w_down = [
        grad.astype(jnp.float32) for grad in (grad_w_gate, grad_w_up, grad_w_down)
    ]
    output = (middle + keep_rows * down_sum).astype(jnp.bfloat16)
    (d_normed,) = permute_sum([d_normed_part], [0], "tensor")
    d_source_norm, grad_gain_one = norm_one_back(d_normed)
    grad_input = grad_middle + d_source_norm
    grad_gain_one = permute_allsum(grad_gain_one, "dp")
    grad_gain_two = permute_allsum(grad_gain_two, "dp")
    grad_w_out, grad_w_query, grad_w_key, grad_w_value = [
        grad.astype(jnp.float32) for grad in (grad_w_out, grad_w_query, grad_w_key, grad_w_value)
    ]
    return (
        output,
        grad_input,
        grad_gain_one,
        grad_w_query,
        grad_w_key,
        grad_w_value,
        grad_w_out,
        grad_gain_two,
        grad_w_gate,
        grad_w_up,
        grad_w_down,
    )


def solution(mesh):
    placed = (
        P("dp", None),
        P("dp"),
        P(),
        P(),
        P(None, "tensor"),
        P(None, "tensor"),
        P(None, "tensor"),
        P("tensor", None),
        P(),
        P(None, "tensor"),
        P(None, "tensor"),
        P("tensor", None),
        P("dp", None),
    )
    return jax.shard_map(
        on_device,
        mesh=mesh,
        in_specs=placed,
        out_specs=(
            P("dp", None),
            P("dp", None),
            P(),
            P(None, "tensor"),
            P(None, "tensor"),
            P(None, "tensor"),
            P("tensor", None),
            P(),
            P(None, "tensor"),
            P(None, "tensor"),
            P("tensor", None),
        ),
        check_vma=False,
    )
```

```python
import functools

import jax
import jax.numpy as jnp
from jax import lax
from jax.experimental import pallas as pl
from jax.experimental.pallas import tpu as pltpu
from jax.sharding import PartitionSpec as P


HEAD_DIM = 128


EPS = 1e-05
MASKED_SCORE = -1e30


def rms_norm(values, scales):
    return values * lax.rsqrt(jnp.mean(values * values, axis=-1, keepdims=True) + EPS) * scales


def rotate(values, cos_table, sin_table):
    middle = values.shape[-1] // 2
    leading = values[..., :middle]
    trailing = values[..., middle:]
    return jnp.concatenate(
        [leading * cos_table - trailing * sin_table, trailing * cos_table + leading * sin_table],
        axis=-1,
    )


def angles_of(positions, head_size):
    frequency = 10000.0 ** (-jnp.arange(0, head_size, 2, dtype=jnp.float32) / head_size)
    angles = positions.astype(jnp.float32)[:, None] * frequency[None, :]
    return (jnp.cos(angles)[:, None, :], jnp.sin(angles)[:, None, :])


def swiglu(gate_value, up_value):
    return jax.nn.silu(gate_value) * up_value


def left_trans(left, right):
    return lax.dot_general(
        left, right, (((0,), (0,)), ((), ())), preferred_element_type=jnp.float32
    )


def right_trans(left, right):
    return lax.dot_general(
        left, right, (((1,), (1,)), ((), ())), preferred_element_type=jnp.float32
    )


def _allowed(qpos, own, kpos, kalive, start, width):
    slots = lax.broadcasted_iota(jnp.int32, (1, width), 1) + start
    return (kpos <= qpos) & ((kalive > 0) | (slots == own))


def _attn_fwd_kernel(
    chunk_ref, qblock_ref, q_ref, k_ref, v_ref, qpos_ref, own_ref, kpos_ref, kalive_ref,
    o_ref, lse_ref, m_ref, l_ref, acc_ref, *, heads, halves, chunk, chunks, scale,
):
    rows = q_ref.shape[0] // halves
    for head in range(heads):
        for half in range(halves):
            row_sl = pl.ds(half * rows, rows)
            col_sl = pl.ds(head * HEAD_DIM, HEAD_DIM)
            q = q_ref[row_sl, col_sl]
            qpos = qpos_ref[row_sl, :]
            own = own_ref[row_sl, :]
            limit = qblock_ref[half]

            def scores(c):
                start = pl.multiple_of(c * chunk, chunk)
                k = k_ref[pl.ds(start, chunk), :]
                s = lax.dot_general(
                    q, k, (((1,), (1,)), ((), ())), preferred_element_type=jnp.float32
                ) * scale
                ok = _allowed(
                    qpos, own, kpos_ref[:, pl.ds(start, chunk)],
                    kalive_ref[:, pl.ds(start, chunk)], start, chunk,
                )
                return jnp.where(ok, s, MASKED_SCORE), start

            m_ref[...] = jnp.full(m_ref.shape, -jnp.inf, jnp.float32)
            l_ref[...] = jnp.zeros(l_ref.shape, jnp.float32)

            def stats(c, carry):
                @pl.when(chunk_ref[c] <= limit)
                def _():
                    s, _ = scores(c)
                    m_old = m_ref[...]
                    m_new = jnp.maximum(m_old, jnp.max(s, axis=1, keepdims=True))
                    l_ref[...] = l_ref[...] * jnp.exp(m_old - m_new) + jnp.sum(
                        jnp.exp(s - m_new), axis=1, keepdims=True
                    )
                    m_ref[...] = m_new

                return carry

            lax.fori_loop(0, chunks, stats, 0)
            lse = m_ref[...] + jnp.log(l_ref[...])
            acc_ref[...] = jnp.zeros(acc_ref.shape, jnp.float32)

            def accumulate(c, carry):
                @pl.when(chunk_ref[c] <= limit)
                def _():
                    s, start = scores(c)
                    p = jnp.exp(s - lse).astype(jnp.bfloat16)
                    v = v_ref[pl.ds(start, chunk), :]
                    acc_ref[...] += jnp.dot(p, v, preferred_element_type=jnp.float32)

                return carry

            lax.fori_loop(0, chunks, accumulate, 0)
            o_ref[row_sl, col_sl] = acc_ref[...].astype(o_ref.dtype)
            lse_ref[head, row_sl, :] = lse


def _attn_bwd_kernel(
    chunk_ref, qblock_ref, q_ref, k_ref, v_ref, do_ref, lse_ref, qpos_ref, own_ref, kpos_ref,
    kalive_ref, dq_ref, dk_ref, dv_ref, delta_ref, dqacc_ref, *, heads, halves, chunk, chunks,
    scale,
):
    rows = q_ref.shape[0] // halves
    dk_ref[...] = jnp.zeros(dk_ref.shape, jnp.float32)
    dv_ref[...] = jnp.zeros(dv_ref.shape, jnp.float32)
    for head in range(heads):
        for half in range(halves):
            row_sl = pl.ds(half * rows, rows)
            col_sl = pl.ds(head * HEAD_DIM, HEAD_DIM)
            q = q_ref[row_sl, col_sl]
            do = do_ref[row_sl, col_sl]
            lse = lse_ref[head, row_sl, :]
            qpos = qpos_ref[row_sl, :]
            own = own_ref[row_sl, :]
            limit = qblock_ref[half]

            def probs_of(c):
                start = pl.multiple_of(c * chunk, chunk)
                k = k_ref[pl.ds(start, chunk), :]
                v = v_ref[pl.ds(start, chunk), :]
                s = lax.dot_general(
                    q, k, (((1,), (1,)), ((), ())), preferred_element_type=jnp.float32
                ) * scale
                ok = _allowed(
                    qpos, own, kpos_ref[:, pl.ds(start, chunk)],
                    kalive_ref[:, pl.ds(start, chunk)], start, chunk,
                )
                p = jnp.where(ok, jnp.exp(jnp.where(ok, s, MASKED_SCORE) - lse), 0.0)
                dp = lax.dot_general(
                    do, v, (((1,), (1,)), ((), ())), preferred_element_type=jnp.float32
                )
                return p, dp, k, start

            delta_ref[...] = jnp.zeros(delta_ref.shape, jnp.float32)

            def deltas(c, carry):
                @pl.when(chunk_ref[c] <= limit)
                def _():
                    p, dp, _, _ = probs_of(c)
                    delta_ref[...] += jnp.sum(p * dp, axis=1, keepdims=True)

                return carry

            lax.fori_loop(0, chunks, deltas, 0)
            delta = delta_ref[...]
            dqacc_ref[...] = jnp.zeros(dqacc_ref.shape, jnp.float32)

            def grads(c, carry):
                @pl.when(chunk_ref[c] <= limit)
                def _():
                    p, dp, k, start = probs_of(c)
                    ds = (p * (dp - delta)).astype(jnp.bfloat16)
                    dqacc_ref[...] += jnp.dot(ds, k, preferred_element_type=jnp.float32)
                    key_sl = pl.ds(start, chunk)
                    dk_ref[key_sl, :] += lax.dot_general(
                        ds, q, (((0,), (0,)), ((), ())), preferred_element_type=jnp.float32
                    ) * scale
                    dv_ref[key_sl, :] += lax.dot_general(
                        p.astype(jnp.bfloat16), do, (((0,), (0,)), ((), ())),
                        preferred_element_type=jnp.float32,
                    )

                return carry

            lax.fori_loop(0, chunks, grads, 0)
            dq_ref[row_sl, col_sl] = dqacc_ref[...] * scale


def _common(query_low, all_kv, local_groups):
    rows = query_low.shape[0]
    length = all_kv.shape[0]
    heads = query_low.shape[1] // HEAD_DIM // local_groups
    return rows, length, heads


def attention_forward(query_low, all_kv, chunk_blocks, query_blocks, query_pos, own_ids,
                      key_pos, key_alive, *, local_groups, chunk):
    rows, length, heads = _common(query_low, all_kv, local_groups)
    halves = 2
    chunks = length // chunk
    kernel = functools.partial(
        _attn_fwd_kernel, heads=heads, halves=halves, chunk=chunk, chunks=chunks,
        scale=HEAD_DIM ** (-0.5),
    )
    group_cols = heads * HEAD_DIM
    grid_spec = pltpu.PrefetchScalarGridSpec(
        num_scalar_prefetch=2,
        grid=(local_groups,),
        in_specs=[
            pl.BlockSpec((rows, group_cols), lambda g, *_: (0, g)),
            pl.BlockSpec((length, HEAD_DIM), lambda g, *_: (0, g)),
            pl.BlockSpec((length, HEAD_DIM), lambda g, *_: (0, local_groups + g)),
            pl.BlockSpec((rows, 1), lambda g, *_: (0, 0)),
            pl.BlockSpec((rows, 1), lambda g, *_: (0, 0)),
            pl.BlockSpec((1, length), lambda g, *_: (0, 0)),
            pl.BlockSpec((1, length), lambda g, *_: (0, 0)),
        ],
        out_specs=[
            pl.BlockSpec((rows, group_cols), lambda g, *_: (0, g)),
            pl.BlockSpec((heads, rows, 1), lambda g, *_: (g, 0, 0)),
        ],
        scratch_shapes=[
            pltpu.VMEM((rows // halves, 1), jnp.float32),
            pltpu.VMEM((rows // halves, 1), jnp.float32),
            pltpu.VMEM((rows // halves, HEAD_DIM), jnp.float32),
        ],
    )
    flops = 4 * rows * length * HEAD_DIM * heads * local_groups
    return pl.pallas_call(
        kernel,
        grid_spec=grid_spec,
        out_shape=[
            jax.ShapeDtypeStruct((rows, heads * local_groups * HEAD_DIM), jnp.bfloat16),
            jax.ShapeDtypeStruct((heads * local_groups, rows, 1), jnp.float32),
        ],
        compiler_params=pltpu.CompilerParams(vmem_limit_bytes=48 * 1024 * 1024),
        cost_estimate=pl.CostEstimate(
            flops=flops, transcendentals=rows * length * heads * local_groups,
            bytes_accessed=2 * length * 4 * HEAD_DIM * local_groups,
        ),
    )(chunk_blocks, query_blocks, query_low, all_kv, all_kv, query_pos, own_ids, key_pos,
      key_alive)


def attention_backward(query_low, all_kv, d_attended, lse, chunk_blocks, query_blocks,
                       query_pos, own_ids, key_pos, key_alive, *, local_groups, chunk):
    rows, length, heads = _common(query_low, all_kv, local_groups)
    halves = 2
    chunks = length // chunk
    kernel = functools.partial(
        _attn_bwd_kernel, heads=heads, halves=halves, chunk=chunk, chunks=chunks,
        scale=HEAD_DIM ** (-0.5),
    )
    group_cols = heads * HEAD_DIM
    grid_spec = pltpu.PrefetchScalarGridSpec(
        num_scalar_prefetch=2,
        grid=(local_groups,),
        in_specs=[
            pl.BlockSpec((rows, group_cols), lambda g, *_: (0, g)),
            pl.BlockSpec((length, HEAD_DIM), lambda g, *_: (0, g)),
            pl.BlockSpec((length, HEAD_DIM), lambda g, *_: (0, local_groups + g)),
            pl.BlockSpec((rows, group_cols), lambda g, *_: (0, g)),
            pl.BlockSpec((heads, rows, 1), lambda g, *_: (g, 0, 0)),
            pl.BlockSpec((rows, 1), lambda g, *_: (0, 0)),
            pl.BlockSpec((rows, 1), lambda g, *_: (0, 0)),
            pl.BlockSpec((1, length), lambda g, *_: (0, 0)),
            pl.BlockSpec((1, length), lambda g, *_: (0, 0)),
        ],
        out_specs=[
            pl.BlockSpec((rows, group_cols), lambda g, *_: (0, g)),
            pl.BlockSpec((length, HEAD_DIM), lambda g, *_: (0, g)),
            pl.BlockSpec((length, HEAD_DIM), lambda g, *_: (0, g)),
        ],
        scratch_shapes=[
            pltpu.VMEM((rows // halves, 1), jnp.float32),
            pltpu.VMEM((rows // halves, HEAD_DIM), jnp.float32),
        ],
    )
    flops = 10 * rows * length * HEAD_DIM * heads * local_groups
    kv_width = local_groups * HEAD_DIM
    return pl.pallas_call(
        kernel,
        grid_spec=grid_spec,
        out_shape=[
            jax.ShapeDtypeStruct((rows, heads * local_groups * HEAD_DIM), jnp.float32),
            jax.ShapeDtypeStruct((length, kv_width), jnp.float32),
            jax.ShapeDtypeStruct((length, kv_width), jnp.float32),
        ],
        compiler_params=pltpu.CompilerParams(vmem_limit_bytes=48 * 1024 * 1024),
        cost_estimate=pl.CostEstimate(
            flops=flops, transcendentals=2 * rows * length * heads * local_groups,
            bytes_accessed=2 * length * 4 * HEAD_DIM * local_groups * 3,
        ),
    )(chunk_blocks, query_blocks, query_low, all_kv, all_kv, d_attended, lse, query_pos,
      own_ids, key_pos, key_alive)


def partner_perm(axis_size, mask):
    return [(index, index ^ mask) for index in range(axis_size)]


def permute_sum(parts, dims, axis):
    size = lax.axis_size(axis)
    steps = size.bit_length() - 1
    assert 1 << steps == size
    me = lax.axis_index(axis)
    pieces = list(parts)
    for step in range(steps):
        bit = (me >> step) & 1
        keep, send = [], []
        for piece, dim in zip(pieces, dims):
            half = piece.shape[dim] // 2
            keep.append(lax.dynamic_slice_in_dim(piece, bit * half, half, axis=dim))
            send.append(
                lax.dynamic_slice_in_dim(piece, (1 - bit) * half, half, axis=dim).astype(jnp.bfloat16)
            )
        got = lax.ppermute(send, axis, partner_perm(size, 1 << step))
        pieces = [mine + theirs.astype(jnp.float32) for mine, theirs in zip(keep, got)]
    pieces = [piece.astype(jnp.bfloat16) for piece in pieces]
    for step in reversed(range(steps)):
        first = ((me >> step) & 1) == 0
        got = lax.ppermute(pieces, axis, partner_perm(size, 1 << step))
        pieces = [
            jnp.concatenate(
                [jnp.where(first, mine, theirs), jnp.where(first, theirs, mine)], axis=dim
            )
            for mine, theirs, dim in zip(pieces, got, dims)
        ]
    return [piece.astype(jnp.float32) for piece in pieces]


def permute_allsum(value, axis):
    size = lax.axis_size(axis)
    steps = size.bit_length() - 1
    for step in range(steps):
        value = value + lax.ppermute(value, axis, partner_perm(size, 1 << step))
    return value


def on_device(
    inputs,
    active,
    block_table,
    gain_one,
    w_query,
    w_key,
    w_value,
    w_out,
    gain_two,
    w_gate,
    w_up,
    w_down,
    cotangent,
):
    row_count = inputs.shape[0]
    local_heads = w_query.shape[1] // HEAD_DIM
    local_groups = w_key.shape[1] // HEAD_DIM
    half_rows = row_count // 2
    length = row_count * lax.axis_size("dp")
    key_pos = (
        block_table[:, None] * half_rows + jnp.arange(half_rows, dtype=jnp.int32)[None, :]
    ).reshape(length)
    row_start = lax.axis_index("dp") * row_count
    query_pos = lax.dynamic_slice_in_dim(key_pos, row_start, row_count)
    slot_ids = jnp.arange(length, dtype=jnp.int32)
    own_ids = row_start + jnp.arange(row_count, dtype=jnp.int32)
    cos_table, sin_table = angles_of(query_pos, HEAD_DIM)
    keep_rows = active.astype(jnp.float32)[:, None]
    source = inputs.astype(jnp.float32)
    normed_full, norm_one_back = jax.vjp(rms_norm, source, gain_one.astype(jnp.float32))
    normed = normed_full.astype(jnp.bfloat16)
    query_raw = jnp.dot(normed, w_query, preferred_element_type=jnp.float32).reshape(
        row_count, local_heads, HEAD_DIM
    )
    key_raw = jnp.dot(normed, w_key, preferred_element_type=jnp.float32).reshape(
        row_count, local_groups, HEAD_DIM
    )
    value_low = jnp.dot(normed, w_value, preferred_element_type=jnp.float32).astype(jnp.bfloat16)
    query_low = (
        rotate(query_raw, cos_table, sin_table)
        .reshape(row_count, local_heads * HEAD_DIM)
        .astype(jnp.bfloat16)
    )
    key_low = (
        rotate(key_raw, cos_table, sin_table)
        .reshape(row_count, local_groups * HEAD_DIM)
        .astype(jnp.bfloat16)
    )
    alive_low = active.astype(jnp.bfloat16)

    kv_width = local_groups * HEAD_DIM
    all_kv = lax.all_gather(
        jnp.concatenate([key_low, value_low], axis=1), "dp", axis=0, tiled=True
    )
    all_alive = lax.all_gather(alive_low, "dp", axis=0, tiled=True)
    mask_args = dict(
        chunk_blocks=block_table,
        query_blocks=lax.dynamic_slice_in_dim(block_table, 2 * lax.axis_index("dp"), 2),
        query_pos=query_pos[:, None],
        own_ids=own_ids[:, None],
        key_pos=key_pos[None, :],
        key_alive=(all_alive > 0).astype(jnp.int32)[None, :],
    )
    attended, lse = attention_forward(
        query_low, all_kv, local_groups=local_groups, chunk=half_rows, **mask_args
    )
    branch_part = jnp.dot(attended, w_out, preferred_element_type=jnp.float32)
    branch_top = lax.psum(branch_part[:half_rows].astype(jnp.bfloat16), "tensor")
    (branch_bottom,) = permute_sum([branch_part[half_rows:]], [0], "tensor")
    branch = jnp.concatenate([branch_top.astype(jnp.float32), branch_bottom], axis=0)
    middle = source + keep_rows * branch
    normed_two_full, norm_two_back = jax.vjp(rms_norm, middle, gain_two.astype(jnp.float32))
    normed_two = normed_two_full.astype(jnp.bfloat16)
    gate_value = jnp.dot(normed_two, w_gate, preferred_element_type=jnp.float32)
    up_value = jnp.dot(normed_two, w_up, preferred_element_type=jnp.float32)
    hidden_full, swiglu_back = jax.vjp(swiglu, gate_value, up_value)
    hidden = hidden_full.astype(jnp.bfloat16)
    down_part = jnp.dot(hidden, w_down, preferred_element_type=jnp.float32)
    grad_out = cotangent.astype(jnp.float32)

    def dp_sum(grads):
        return [lax.psum(grad.astype(jnp.bfloat16), "dp") for grad in grads]

    d_down = (keep_rows * grad_out).astype(jnp.bfloat16)
    grad_w_down = left_trans(hidden, d_down)
    d_hidden = right_trans(d_down, w_down)
    d_gate_full, d_up_full = swiglu_back(d_hidden)
    d_gate = d_gate_full.astype(jnp.bfloat16)
    d_up = d_up_full.astype(jnp.bfloat16)
    grad_w_gate = left_trans(normed_two, d_gate)
    grad_w_up = left_trans(normed_two, d_up)
    d_normed_two_part = right_trans(d_gate, w_gate) + right_trans(d_up, w_up)
    grad_w_gate, grad_w_up, grad_w_down, d_normed_two_part = lax.optimization_barrier(
        (grad_w_gate, grad_w_up, grad_w_down, d_normed_two_part)
    )
    mlp_grads = dp_sum([grad_w_gate, grad_w_up, grad_w_down])
    grad_w_gate, grad_w_up, grad_w_down = mlp_grads
    (d_normed_two,) = permute_sum([d_normed_two_part], [0], "tensor")
    down_part, d_normed_two = lax.optimization_barrier((down_part, d_normed_two))
    (down_sum,) = permute_sum([down_part], [0], "tensor")
    d_middle_norm, grad_gain_two = norm_two_back(d_normed_two)
    grad_middle = grad_out + d_middle_norm
    d_branch = (keep_rows * grad_middle).astype(jnp.bfloat16)
    grad_w_out = left_trans(attended, d_branch)
    grad_w_gate, grad_w_up, grad_w_down, grad_w_out = lax.optimization_barrier(
        (grad_w_gate, grad_w_up, grad_w_down, grad_w_out)
    )
    d_attended = right_trans(d_branch, w_out).astype(jnp.bfloat16)
    d_queries, d_key_all, d_value_all = attention_backward(
        query_low, all_kv, d_attended, lse, local_groups=local_groups, chunk=half_rows,
        **mask_args,
    )
    d_kv_cat = jnp.concatenate([d_key_all, d_value_all], axis=1).astype(jnp.bfloat16)
    d_kv_own = lax.psum_scatter(
        d_kv_cat,
        "dp",
        scatter_dimension=0,
        tiled=True,
    ).astype(jnp.float32)
    d_kv_own, grad_w_out = lax.optimization_barrier((d_kv_own, grad_w_out))
    d_key_own = d_kv_own[:, :kv_width]
    d_value_own = d_kv_own[:, kv_width:]
    d_queries = d_queries.reshape(row_count, local_heads, HEAD_DIM)
    d_query_low = (
        rotate(d_queries, cos_table, -sin_table)
        .reshape(row_count, local_heads * HEAD_DIM)
        .astype(jnp.bfloat16)
    )
    d_key_low = (
        rotate(d_key_own.reshape(row_count, local_groups, HEAD_DIM), cos_table, -sin_table)
        .reshape(row_count, local_groups * HEAD_DIM)
        .astype(jnp.bfloat16)
    )
    d_value_low = d_value_own.astype(jnp.bfloat16)
    grad_w_query = left_trans(normed, d_query_low)
    grad_w_key = left_trans(normed, d_key_low)
    grad_w_value = left_trans(normed, d_value_low)
    d_normed_part = (
        right_trans(d_query_low, w_query)
        + right_trans(d_key_low, w_key)
        + right_trans(d_value_low, w_value)
    )
    (
        down_sum,
        d_normed_part,
        grad_w_out,
        grad_w_query,
        grad_w_key,
        grad_w_value,
    ) = lax.optimization_barrier(
        (down_sum, d_normed_part, grad_w_out, grad_w_query, grad_w_key, grad_w_value)
    )
    grad_w_out, grad_w_query, grad_w_key, grad_w_value = dp_sum(
        [grad_w_out, grad_w_query, grad_w_key, grad_w_value]
    )
    grad_w_gate, grad_w_up, grad_w_down = [
        grad.astype(jnp.float32) for grad in (grad_w_gate, grad_w_up, grad_w_down)
    ]
    output = (middle + keep_rows * down_sum).astype(jnp.bfloat16)
    (d_normed,) = permute_sum([d_normed_part], [0], "tensor")
    d_source_norm, grad_gain_one = norm_one_back(d_normed)
    grad_input = grad_middle + d_source_norm
    grad_gain_one = permute_allsum(grad_gain_one, "dp")
    grad_gain_two = permute_allsum(grad_gain_two, "dp")
    grad_w_out, grad_w_query, grad_w_key, grad_w_value = [
        grad.astype(jnp.float32) for grad in (grad_w_out, grad_w_query, grad_w_key, grad_w_value)
    ]
    return (
        output,
        grad_input,
        grad_gain_one,
        grad_w_query,
        grad_w_key,
        grad_w_value,
        grad_w_out,
        grad_gain_two,
        grad_w_gate,
        grad_w_up,
        grad_w_down,
    )


def solution(mesh):
    placed = (
        P("dp", None),
        P("dp"),
        P(),
        P(),
        P(None, "tensor"),
        P(None, "tensor"),
        P(None, "tensor"),
        P("tensor", None),
        P(),
        P(None, "tensor"),
        P(None, "tensor"),
        P("tensor", None),
        P("dp", None),
    )
    return jax.shard_map(
        on_device,
        mesh=mesh,
        in_specs=placed,
        out_specs=(
            P("dp", None),
            P("dp", None),
            P(),
            P(None, "tensor"),
            P(None, "tensor"),
            P(None, "tensor"),
            P("tensor", None),
            P(),
            P(None, "tensor"),
            P(None, "tensor"),
            P("tensor", None),
        ),
        check_vma=False,
    )
```

```python
import functools

import jax
import jax.numpy as jnp
from jax import lax
from jax.experimental import pallas as pl
from jax.experimental.pallas import tpu as pltpu
from jax.sharding import PartitionSpec as P


HEAD_DIM = 128


EPS = 1e-05
MASKED_SCORE = -1e30


def rms_norm(values, scales):
    return values * lax.rsqrt(jnp.mean(values * values, axis=-1, keepdims=True) + EPS) * scales


def rotate(values, cos_table, sin_table):
    middle = values.shape[-1] // 2
    leading = values[..., :middle]
    trailing = values[..., middle:]
    return jnp.concatenate(
        [leading * cos_table - trailing * sin_table, trailing * cos_table + leading * sin_table],
        axis=-1,
    )


def angles_of(positions, head_size):
    frequency = 10000.0 ** (-jnp.arange(0, head_size, 2, dtype=jnp.float32) / head_size)
    angles = positions.astype(jnp.float32)[:, None] * frequency[None, :]
    return (jnp.cos(angles)[:, None, :], jnp.sin(angles)[:, None, :])


def swiglu(gate_value, up_value):
    return jax.nn.silu(gate_value) * up_value


def left_trans(left, right):
    return lax.dot_general(
        left, right, (((0,), (0,)), ((), ())), preferred_element_type=jnp.float32
    )


def right_trans(left, right):
    return lax.dot_general(
        left, right, (((1,), (1,)), ((), ())), preferred_element_type=jnp.float32
    )


def _allowed(qpos, own, kpos, kalive, start, width):
    slots = lax.broadcasted_iota(jnp.int32, (1, width), 1) + start
    return (kpos <= qpos) & ((kalive > 0) | (slots == own))


def _attn_bwd_kernel(
    chunk_ref, qblock_ref, q_ref, k_ref, v_ref, do_ref, lse_ref, qpos_ref, own_ref, kpos_ref,
    kalive_ref, dq_ref, dk_ref, dv_ref, delta_ref, dqacc_ref, *, heads, halves, chunk, chunks,
    scale,
):
    rows = q_ref.shape[0] // halves
    dk_ref[...] = jnp.zeros(dk_ref.shape, jnp.float32)
    dv_ref[...] = jnp.zeros(dv_ref.shape, jnp.float32)
    for head in range(heads):
        for half in range(halves):
            row_sl = pl.ds(half * rows, rows)
            col_sl = pl.ds(head * HEAD_DIM, HEAD_DIM)
            q = q_ref[row_sl, col_sl]
            do = do_ref[row_sl, col_sl]
            lse = lse_ref[head, row_sl, :]
            qpos = qpos_ref[row_sl, :]
            own = own_ref[row_sl, :]
            limit = qblock_ref[half]

            def probs_of(c):
                start = pl.multiple_of(c * chunk, chunk)
                k = k_ref[pl.ds(start, chunk), :]
                v = v_ref[pl.ds(start, chunk), :]
                s = lax.dot_general(
                    q, k, (((1,), (1,)), ((), ())), preferred_element_type=jnp.float32
                ) * scale
                ok = _allowed(
                    qpos, own, kpos_ref[:, pl.ds(start, chunk)],
                    kalive_ref[:, pl.ds(start, chunk)], start, chunk,
                )
                p = jnp.where(ok, jnp.exp(jnp.where(ok, s, MASKED_SCORE) - lse), 0.0)
                dp = lax.dot_general(
                    do, v, (((1,), (1,)), ((), ())), preferred_element_type=jnp.float32
                )
                return p, dp, k, start

            delta_ref[...] = jnp.zeros(delta_ref.shape, jnp.float32)

            def deltas(c, carry):
                @pl.when(chunk_ref[c] <= limit)
                def _():
                    p, dp, _, _ = probs_of(c)
                    delta_ref[...] += jnp.sum(p * dp, axis=1, keepdims=True)

                return carry

            lax.fori_loop(0, chunks, deltas, 0)
            delta = delta_ref[...]
            dqacc_ref[...] = jnp.zeros(dqacc_ref.shape, jnp.float32)

            def grads(c, carry):
                @pl.when(chunk_ref[c] <= limit)
                def _():
                    p, dp, k, start = probs_of(c)
                    ds = (p * (dp - delta)).astype(jnp.bfloat16)
                    dqacc_ref[...] += jnp.dot(ds, k, preferred_element_type=jnp.float32)
                    key_sl = pl.ds(start, chunk)
                    dk_ref[key_sl, :] += lax.dot_general(
                        ds, q, (((0,), (0,)), ((), ())), preferred_element_type=jnp.float32
                    ) * scale
                    dv_ref[key_sl, :] += lax.dot_general(
                        p.astype(jnp.bfloat16), do, (((0,), (0,)), ((), ())),
                        preferred_element_type=jnp.float32,
                    )

                return carry

            lax.fori_loop(0, chunks, grads, 0)
            dq_ref[row_sl, col_sl] = dqacc_ref[...] * scale


def _common(query_low, all_kv, local_groups):
    rows = query_low.shape[0]
    length = all_kv.shape[0]
    heads = query_low.shape[1] // HEAD_DIM // local_groups
    return rows, length, heads


def attention_backward(query_low, all_kv, d_attended, lse, chunk_blocks, query_blocks,
                       query_pos, own_ids, key_pos, key_alive, *, local_groups, chunk):
    rows, length, heads = _common(query_low, all_kv, local_groups)
    halves = 2
    chunks = length // chunk
    kernel = functools.partial(
        _attn_bwd_kernel, heads=heads, halves=halves, chunk=chunk, chunks=chunks,
        scale=HEAD_DIM ** (-0.5),
    )
    group_cols = heads * HEAD_DIM
    grid_spec = pltpu.PrefetchScalarGridSpec(
        num_scalar_prefetch=2,
        grid=(local_groups,),
        in_specs=[
            pl.BlockSpec((rows, group_cols), lambda g, *_: (0, g)),
            pl.BlockSpec((length, HEAD_DIM), lambda g, *_: (0, g)),
            pl.BlockSpec((length, HEAD_DIM), lambda g, *_: (0, local_groups + g)),
            pl.BlockSpec((rows, group_cols), lambda g, *_: (0, g)),
            pl.BlockSpec((heads, rows, 1), lambda g, *_: (g, 0, 0)),
            pl.BlockSpec((rows, 1), lambda g, *_: (0, 0)),
            pl.BlockSpec((rows, 1), lambda g, *_: (0, 0)),
            pl.BlockSpec((1, length), lambda g, *_: (0, 0)),
            pl.BlockSpec((1, length), lambda g, *_: (0, 0)),
        ],
        out_specs=[
            pl.BlockSpec((rows, group_cols), lambda g, *_: (0, g)),
            pl.BlockSpec((length, HEAD_DIM), lambda g, *_: (0, g)),
            pl.BlockSpec((length, HEAD_DIM), lambda g, *_: (0, g)),
        ],
        scratch_shapes=[
            pltpu.VMEM((rows // halves, 1), jnp.float32),
            pltpu.VMEM((rows // halves, HEAD_DIM), jnp.float32),
        ],
    )
    flops = 10 * rows * length * HEAD_DIM * heads * local_groups
    kv_width = local_groups * HEAD_DIM
    return pl.pallas_call(
        kernel,
        grid_spec=grid_spec,
        out_shape=[
            jax.ShapeDtypeStruct((rows, heads * local_groups * HEAD_DIM), jnp.float32),
            jax.ShapeDtypeStruct((length, kv_width), jnp.float32),
            jax.ShapeDtypeStruct((length, kv_width), jnp.float32),
        ],
        compiler_params=pltpu.CompilerParams(vmem_limit_bytes=48 * 1024 * 1024),
        cost_estimate=pl.CostEstimate(
            flops=flops, transcendentals=2 * rows * length * heads * local_groups,
            bytes_accessed=2 * length * 4 * HEAD_DIM * local_groups * 3,
        ),
    )(chunk_blocks, query_blocks, query_low, all_kv, all_kv, d_attended, lse, query_pos,
      own_ids, key_pos, key_alive)


def partner_perm(axis_size, mask):
    return [(index, index ^ mask) for index in range(axis_size)]


def permute_sum(parts, dims, axis):
    size = lax.axis_size(axis)
    steps = size.bit_length() - 1
    assert 1 << steps == size
    me = lax.axis_index(axis)
    pieces = list(parts)
    for step in range(steps):
        bit = (me >> step) & 1
        keep, send = [], []
        for piece, dim in zip(pieces, dims):
            half = piece.shape[dim] // 2
            keep.append(lax.dynamic_slice_in_dim(piece, bit * half, half, axis=dim))
            send.append(
                lax.dynamic_slice_in_dim(piece, (1 - bit) * half, half, axis=dim).astype(jnp.bfloat16)
            )
        got = lax.ppermute(send, axis, partner_perm(size, 1 << step))
        pieces = [mine + theirs.astype(jnp.float32) for mine, theirs in zip(keep, got)]
    pieces = [piece.astype(jnp.bfloat16) for piece in pieces]
    for step in reversed(range(steps)):
        first = ((me >> step) & 1) == 0
        got = lax.ppermute(pieces, axis, partner_perm(size, 1 << step))
        pieces = [
            jnp.concatenate(
                [jnp.where(first, mine, theirs), jnp.where(first, theirs, mine)], axis=dim
            )
            for mine, theirs, dim in zip(pieces, got, dims)
        ]
    return [piece.astype(jnp.float32) for piece in pieces]


def permute_allsum(value, axis):
    size = lax.axis_size(axis)
    steps = size.bit_length() - 1
    for step in range(steps):
        value = value + lax.ppermute(value, axis, partner_perm(size, 1 << step))
    return value


def on_device(
    inputs,
    active,
    block_table,
    gain_one,
    w_query,
    w_key,
    w_value,
    w_out,
    gain_two,
    w_gate,
    w_up,
    w_down,
    cotangent,
):
    row_count = inputs.shape[0]
    local_heads = w_query.shape[1] // HEAD_DIM
    local_groups = w_key.shape[1] // HEAD_DIM
    group_size = local_heads // local_groups
    half_rows = row_count // 2
    length = row_count * lax.axis_size("dp")
    score_scale = HEAD_DIM ** (-0.5)
    key_pos = (
        block_table[:, None] * half_rows + jnp.arange(half_rows, dtype=jnp.int32)[None, :]
    ).reshape(length)
    row_start = lax.axis_index("dp") * row_count
    query_pos = lax.dynamic_slice_in_dim(key_pos, row_start, row_count)
    slot_ids = jnp.arange(length, dtype=jnp.int32)
    own_ids = row_start + jnp.arange(row_count, dtype=jnp.int32)
    cos_table, sin_table = angles_of(query_pos, HEAD_DIM)
    keep_rows = active.astype(jnp.float32)[:, None]
    source = inputs.astype(jnp.float32)
    normed_full, norm_one_back = jax.vjp(rms_norm, source, gain_one.astype(jnp.float32))
    normed = normed_full.astype(jnp.bfloat16)
    query_raw = jnp.dot(normed, w_query, preferred_element_type=jnp.float32).reshape(
        row_count, local_heads, HEAD_DIM
    )
    key_raw = jnp.dot(normed, w_key, preferred_element_type=jnp.float32).reshape(
        row_count, local_groups, HEAD_DIM
    )
    value_low = jnp.dot(normed, w_value, preferred_element_type=jnp.float32).astype(jnp.bfloat16)
    query_low = (
        rotate(query_raw, cos_table, sin_table)
        .reshape(row_count, local_heads * HEAD_DIM)
        .astype(jnp.bfloat16)
    )
    key_low = (
        rotate(key_raw, cos_table, sin_table)
        .reshape(row_count, local_groups * HEAD_DIM)
        .astype(jnp.bfloat16)
    )
    alive_low = active.astype(jnp.bfloat16)

    kv_width = local_groups * HEAD_DIM
    all_kv = lax.all_gather(
        jnp.concatenate([key_low, value_low], axis=1), "dp", axis=0, tiled=True
    )
    all_alive = lax.all_gather(alive_low, "dp", axis=0, tiled=True)
    mask_args = dict(
        chunk_blocks=block_table,
        query_blocks=lax.dynamic_slice_in_dim(block_table, 2 * lax.axis_index("dp"), 2),
        query_pos=query_pos[:, None],
        own_ids=own_ids[:, None],
        key_pos=key_pos[None, :],
        key_alive=(all_alive > 0).astype(jnp.int32)[None, :],
    )

    def allowed_of(alive_all):
        return (key_pos[None, :] <= query_pos[:, None]) & (
            (alive_all[None, :] > 0) | (slot_ids[None, :] == own_ids[:, None])
        )

    def head_scores(head_index, keys_all, allowed):
        query_part = query_low[:, head_index * HEAD_DIM : (head_index + 1) * HEAD_DIM]
        group_index = head_index // group_size
        key_part = keys_all[:, group_index * HEAD_DIM : (group_index + 1) * HEAD_DIM]
        raw_scores = right_trans(query_part, key_part) * score_scale
        return jnp.where(allowed, raw_scores, MASKED_SCORE)

    all_keys = all_kv[:, :kv_width]
    all_values = all_kv[:, kv_width:]
    allowed_fwd = allowed_of(all_alive)
    mixed_parts = []
    lse_parts = []
    for head_index in range(local_heads):
        masked = head_scores(head_index, all_keys, allowed_fwd)
        row_max = jnp.max(masked, axis=1, keepdims=True)
        shifted = jnp.exp(masked - row_max)
        row_total = jnp.sum(shifted, axis=1, keepdims=True)
        probs_low = (shifted / row_total).astype(jnp.bfloat16)
        lse_parts.append(row_max + jnp.log(row_total))
        group_index = head_index // group_size
        value_part = all_values[:, group_index * HEAD_DIM : (group_index + 1) * HEAD_DIM]
        mixed_parts.append(jnp.dot(probs_low, value_part, preferred_element_type=jnp.float32))
    attended = jnp.concatenate(mixed_parts, axis=1).astype(jnp.bfloat16)
    lse = jnp.stack(lse_parts)
    branch_part = jnp.dot(attended, w_out, preferred_element_type=jnp.float32)
    branch_top = lax.psum(branch_part[:half_rows].astype(jnp.bfloat16), "tensor")
    (branch_bottom,) = permute_sum([branch_part[half_rows:]], [0], "tensor")
    branch = jnp.concatenate([branch_top.astype(jnp.float32), branch_bottom], axis=0)
    middle = source + keep_rows * branch
    normed_two_full, norm_two_back = jax.vjp(rms_norm, middle, gain_two.astype(jnp.float32))
    normed_two = normed_two_full.astype(jnp.bfloat16)
    gate_value = jnp.dot(normed_two, w_gate, preferred_element_type=jnp.float32)
    up_value = jnp.dot(normed_two, w_up, preferred_element_type=jnp.float32)
    hidden_full, swiglu_back = jax.vjp(swiglu, gate_value, up_value)
    hidden = hidden_full.astype(jnp.bfloat16)
    down_part = jnp.dot(hidden, w_down, preferred_element_type=jnp.float32)
    grad_out = cotangent.astype(jnp.float32)

    def dp_sum(grads):
        return [lax.psum(grad.astype(jnp.bfloat16), "dp") for grad in grads]

    d_down = (keep_rows * grad_out).astype(jnp.bfloat16)
    grad_w_down = left_trans(hidden, d_down)
    d_hidden = right_trans(d_down, w_down)
    d_gate_full, d_up_full = swiglu_back(d_hidden)
    d_gate = d_gate_full.astype(jnp.bfloat16)
    d_up = d_up_full.astype(jnp.bfloat16)
    grad_w_gate = left_trans(normed_two, d_gate)
    grad_w_up = left_trans(normed_two, d_up)
    d_normed_two_part = right_trans(d_gate, w_gate) + right_trans(d_up, w_up)
    grad_w_gate, grad_w_up, grad_w_down, d_normed_two_part = lax.optimization_barrier(
        (grad_w_gate, grad_w_up, grad_w_down, d_normed_two_part)
    )
    mlp_grads = dp_sum([grad_w_gate, grad_w_up, grad_w_down])
    grad_w_gate, grad_w_up, grad_w_down = mlp_grads
    (d_normed_two,) = permute_sum([d_normed_two_part], [0], "tensor")
    down_part, d_normed_two = lax.optimization_barrier((down_part, d_normed_two))
    (down_sum,) = permute_sum([down_part], [0], "tensor")
    d_middle_norm, grad_gain_two = norm_two_back(d_normed_two)
    grad_middle = grad_out + d_middle_norm
    d_branch = (keep_rows * grad_middle).astype(jnp.bfloat16)
    grad_w_out = left_trans(attended, d_branch)
    grad_w_gate, grad_w_up, grad_w_down, grad_w_out = lax.optimization_barrier(
        (grad_w_gate, grad_w_up, grad_w_down, grad_w_out)
    )
    d_attended = right_trans(d_branch, w_out).astype(jnp.bfloat16)
    d_queries, d_key_all, d_value_all = attention_backward(
        query_low, all_kv, d_attended, lse, local_groups=local_groups, chunk=half_rows,
        **mask_args,
    )
    d_kv_cat = jnp.concatenate([d_key_all, d_value_all], axis=1).astype(jnp.bfloat16)
    d_kv_own = lax.psum_scatter(
        d_kv_cat,
        "dp",
        scatter_dimension=0,
        tiled=True,
    ).astype(jnp.float32)
    d_kv_own, grad_w_out = lax.optimization_barrier((d_kv_own, grad_w_out))
    d_key_own = d_kv_own[:, :kv_width]
    d_value_own = d_kv_own[:, kv_width:]
    d_queries = d_queries.reshape(row_count, local_heads, HEAD_DIM)
    d_query_low = (
        rotate(d_queries, cos_table, -sin_table)
        .reshape(row_count, local_heads * HEAD_DIM)
        .astype(jnp.bfloat16)
    )
    d_key_low = (
        rotate(d_key_own.reshape(row_count, local_groups, HEAD_DIM), cos_table, -sin_table)
        .reshape(row_count, local_groups * HEAD_DIM)
        .astype(jnp.bfloat16)
    )
    d_value_low = d_value_own.astype(jnp.bfloat16)
    grad_w_query = left_trans(normed, d_query_low)
    grad_w_key = left_trans(normed, d_key_low)
    grad_w_value = left_trans(normed, d_value_low)
    d_normed_part = (
        right_trans(d_query_low, w_query)
        + right_trans(d_key_low, w_key)
        + right_trans(d_value_low, w_value)
    )
    (
        down_sum,
        d_normed_part,
        grad_w_out,
        grad_w_query,
        grad_w_key,
        grad_w_value,
    ) = lax.optimization_barrier(
        (down_sum, d_normed_part, grad_w_out, grad_w_query, grad_w_key, grad_w_value)
    )
    grad_w_out, grad_w_query, grad_w_key, grad_w_value = dp_sum(
        [grad_w_out, grad_w_query, grad_w_key, grad_w_value]
    )
    grad_w_gate, grad_w_up, grad_w_down = [
        grad.astype(jnp.float32) for grad in (grad_w_gate, grad_w_up, grad_w_down)
    ]
    output = (middle + keep_rows * down_sum).astype(jnp.bfloat16)
    (d_normed,) = permute_sum([d_normed_part], [0], "tensor")
    d_source_norm, grad_gain_one = norm_one_back(d_normed)
    grad_input = grad_middle + d_source_norm
    grad_gain_one = permute_allsum(grad_gain_one, "dp")
    grad_gain_two = permute_allsum(grad_gain_two, "dp")
    grad_w_out, grad_w_query, grad_w_key, grad_w_value = [
        grad.astype(jnp.float32) for grad in (grad_w_out, grad_w_query, grad_w_key, grad_w_value)
    ]
    return (
        output,
        grad_input,
        grad_gain_one,
        grad_w_query,
        grad_w_key,
        grad_w_value,
        grad_w_out,
        grad_gain_two,
        grad_w_gate,
        grad_w_up,
        grad_w_down,
    )


def solution(mesh):
    placed = (
        P("dp", None),
        P("dp"),
        P(),
        P(),
        P(None, "tensor"),
        P(None, "tensor"),
        P(None, "tensor"),
        P("tensor", None),
        P(),
        P(None, "tensor"),
        P(None, "tensor"),
        P("tensor", None),
        P("dp", None),
    )
    return jax.shard_map(
        on_device,
        mesh=mesh,
        in_specs=placed,
        out_specs=(
            P("dp", None),
            P("dp", None),
            P(),
            P(None, "tensor"),
            P(None, "tensor"),
            P(None, "tensor"),
            P("tensor", None),
            P(),
            P(None, "tensor"),
            P(None, "tensor"),
            P("tensor", None),
        ),
        check_vma=False,
    )
```

```python
import functools

import jax
import jax.numpy as jnp
from jax import lax
from jax.experimental import pallas as pl
from jax.experimental.pallas import tpu as pltpu
from jax.sharding import PartitionSpec as P


HEAD_DIM = 128


EPS = 1e-05
MASKED_SCORE = -1e30


def rms_norm(values, scales):
    return values * lax.rsqrt(jnp.mean(values * values, axis=-1, keepdims=True) + EPS) * scales


def rotate(values, cos_table, sin_table):
    middle = values.shape[-1] // 2
    leading = values[..., :middle]
    trailing = values[..., middle:]
    return jnp.concatenate(
        [leading * cos_table - trailing * sin_table, trailing * cos_table + leading * sin_table],
        axis=-1,
    )


def angles_of(positions, head_size):
    frequency = 10000.0 ** (-jnp.arange(0, head_size, 2, dtype=jnp.float32) / head_size)
    angles = positions.astype(jnp.float32)[:, None] * frequency[None, :]
    return (jnp.cos(angles)[:, None, :], jnp.sin(angles)[:, None, :])


def swiglu(gate_value, up_value):
    return jax.nn.silu(gate_value) * up_value


def left_trans(left, right):
    return lax.dot_general(
        left, right, (((0,), (0,)), ((), ())), preferred_element_type=jnp.float32
    )


def right_trans(left, right):
    return lax.dot_general(
        left, right, (((1,), (1,)), ((), ())), preferred_element_type=jnp.float32
    )


def _allowed(qpos, own, kpos, kalive, start, width):
    slots = lax.broadcasted_iota(jnp.int32, (1, width), 1) + start
    return (kpos <= qpos) & ((kalive > 0) | (slots == own))


def _attn_bwd_kernel(
    chunk_ref, qblock_ref, q_ref, k_ref, v_ref, do_ref, lse_ref, qpos_ref, own_ref, kpos_ref,
    kalive_ref, dq_ref, dk_ref, dv_ref, delta_ref, dqacc_ref, *, heads, halves, chunk, chunks,
    scale,
):
    rows = q_ref.shape[0] // halves
    dk_ref[...] = jnp.zeros(dk_ref.shape, jnp.float32)
    dv_ref[...] = jnp.zeros(dv_ref.shape, jnp.float32)
    for head in range(heads):
        for half in range(halves):
            row_sl = pl.ds(half * rows, rows)
            col_sl = pl.ds(head * HEAD_DIM, HEAD_DIM)
            q = q_ref[row_sl, col_sl]
            do = do_ref[row_sl, col_sl]
            lse = lse_ref[head, row_sl, :]
            qpos = qpos_ref[row_sl, :]
            own = own_ref[row_sl, :]
            limit = qblock_ref[half]

            def probs_of(c):
                start = pl.multiple_of(c * chunk, chunk)
                k = k_ref[pl.ds(start, chunk), :]
                v = v_ref[pl.ds(start, chunk), :]
                s = lax.dot_general(
                    q, k, (((1,), (1,)), ((), ())), preferred_element_type=jnp.float32
                ) * scale
                ok = _allowed(
                    qpos, own, kpos_ref[:, pl.ds(start, chunk)],
                    kalive_ref[:, pl.ds(start, chunk)], start, chunk,
                )
                p = jnp.where(ok, jnp.exp(jnp.where(ok, s, MASKED_SCORE) - lse), 0.0)
                dp = lax.dot_general(
                    do, v, (((1,), (1,)), ((), ())), preferred_element_type=jnp.float32
                )
                return p, dp, k, start

            delta_ref[...] = jnp.zeros(delta_ref.shape, jnp.float32)

            def deltas(c, carry):
                @pl.when(chunk_ref[c] <= limit)
                def _():
                    p, dp, _, _ = probs_of(c)
                    delta_ref[...] += jnp.sum(p * dp, axis=1, keepdims=True)

                return carry

            lax.fori_loop(0, chunks, deltas, 0)
            delta = delta_ref[...]
            dqacc_ref[...] = jnp.zeros(dqacc_ref.shape, jnp.float32)

            def grads(c, carry):
                @pl.when(chunk_ref[c] <= limit)
                def _():
                    p, dp, k, start = probs_of(c)
                    ds = (p * (dp - delta)).astype(jnp.bfloat16)
                    dqacc_ref[...] += jnp.dot(ds, k, preferred_element_type=jnp.float32)
                    key_sl = pl.ds(start, chunk)
                    dk_ref[key_sl, :] += lax.dot_general(
                        ds, q, (((0,), (0,)), ((), ())), preferred_element_type=jnp.float32
                    ) * scale
                    dv_ref[key_sl, :] += lax.dot_general(
                        p.astype(jnp.bfloat16), do, (((0,), (0,)), ((), ())),
                        preferred_element_type=jnp.float32,
                    )

                return carry

            lax.fori_loop(0, chunks, grads, 0)
            dq_ref[row_sl, col_sl] = dqacc_ref[...] * scale


def _common(query_low, all_kv, local_groups):
    rows = query_low.shape[0]
    length = all_kv.shape[0]
    heads = query_low.shape[1] // HEAD_DIM // local_groups
    return rows, length, heads


def attention_backward(query_low, all_kv, d_attended, lse, chunk_blocks, query_blocks,
                       query_pos, own_ids, key_pos, key_alive, *, local_groups, chunk):
    rows, length, heads = _common(query_low, all_kv, local_groups)
    halves = 2
    chunks = length // chunk
    kernel = functools.partial(
        _attn_bwd_kernel, heads=heads, halves=halves, chunk=chunk, chunks=chunks,
        scale=HEAD_DIM ** (-0.5),
    )
    group_cols = heads * HEAD_DIM
    grid_spec = pltpu.PrefetchScalarGridSpec(
        num_scalar_prefetch=2,
        grid=(local_groups,),
        in_specs=[
            pl.BlockSpec((rows, group_cols), lambda g, *_: (0, g)),
            pl.BlockSpec((length, HEAD_DIM), lambda g, *_: (0, g)),
            pl.BlockSpec((length, HEAD_DIM), lambda g, *_: (0, local_groups + g)),
            pl.BlockSpec((rows, group_cols), lambda g, *_: (0, g)),
            pl.BlockSpec((heads, rows, 1), lambda g, *_: (g, 0, 0)),
            pl.BlockSpec((rows, 1), lambda g, *_: (0, 0)),
            pl.BlockSpec((rows, 1), lambda g, *_: (0, 0)),
            pl.BlockSpec((1, length), lambda g, *_: (0, 0)),
            pl.BlockSpec((1, length), lambda g, *_: (0, 0)),
        ],
        out_specs=[
            pl.BlockSpec((rows, group_cols), lambda g, *_: (0, g)),
            pl.BlockSpec((length, HEAD_DIM), lambda g, *_: (0, g)),
            pl.BlockSpec((length, HEAD_DIM), lambda g, *_: (0, g)),
        ],
        scratch_shapes=[
            pltpu.VMEM((rows // halves, 1), jnp.float32),
            pltpu.VMEM((rows // halves, HEAD_DIM), jnp.float32),
        ],
    )
    flops = 10 * rows * length * HEAD_DIM * heads * local_groups
    kv_width = local_groups * HEAD_DIM
    return pl.pallas_call(
        kernel,
        grid_spec=grid_spec,
        out_shape=[
            jax.ShapeDtypeStruct((rows, heads * local_groups * HEAD_DIM), jnp.float32),
            jax.ShapeDtypeStruct((length, kv_width), jnp.float32),
            jax.ShapeDtypeStruct((length, kv_width), jnp.float32),
        ],
        compiler_params=pltpu.CompilerParams(vmem_limit_bytes=48 * 1024 * 1024),
        cost_estimate=pl.CostEstimate(
            flops=flops, transcendentals=2 * rows * length * heads * local_groups,
            bytes_accessed=2 * length * 4 * HEAD_DIM * local_groups * 3,
        ),
    )(chunk_blocks, query_blocks, query_low, all_kv, all_kv, d_attended, lse, query_pos,
      own_ids, key_pos, key_alive)


def partner_perm(axis_size, mask):
    return [(index, index ^ mask) for index in range(axis_size)]


def permute_sum(parts, dims, axis):
    size = lax.axis_size(axis)
    steps = size.bit_length() - 1
    assert 1 << steps == size
    me = lax.axis_index(axis)
    pieces = list(parts)
    for step in range(steps):
        bit = (me >> step) & 1
        keep, send = [], []
        for piece, dim in zip(pieces, dims):
            half = piece.shape[dim] // 2
            keep.append(lax.dynamic_slice_in_dim(piece, bit * half, half, axis=dim))
            send.append(
                lax.dynamic_slice_in_dim(piece, (1 - bit) * half, half, axis=dim).astype(jnp.bfloat16)
            )
        got = lax.ppermute(send, axis, partner_perm(size, 1 << step))
        pieces = [mine + theirs.astype(jnp.float32) for mine, theirs in zip(keep, got)]
    pieces = [piece.astype(jnp.bfloat16) for piece in pieces]
    for step in reversed(range(steps)):
        first = ((me >> step) & 1) == 0
        got = lax.ppermute(pieces, axis, partner_perm(size, 1 << step))
        pieces = [
            jnp.concatenate(
                [jnp.where(first, mine, theirs), jnp.where(first, theirs, mine)], axis=dim
            )
            for mine, theirs, dim in zip(pieces, got, dims)
        ]
    return [piece.astype(jnp.float32) for piece in pieces]


def permute_allsum(value, axis):
    size = lax.axis_size(axis)
    steps = size.bit_length() - 1
    for step in range(steps):
        value = value + lax.ppermute(value, axis, partner_perm(size, 1 << step))
    return value


def on_device(
    inputs,
    active,
    block_table,
    gain_one,
    w_query,
    w_key,
    w_value,
    w_out,
    gain_two,
    w_gate,
    w_up,
    w_down,
    cotangent,
):
    row_count = inputs.shape[0]
    local_heads = w_query.shape[1] // HEAD_DIM
    local_groups = w_key.shape[1] // HEAD_DIM
    group_size = local_heads // local_groups
    half_rows = row_count // 2
    length = row_count * lax.axis_size("dp")
    score_scale = HEAD_DIM ** (-0.5)
    key_pos = (
        block_table[:, None] * half_rows + jnp.arange(half_rows, dtype=jnp.int32)[None, :]
    ).reshape(length)
    row_start = lax.axis_index("dp") * row_count
    query_pos = lax.dynamic_slice_in_dim(key_pos, row_start, row_count)
    slot_ids = jnp.arange(length, dtype=jnp.int32)
    own_ids = row_start + jnp.arange(row_count, dtype=jnp.int32)
    cos_table, sin_table = angles_of(query_pos, HEAD_DIM)
    keep_rows = active.astype(jnp.float32)[:, None]
    source = inputs.astype(jnp.float32)
    normed_full, norm_one_back = jax.vjp(rms_norm, source, gain_one.astype(jnp.float32))
    normed = normed_full.astype(jnp.bfloat16)
    query_raw = jnp.dot(normed, w_query, preferred_element_type=jnp.float32).reshape(
        row_count, local_heads, HEAD_DIM
    )
    key_raw = jnp.dot(normed, w_key, preferred_element_type=jnp.float32).reshape(
        row_count, local_groups, HEAD_DIM
    )
    value_low = jnp.dot(normed, w_value, preferred_element_type=jnp.float32).astype(jnp.bfloat16)
    query_low = (
        rotate(query_raw, cos_table, sin_table)
        .reshape(row_count, local_heads * HEAD_DIM)
        .astype(jnp.bfloat16)
    )
    key_low = (
        rotate(key_raw, cos_table, sin_table)
        .reshape(row_count, local_groups * HEAD_DIM)
        .astype(jnp.bfloat16)
    )
    alive_low = active.astype(jnp.bfloat16)

    kv_width = local_groups * HEAD_DIM
    all_kv = lax.all_gather(
        jnp.concatenate([key_low, value_low], axis=1), "dp", axis=0, tiled=True
    )
    all_alive = lax.all_gather(alive_low, "dp", axis=0, tiled=True)
    mask_args = dict(
        chunk_blocks=block_table,
        query_blocks=lax.dynamic_slice_in_dim(block_table, 2 * lax.axis_index("dp"), 2),
        query_pos=query_pos[:, None],
        own_ids=own_ids[:, None],
        key_pos=key_pos[None, :],
        key_alive=(all_alive > 0).astype(jnp.int32)[None, :],
    )

    def allowed_of(alive_all):
        return (key_pos[None, :] <= query_pos[:, None]) & (
            (alive_all[None, :] > 0) | (slot_ids[None, :] == own_ids[:, None])
        )

    def head_scores(head_index, keys_all, allowed):
        query_part = query_low[:, head_index * HEAD_DIM : (head_index + 1) * HEAD_DIM]
        group_index = head_index // group_size
        key_part = keys_all[:, group_index * HEAD_DIM : (group_index + 1) * HEAD_DIM]
        raw_scores = right_trans(query_part, key_part) * score_scale
        return jnp.where(allowed, raw_scores, MASKED_SCORE)

    all_keys = all_kv[:, :kv_width]
    all_values = all_kv[:, kv_width:]
    allowed_fwd = allowed_of(all_alive)
    mixed_parts = []
    lse_parts = []
    for head_index in range(local_heads):
        masked = head_scores(head_index, all_keys, allowed_fwd)
        row_max = jnp.max(masked, axis=1, keepdims=True)
        shifted = jnp.exp(masked - row_max)
        row_total = jnp.sum(shifted, axis=1, keepdims=True)
        probs_low = (shifted / row_total).astype(jnp.bfloat16)
        lse_parts.append(row_max + jnp.log(row_total))
        group_index = head_index // group_size
        value_part = all_values[:, group_index * HEAD_DIM : (group_index + 1) * HEAD_DIM]
        mixed_parts.append(jnp.dot(probs_low, value_part, preferred_element_type=jnp.float32))
    attended = jnp.concatenate(mixed_parts, axis=1).astype(jnp.bfloat16)
    lse = jnp.stack(lse_parts)
    branch_part = jnp.dot(attended, w_out, preferred_element_type=jnp.float32)
    sc_rows = row_count * 5 // 8
    branch_top = lax.psum(branch_part[:sc_rows].astype(jnp.bfloat16), "tensor")
    (branch_bottom,) = permute_sum([branch_part[sc_rows:]], [0], "tensor")
    branch = jnp.concatenate([branch_top.astype(jnp.float32), branch_bottom], axis=0)
    middle = source + keep_rows * branch
    normed_two_full, norm_two_back = jax.vjp(rms_norm, middle, gain_two.astype(jnp.float32))
    normed_two = normed_two_full.astype(jnp.bfloat16)
    gate_value = jnp.dot(normed_two, w_gate, preferred_element_type=jnp.float32)
    up_value = jnp.dot(normed_two, w_up, preferred_element_type=jnp.float32)
    hidden_full, swiglu_back = jax.vjp(swiglu, gate_value, up_value)
    hidden = hidden_full.astype(jnp.bfloat16)
    down_part = jnp.dot(hidden, w_down, preferred_element_type=jnp.float32)
    grad_out = cotangent.astype(jnp.float32)

    def dp_sum(grads):
        return [lax.psum(grad.astype(jnp.bfloat16), "dp") for grad in grads]

    d_down = (keep_rows * grad_out).astype(jnp.bfloat16)
    grad_w_down = left_trans(hidden, d_down)
    d_hidden = right_trans(d_down, w_down)
    d_gate_full, d_up_full = swiglu_back(d_hidden)
    d_gate = d_gate_full.astype(jnp.bfloat16)
    d_up = d_up_full.astype(jnp.bfloat16)
    grad_w_gate = left_trans(normed_two, d_gate)
    grad_w_up = left_trans(normed_two, d_up)
    d_normed_two_part = right_trans(d_gate, w_gate) + right_trans(d_up, w_up)
    grad_w_gate, grad_w_up, grad_w_down, d_normed_two_part = lax.optimization_barrier(
        (grad_w_gate, grad_w_up, grad_w_down, d_normed_two_part)
    )
    mlp_grads = dp_sum([grad_w_gate, grad_w_up, grad_w_down])
    grad_w_gate, grad_w_up, grad_w_down = mlp_grads
    (d_normed_two,) = permute_sum([d_normed_two_part], [0], "tensor")
    down_part, d_normed_two = lax.optimization_barrier((down_part, d_normed_two))
    (down_sum,) = permute_sum([down_part], [0], "tensor")
    d_middle_norm, grad_gain_two = norm_two_back(d_normed_two)
    grad_middle = grad_out + d_middle_norm
    d_branch = (keep_rows * grad_middle).astype(jnp.bfloat16)
    grad_w_out = left_trans(attended, d_branch)
    grad_w_gate, grad_w_up, grad_w_down, grad_w_out = lax.optimization_barrier(
        (grad_w_gate, grad_w_up, grad_w_down, grad_w_out)
    )
    d_attended = right_trans(d_branch, w_out).astype(jnp.bfloat16)
    d_queries, d_key_all, d_value_all = attention_backward(
        query_low, all_kv, d_attended, lse, local_groups=local_groups, chunk=half_rows,
        **mask_args,
    )
    d_kv_cat = jnp.concatenate([d_key_all, d_value_all], axis=1).astype(jnp.bfloat16)
    d_kv_own = lax.psum_scatter(
        d_kv_cat,
        "dp",
        scatter_dimension=0,
        tiled=True,
    ).astype(jnp.float32)
    d_kv_own, grad_w_out = lax.optimization_barrier((d_kv_own, grad_w_out))
    d_key_own = d_kv_own[:, :kv_width]
    d_value_own = d_kv_own[:, kv_width:]
    d_queries = d_queries.reshape(row_count, local_heads, HEAD_DIM)
    d_query_low = (
        rotate(d_queries, cos_table, -sin_table)
        .reshape(row_count, local_heads * HEAD_DIM)
        .astype(jnp.bfloat16)
    )
    d_key_low = (
        rotate(d_key_own.reshape(row_count, local_groups, HEAD_DIM), cos_table, -sin_table)
        .reshape(row_count, local_groups * HEAD_DIM)
        .astype(jnp.bfloat16)
    )
    d_value_low = d_value_own.astype(jnp.bfloat16)
    grad_w_query = left_trans(normed, d_query_low)
    grad_w_key = left_trans(normed, d_key_low)
    grad_w_value = left_trans(normed, d_value_low)
    d_normed_part = (
        right_trans(d_query_low, w_query)
        + right_trans(d_key_low, w_key)
        + right_trans(d_value_low, w_value)
    )
    (
        down_sum,
        d_normed_part,
        grad_w_out,
        grad_w_query,
        grad_w_key,
        grad_w_value,
    ) = lax.optimization_barrier(
        (down_sum, d_normed_part, grad_w_out, grad_w_query, grad_w_key, grad_w_value)
    )
    grad_w_out, grad_w_query, grad_w_key, grad_w_value = dp_sum(
        [grad_w_out, grad_w_query, grad_w_key, grad_w_value]
    )
    grad_w_gate, grad_w_up, grad_w_down = [
        grad.astype(jnp.float32) for grad in (grad_w_gate, grad_w_up, grad_w_down)
    ]
    output = (middle + keep_rows * down_sum).astype(jnp.bfloat16)
    (d_normed,) = permute_sum([d_normed_part], [0], "tensor")
    d_source_norm, grad_gain_one = norm_one_back(d_normed)
    grad_input = grad_middle + d_source_norm
    grad_gain_one = permute_allsum(grad_gain_one, "dp")
    grad_gain_two = permute_allsum(grad_gain_two, "dp")
    grad_w_out, grad_w_query, grad_w_key, grad_w_value = [
        grad.astype(jnp.float32) for grad in (grad_w_out, grad_w_query, grad_w_key, grad_w_value)
    ]
    return (
        output,
        grad_input,
        grad_gain_one,
        grad_w_query,
        grad_w_key,
        grad_w_value,
        grad_w_out,
        grad_gain_two,
        grad_w_gate,
        grad_w_up,
        grad_w_down,
    )


def solution(mesh):
    placed = (
        P("dp", None),
        P("dp"),
        P(),
        P(),
        P(None, "tensor"),
        P(None, "tensor"),
        P(None, "tensor"),
        P("tensor", None),
        P(),
        P(None, "tensor"),
        P(None, "tensor"),
        P("tensor", None),
        P("dp", None),
    )
    return jax.shard_map(
        on_device,
        mesh=mesh,
        in_specs=placed,
        out_specs=(
            P("dp", None),
            P("dp", None),
            P(),
            P(None, "tensor"),
            P(None, "tensor"),
            P(None, "tensor"),
            P("tensor", None),
            P(),
            P(None, "tensor"),
            P(None, "tensor"),
            P("tensor", None),
        ),
        check_vma=False,
    )
```

```python
import functools

import jax
import jax.numpy as jnp
from jax import lax
from jax.experimental import pallas as pl
from jax.experimental.pallas import tpu as pltpu
from jax.sharding import PartitionSpec as P


HEAD_DIM = 128


EPS = 1e-05
MASKED_SCORE = -1e30


def rms_norm(values, scales):
    return values * lax.rsqrt(jnp.mean(values * values, axis=-1, keepdims=True) + EPS) * scales


def rotate(values, cos_table, sin_table):
    middle = values.shape[-1] // 2
    leading = values[..., :middle]
    trailing = values[..., middle:]
    return jnp.concatenate(
        [leading * cos_table - trailing * sin_table, trailing * cos_table + leading * sin_table],
        axis=-1,
    )


def angles_of(positions, head_size):
    frequency = 10000.0 ** (-jnp.arange(0, head_size, 2, dtype=jnp.float32) / head_size)
    angles = positions.astype(jnp.float32)[:, None] * frequency[None, :]
    return (jnp.cos(angles)[:, None, :], jnp.sin(angles)[:, None, :])


def swiglu(gate_value, up_value):
    return jax.nn.silu(gate_value) * up_value


def left_trans(left, right):
    return lax.dot_general(
        left, right, (((0,), (0,)), ((), ())), preferred_element_type=jnp.float32
    )


def right_trans(left, right):
    return lax.dot_general(
        left, right, (((1,), (1,)), ((), ())), preferred_element_type=jnp.float32
    )


def _allowed(qpos, own, kpos, kalive, start, width):
    slots = lax.broadcasted_iota(jnp.int32, (1, width), 1) + start
    return (kpos <= qpos) & ((kalive > 0) | (slots == own))


def _attn_bwd_kernel(
    chunk_ref, qblock_ref, q_ref, k_ref, v_ref, do_ref, lse_ref, qpos_ref, own_ref, kpos_ref,
    kalive_ref, dq_ref, dk_ref, dv_ref, delta_ref, dqacc_ref, *, heads, halves, chunk, chunks,
    scale,
):
    rows = q_ref.shape[0] // halves
    dk_ref[...] = jnp.zeros(dk_ref.shape, jnp.float32)
    dv_ref[...] = jnp.zeros(dv_ref.shape, jnp.float32)
    for head in range(heads):
        for half in range(halves):
            row_sl = pl.ds(half * rows, rows)
            col_sl = pl.ds(head * HEAD_DIM, HEAD_DIM)
            q = q_ref[row_sl, col_sl]
            do = do_ref[row_sl, col_sl]
            lse = lse_ref[head, row_sl, :]
            qpos = qpos_ref[row_sl, :]
            own = own_ref[row_sl, :]
            limit = qblock_ref[half]

            def probs_of(c):
                start = pl.multiple_of(c * chunk, chunk)
                k = k_ref[pl.ds(start, chunk), :]
                v = v_ref[pl.ds(start, chunk), :]
                s = lax.dot_general(
                    q, k, (((1,), (1,)), ((), ())), preferred_element_type=jnp.float32
                ) * scale
                ok = _allowed(
                    qpos, own, kpos_ref[:, pl.ds(start, chunk)],
                    kalive_ref[:, pl.ds(start, chunk)], start, chunk,
                )
                p = jnp.where(ok, jnp.exp(jnp.where(ok, s, MASKED_SCORE) - lse), 0.0)
                dp = lax.dot_general(
                    do, v, (((1,), (1,)), ((), ())), preferred_element_type=jnp.float32
                )
                return p, dp, k, start

            delta_ref[...] = jnp.zeros(delta_ref.shape, jnp.float32)

            def deltas(c, carry):
                @pl.when(chunk_ref[c] <= limit)
                def _():
                    p, dp, _, _ = probs_of(c)
                    delta_ref[...] += jnp.sum(p * dp, axis=1, keepdims=True)

                return carry

            lax.fori_loop(0, chunks, deltas, 0)
            delta = delta_ref[...]
            dqacc_ref[...] = jnp.zeros(dqacc_ref.shape, jnp.float32)

            def grads(c, carry):
                @pl.when(chunk_ref[c] <= limit)
                def _():
                    p, dp, k, start = probs_of(c)
                    ds = (p * (dp - delta)).astype(jnp.bfloat16)
                    dqacc_ref[...] += jnp.dot(ds, k, preferred_element_type=jnp.float32)
                    key_sl = pl.ds(start, chunk)
                    dk_ref[key_sl, :] += lax.dot_general(
                        ds, q, (((0,), (0,)), ((), ())), preferred_element_type=jnp.float32
                    ) * scale
                    dv_ref[key_sl, :] += lax.dot_general(
                        p.astype(jnp.bfloat16), do, (((0,), (0,)), ((), ())),
                        preferred_element_type=jnp.float32,
                    )

                return carry

            lax.fori_loop(0, chunks, grads, 0)
            dq_ref[row_sl, col_sl] = dqacc_ref[...] * scale


def _common(query_low, all_kv, local_groups):
    rows = query_low.shape[0]
    length = all_kv.shape[0]
    heads = query_low.shape[1] // HEAD_DIM // local_groups
    return rows, length, heads


def attention_backward(query_low, all_kv, d_attended, lse, chunk_blocks, query_blocks,
                       query_pos, own_ids, key_pos, key_alive, *, local_groups, chunk):
    rows, length, heads = _common(query_low, all_kv, local_groups)
    halves = 2
    chunks = length // chunk
    kernel = functools.partial(
        _attn_bwd_kernel, heads=heads, halves=halves, chunk=chunk, chunks=chunks,
        scale=HEAD_DIM ** (-0.5),
    )
    group_cols = heads * HEAD_DIM
    grid_spec = pltpu.PrefetchScalarGridSpec(
        num_scalar_prefetch=2,
        grid=(local_groups,),
        in_specs=[
            pl.BlockSpec((rows, group_cols), lambda g, *_: (0, g)),
            pl.BlockSpec((length, HEAD_DIM), lambda g, *_: (0, g)),
            pl.BlockSpec((length, HEAD_DIM), lambda g, *_: (0, local_groups + g)),
            pl.BlockSpec((rows, group_cols), lambda g, *_: (0, g)),
            pl.BlockSpec((heads, rows, 1), lambda g, *_: (g, 0, 0)),
            pl.BlockSpec((rows, 1), lambda g, *_: (0, 0)),
            pl.BlockSpec((rows, 1), lambda g, *_: (0, 0)),
            pl.BlockSpec((1, length), lambda g, *_: (0, 0)),
            pl.BlockSpec((1, length), lambda g, *_: (0, 0)),
        ],
        out_specs=[
            pl.BlockSpec((rows, group_cols), lambda g, *_: (0, g)),
            pl.BlockSpec((length, HEAD_DIM), lambda g, *_: (0, g)),
            pl.BlockSpec((length, HEAD_DIM), lambda g, *_: (0, g)),
        ],
        scratch_shapes=[
            pltpu.VMEM((rows // halves, 1), jnp.float32),
            pltpu.VMEM((rows // halves, HEAD_DIM), jnp.float32),
        ],
    )
    flops = 10 * rows * length * HEAD_DIM * heads * local_groups
    kv_width = local_groups * HEAD_DIM
    return pl.pallas_call(
        kernel,
        grid_spec=grid_spec,
        out_shape=[
            jax.ShapeDtypeStruct((rows, heads * local_groups * HEAD_DIM), jnp.float32),
            jax.ShapeDtypeStruct((length, kv_width), jnp.float32),
            jax.ShapeDtypeStruct((length, kv_width), jnp.float32),
        ],
        compiler_params=pltpu.CompilerParams(vmem_limit_bytes=48 * 1024 * 1024),
        cost_estimate=pl.CostEstimate(
            flops=flops, transcendentals=2 * rows * length * heads * local_groups,
            bytes_accessed=2 * length * 4 * HEAD_DIM * local_groups * 3,
        ),
    )(chunk_blocks, query_blocks, query_low, all_kv, all_kv, d_attended, lse, query_pos,
      own_ids, key_pos, key_alive)


def partner_perm(axis_size, mask):
    return [(index, index ^ mask) for index in range(axis_size)]


def permute_sum(parts, dims, axis):
    size = lax.axis_size(axis)
    steps = size.bit_length() - 1
    assert 1 << steps == size
    me = lax.axis_index(axis)
    pieces = list(parts)
    for step in range(steps):
        bit = (me >> step) & 1
        keep, send = [], []
        for piece, dim in zip(pieces, dims):
            half = piece.shape[dim] // 2
            keep.append(lax.dynamic_slice_in_dim(piece, bit * half, half, axis=dim))
            send.append(
                lax.dynamic_slice_in_dim(piece, (1 - bit) * half, half, axis=dim).astype(jnp.bfloat16)
            )
        got = lax.ppermute(send, axis, partner_perm(size, 1 << step))
        pieces = [mine + theirs.astype(jnp.float32) for mine, theirs in zip(keep, got)]
    pieces = [piece.astype(jnp.bfloat16) for piece in pieces]
    for step in reversed(range(steps)):
        first = ((me >> step) & 1) == 0
        got = lax.ppermute(pieces, axis, partner_perm(size, 1 << step))
        pieces = [
            jnp.concatenate(
                [jnp.where(first, mine, theirs), jnp.where(first, theirs, mine)], axis=dim
            )
            for mine, theirs, dim in zip(pieces, got, dims)
        ]
    return [piece.astype(jnp.float32) for piece in pieces]


def permute_scatter(value, axis):
    size = lax.axis_size(axis)
    steps = size.bit_length() - 1
    assert 1 << steps == size
    block = value.shape[0] // size

    def reverse(index):
        return int(format(index, f"0{steps}b")[::-1], 2) if steps else 0

    value = jnp.concatenate(
        [value[reverse(place) * block : (reverse(place) + 1) * block] for place in range(size)], axis=0
    )
    me = lax.axis_index(axis)
    for step in range(steps):
        bit = (me >> step) & 1
        half = value.shape[0] // 2
        keep = lax.dynamic_slice_in_dim(value, bit * half, half, axis=0)
        send = lax.dynamic_slice_in_dim(value, (1 - bit) * half, half, axis=0).astype(jnp.bfloat16)
        got = lax.ppermute(send, axis, partner_perm(size, 1 << step))
        value = keep.astype(jnp.float32) + got.astype(jnp.float32)
    return value


def permute_allsum(value, axis):
    size = lax.axis_size(axis)
    steps = size.bit_length() - 1
    for step in range(steps):
        value = value + lax.ppermute(value, axis, partner_perm(size, 1 << step))
    return value


def on_device(
    inputs,
    active,
    block_table,
    gain_one,
    w_query,
    w_key,
    w_value,
    w_out,
    gain_two,
    w_gate,
    w_up,
    w_down,
    cotangent,
):
    row_count = inputs.shape[0]
    local_heads = w_query.shape[1] // HEAD_DIM
    local_groups = w_key.shape[1] // HEAD_DIM
    group_size = local_heads // local_groups
    half_rows = row_count // 2
    length = row_count * lax.axis_size("dp")
    score_scale = HEAD_DIM ** (-0.5)
    key_pos = (
        block_table[:, None] * half_rows + jnp.arange(half_rows, dtype=jnp.int32)[None, :]
    ).reshape(length)
    row_start = lax.axis_index("dp") * row_count
    query_pos = lax.dynamic_slice_in_dim(key_pos, row_start, row_count)
    slot_ids = jnp.arange(length, dtype=jnp.int32)
    own_ids = row_start + jnp.arange(row_count, dtype=jnp.int32)
    cos_table, sin_table = angles_of(query_pos, HEAD_DIM)
    keep_rows = active.astype(jnp.float32)[:, None]
    source = inputs.astype(jnp.float32)
    normed_full, norm_one_back = jax.vjp(rms_norm, source, gain_one.astype(jnp.float32))
    normed = normed_full.astype(jnp.bfloat16)
    query_raw = jnp.dot(normed, w_query, preferred_element_type=jnp.float32).reshape(
        row_count, local_heads, HEAD_DIM
    )
    key_raw = jnp.dot(normed, w_key, preferred_element_type=jnp.float32).reshape(
        row_count, local_groups, HEAD_DIM
    )
    value_low = jnp.dot(normed, w_value, preferred_element_type=jnp.float32).astype(jnp.bfloat16)
    query_low = (
        rotate(query_raw, cos_table, sin_table)
        .reshape(row_count, local_heads * HEAD_DIM)
        .astype(jnp.bfloat16)
    )
    key_low = (
        rotate(key_raw, cos_table, sin_table)
        .reshape(row_count, local_groups * HEAD_DIM)
        .astype(jnp.bfloat16)
    )
    alive_low = active.astype(jnp.bfloat16)

    kv_width = local_groups * HEAD_DIM
    all_kv = lax.all_gather(
        jnp.concatenate([key_low, value_low], axis=1), "dp", axis=0, tiled=True
    )
    all_alive = lax.all_gather(alive_low, "dp", axis=0, tiled=True)
    mask_args = dict(
        chunk_blocks=block_table,
        query_blocks=lax.dynamic_slice_in_dim(block_table, 2 * lax.axis_index("dp"), 2),
        query_pos=query_pos[:, None],
        own_ids=own_ids[:, None],
        key_pos=key_pos[None, :],
        key_alive=(all_alive > 0).astype(jnp.int32)[None, :],
    )

    def allowed_of(alive_all):
        return (key_pos[None, :] <= query_pos[:, None]) & (
            (alive_all[None, :] > 0) | (slot_ids[None, :] == own_ids[:, None])
        )

    def head_scores(head_index, keys_all, allowed):
        query_part = query_low[:, head_index * HEAD_DIM : (head_index + 1) * HEAD_DIM]
        group_index = head_index // group_size
        key_part = keys_all[:, group_index * HEAD_DIM : (group_index + 1) * HEAD_DIM]
        raw_scores = right_trans(query_part, key_part) * score_scale
        return jnp.where(allowed, raw_scores, MASKED_SCORE)

    all_keys = all_kv[:, :kv_width]
    all_values = all_kv[:, kv_width:]
    allowed_fwd = allowed_of(all_alive)
    mixed_parts = []
    lse_parts = []
    for head_index in range(local_heads):
        masked = head_scores(head_index, all_keys, allowed_fwd)
        row_max = jnp.max(masked, axis=1, keepdims=True)
        shifted = jnp.exp(masked - row_max)
        row_total = jnp.sum(shifted, axis=1, keepdims=True)
        probs_low = (shifted / row_total).astype(jnp.bfloat16)
        lse_parts.append(row_max + jnp.log(row_total))
        group_index = head_index // group_size
        value_part = all_values[:, group_index * HEAD_DIM : (group_index + 1) * HEAD_DIM]
        mixed_parts.append(jnp.dot(probs_low, value_part, preferred_element_type=jnp.float32))
    attended = jnp.concatenate(mixed_parts, axis=1).astype(jnp.bfloat16)
    lse = jnp.stack(lse_parts)
    branch_part = jnp.dot(attended, w_out, preferred_element_type=jnp.float32)
    sc_rows = row_count * 5 // 8
    branch_top = lax.psum(branch_part[:sc_rows].astype(jnp.bfloat16), "tensor")
    (branch_bottom,) = permute_sum([branch_part[sc_rows:]], [0], "tensor")
    branch = jnp.concatenate([branch_top.astype(jnp.float32), branch_bottom], axis=0)
    middle = source + keep_rows * branch
    normed_two_full, norm_two_back = jax.vjp(rms_norm, middle, gain_two.astype(jnp.float32))
    normed_two = normed_two_full.astype(jnp.bfloat16)
    gate_value = jnp.dot(normed_two, w_gate, preferred_element_type=jnp.float32)
    up_value = jnp.dot(normed_two, w_up, preferred_element_type=jnp.float32)
    hidden_full, swiglu_back = jax.vjp(swiglu, gate_value, up_value)
    hidden = hidden_full.astype(jnp.bfloat16)
    down_part = jnp.dot(hidden, w_down, preferred_element_type=jnp.float32)
    grad_out = cotangent.astype(jnp.float32)

    def dp_sum(grads):
        return [lax.psum(grad.astype(jnp.bfloat16), "dp") for grad in grads]

    d_down = (keep_rows * grad_out).astype(jnp.bfloat16)
    grad_w_down = left_trans(hidden, d_down)
    d_hidden = right_trans(d_down, w_down)
    d_gate_full, d_up_full = swiglu_back(d_hidden)
    d_gate = d_gate_full.astype(jnp.bfloat16)
    d_up = d_up_full.astype(jnp.bfloat16)
    grad_w_gate = left_trans(normed_two, d_gate)
    grad_w_up = left_trans(normed_two, d_up)
    d_normed_two_part = right_trans(d_gate, w_gate) + right_trans(d_up, w_up)
    grad_w_gate, grad_w_up, grad_w_down, d_normed_two_part = lax.optimization_barrier(
        (grad_w_gate, grad_w_up, grad_w_down, d_normed_two_part)
    )
    mlp_grads = dp_sum([grad_w_gate, grad_w_up, grad_w_down])
    grad_w_gate, grad_w_up, grad_w_down = mlp_grads
    (d_normed_two,) = permute_sum([d_normed_two_part], [0], "tensor")
    down_part, d_normed_two = lax.optimization_barrier((down_part, d_normed_two))
    (down_sum,) = permute_sum([down_part], [0], "tensor")
    d_middle_norm, grad_gain_two = norm_two_back(d_normed_two)
    grad_middle = grad_out + d_middle_norm
    d_branch = (keep_rows * grad_middle).astype(jnp.bfloat16)
    grad_w_out = left_trans(attended, d_branch)
    grad_w_gate, grad_w_up, grad_w_down, grad_w_out = lax.optimization_barrier(
        (grad_w_gate, grad_w_up, grad_w_down, grad_w_out)
    )
    d_attended = right_trans(d_branch, w_out).astype(jnp.bfloat16)
    d_queries, d_key_all, d_value_all = attention_backward(
        query_low, all_kv, d_attended, lse, local_groups=local_groups, chunk=half_rows,
        **mask_args,
    )
    d_kv_own = permute_scatter(jnp.concatenate([d_key_all, d_value_all], axis=1), "dp")
    d_kv_own, grad_w_out = lax.optimization_barrier((d_kv_own, grad_w_out))
    d_key_own = d_kv_own[:, :kv_width]
    d_value_own = d_kv_own[:, kv_width:]
    d_queries = d_queries.reshape(row_count, local_heads, HEAD_DIM)
    d_query_low = (
        rotate(d_queries, cos_table, -sin_table)
        .reshape(row_count, local_heads * HEAD_DIM)
        .astype(jnp.bfloat16)
    )
    d_key_low = (
        rotate(d_key_own.reshape(row_count, local_groups, HEAD_DIM), cos_table, -sin_table)
        .reshape(row_count, local_groups * HEAD_DIM)
        .astype(jnp.bfloat16)
    )
    d_value_low = d_value_own.astype(jnp.bfloat16)
    grad_w_query = left_trans(normed, d_query_low)
    grad_w_key = left_trans(normed, d_key_low)
    grad_w_value = left_trans(normed, d_value_low)
    d_normed_part = (
        right_trans(d_query_low, w_query)
        + right_trans(d_key_low, w_key)
        + right_trans(d_value_low, w_value)
    )
    (
        down_sum,
        d_normed_part,
        grad_w_out,
        grad_w_query,
        grad_w_key,
        grad_w_value,
    ) = lax.optimization_barrier(
        (down_sum, d_normed_part, grad_w_out, grad_w_query, grad_w_key, grad_w_value)
    )
    grad_w_out, grad_w_query, grad_w_key, grad_w_value = dp_sum(
        [grad_w_out, grad_w_query, grad_w_key, grad_w_value]
    )
    grad_w_gate, grad_w_up, grad_w_down = [
        grad.astype(jnp.float32) for grad in (grad_w_gate, grad_w_up, grad_w_down)
    ]
    output = (middle + keep_rows * down_sum).astype(jnp.bfloat16)
    (d_normed,) = permute_sum([d_normed_part], [0], "tensor")
    d_source_norm, grad_gain_one = norm_one_back(d_normed)
    grad_input = grad_middle + d_source_norm
    grad_gain_one = permute_allsum(grad_gain_one, "dp")
    grad_gain_two = permute_allsum(grad_gain_two, "dp")
    grad_w_out, grad_w_query, grad_w_key, grad_w_value = [
        grad.astype(jnp.float32) for grad in (grad_w_out, grad_w_query, grad_w_key, grad_w_value)
    ]
    return (
        output,
        grad_input,
        grad_gain_one,
        grad_w_query,
        grad_w_key,
        grad_w_value,
        grad_w_out,
        grad_gain_two,
        grad_w_gate,
        grad_w_up,
        grad_w_down,
    )


def solution(mesh):
    placed = (
        P("dp", None),
        P("dp"),
        P(),
        P(),
        P(None, "tensor"),
        P(None, "tensor"),
        P(None, "tensor"),
        P("tensor", None),
        P(),
        P(None, "tensor"),
        P(None, "tensor"),
        P("tensor", None),
        P("dp", None),
    )
    return jax.shard_map(
        on_device,
        mesh=mesh,
        in_specs=placed,
        out_specs=(
            P("dp", None),
            P("dp", None),
            P(),
            P(None, "tensor"),
            P(None, "tensor"),
            P(None, "tensor"),
            P("tensor", None),
            P(),
            P(None, "tensor"),
            P(None, "tensor"),
            P("tensor", None),
        ),
        check_vma=False,
    )
```

```python
import functools

import jax
import jax.numpy as jnp
from jax import lax
from jax.experimental import pallas as pl
from jax.experimental.pallas import tpu as pltpu
from jax.sharding import PartitionSpec as P


HEAD_DIM = 128


EPS = 1e-05
MASKED_SCORE = -1e30


def rms_norm(values, scales):
    return values * lax.rsqrt(jnp.mean(values * values, axis=-1, keepdims=True) + EPS) * scales


def rotate(values, cos_table, sin_table):
    middle = values.shape[-1] // 2
    leading = values[..., :middle]
    trailing = values[..., middle:]
    return jnp.concatenate(
        [leading * cos_table - trailing * sin_table, trailing * cos_table + leading * sin_table],
        axis=-1,
    )


def angles_of(positions, head_size):
    frequency = 10000.0 ** (-jnp.arange(0, head_size, 2, dtype=jnp.float32) / head_size)
    angles = positions.astype(jnp.float32)[:, None] * frequency[None, :]
    return (jnp.cos(angles)[:, None, :], jnp.sin(angles)[:, None, :])


def swiglu(gate_value, up_value):
    return jax.nn.silu(gate_value) * up_value


def left_trans(left, right):
    return lax.dot_general(
        left, right, (((0,), (0,)), ((), ())), preferred_element_type=jnp.float32
    )


def right_trans(left, right):
    return lax.dot_general(
        left, right, (((1,), (1,)), ((), ())), preferred_element_type=jnp.float32
    )


def _allowed(qpos, own, kpos, kalive, start, width):
    slots = lax.broadcasted_iota(jnp.int32, (1, width), 1) + start
    return (kpos <= qpos) & ((kalive > 0) | (slots == own))


def _attn_bwd_kernel(
    chunk_ref, qblock_ref, q_ref, k_ref, v_ref, do_ref, lse_ref, qpos_ref, own_ref, kpos_ref,
    kalive_ref, dq_ref, dk_ref, dv_ref, delta_ref, dqacc_ref, *, heads, halves, chunk, chunks,
    scale,
):
    rows = q_ref.shape[0] // halves
    dk_ref[...] = jnp.zeros(dk_ref.shape, jnp.float32)
    dv_ref[...] = jnp.zeros(dv_ref.shape, jnp.float32)
    for head in range(heads):
        for half in range(halves):
            row_sl = pl.ds(half * rows, rows)
            col_sl = pl.ds(head * HEAD_DIM, HEAD_DIM)
            q = q_ref[row_sl, col_sl]
            do = do_ref[row_sl, col_sl]
            lse = lse_ref[head, row_sl, :]
            qpos = qpos_ref[row_sl, :]
            own = own_ref[row_sl, :]
            limit = qblock_ref[half]

            def probs_of(c):
                start = pl.multiple_of(c * chunk, chunk)
                k = k_ref[pl.ds(start, chunk), :]
                v = v_ref[pl.ds(start, chunk), :]
                s = lax.dot_general(
                    q, k, (((1,), (1,)), ((), ())), preferred_element_type=jnp.float32
                ) * scale
                ok = _allowed(
                    qpos, own, kpos_ref[:, pl.ds(start, chunk)],
                    kalive_ref[:, pl.ds(start, chunk)], start, chunk,
                )
                p = jnp.where(ok, jnp.exp(jnp.where(ok, s, MASKED_SCORE) - lse), 0.0)
                dp = lax.dot_general(
                    do, v, (((1,), (1,)), ((), ())), preferred_element_type=jnp.float32
                )
                return p, dp, k, start

            delta_ref[...] = jnp.zeros(delta_ref.shape, jnp.float32)

            def deltas(c, carry):
                @pl.when(chunk_ref[c] <= limit)
                def _():
                    p, dp, _, _ = probs_of(c)
                    delta_ref[...] += jnp.sum(p * dp, axis=1, keepdims=True)

                return carry

            lax.fori_loop(0, chunks, deltas, 0)
            delta = delta_ref[...]
            dqacc_ref[...] = jnp.zeros(dqacc_ref.shape, jnp.float32)

            def grads(c, carry):
                @pl.when(chunk_ref[c] <= limit)
                def _():
                    p, dp, k, start = probs_of(c)
                    ds = (p * (dp - delta)).astype(jnp.bfloat16)
                    dqacc_ref[...] += jnp.dot(ds, k, preferred_element_type=jnp.float32)
                    key_sl = pl.ds(start, chunk)
                    dk_ref[key_sl, :] += lax.dot_general(
                        ds, q, (((0,), (0,)), ((), ())), preferred_element_type=jnp.float32
                    ) * scale
                    dv_ref[key_sl, :] += lax.dot_general(
                        p.astype(jnp.bfloat16), do, (((0,), (0,)), ((), ())),
                        preferred_element_type=jnp.float32,
                    )

                return carry

            lax.fori_loop(0, chunks, grads, 0)
            dq_ref[row_sl, col_sl] = dqacc_ref[...] * scale


def _common(query_low, all_kv, local_groups):
    rows = query_low.shape[0]
    length = all_kv.shape[0]
    heads = query_low.shape[1] // HEAD_DIM // local_groups
    return rows, length, heads


def attention_backward(query_low, all_kv, d_attended, lse, chunk_blocks, query_blocks,
                       query_pos, own_ids, key_pos, key_alive, *, local_groups, chunk,
                       first_group=0, groups=None):
    rows, length, heads = _common(query_low, all_kv, local_groups)
    groups = local_groups if groups is None else groups
    at = first_group
    halves = 2
    chunks = length // chunk
    kernel = functools.partial(
        _attn_bwd_kernel, heads=heads, halves=halves, chunk=chunk, chunks=chunks,
        scale=HEAD_DIM ** (-0.5),
    )
    group_cols = heads * HEAD_DIM
    grid_spec = pltpu.PrefetchScalarGridSpec(
        num_scalar_prefetch=2,
        grid=(groups,),
        in_specs=[
            pl.BlockSpec((rows, group_cols), lambda g, *_: (0, at + g)),
            pl.BlockSpec((length, HEAD_DIM), lambda g, *_: (0, at + g)),
            pl.BlockSpec((length, HEAD_DIM), lambda g, *_: (0, local_groups + at + g)),
            pl.BlockSpec((rows, group_cols), lambda g, *_: (0, at + g)),
            pl.BlockSpec((heads, rows, 1), lambda g, *_: (at + g, 0, 0)),
            pl.BlockSpec((rows, 1), lambda g, *_: (0, 0)),
            pl.BlockSpec((rows, 1), lambda g, *_: (0, 0)),
            pl.BlockSpec((1, length), lambda g, *_: (0, 0)),
            pl.BlockSpec((1, length), lambda g, *_: (0, 0)),
        ],
        out_specs=[
            pl.BlockSpec((rows, group_cols), lambda g, *_: (0, g)),
            pl.BlockSpec((length, HEAD_DIM), lambda g, *_: (0, g)),
            pl.BlockSpec((length, HEAD_DIM), lambda g, *_: (0, g)),
        ],
        scratch_shapes=[
            pltpu.VMEM((rows // halves, 1), jnp.float32),
            pltpu.VMEM((rows // halves, HEAD_DIM), jnp.float32),
        ],
    )
    flops = 10 * rows * length * HEAD_DIM * heads * groups
    kv_width = groups * HEAD_DIM
    return pl.pallas_call(
        kernel,
        grid_spec=grid_spec,
        out_shape=[
            jax.ShapeDtypeStruct((rows, heads * groups * HEAD_DIM), jnp.float32),
            jax.ShapeDtypeStruct((length, kv_width), jnp.float32),
            jax.ShapeDtypeStruct((length, kv_width), jnp.float32),
        ],
        compiler_params=pltpu.CompilerParams(vmem_limit_bytes=48 * 1024 * 1024),
        cost_estimate=pl.CostEstimate(
            flops=flops, transcendentals=2 * rows * length * heads * groups,
            bytes_accessed=2 * length * 4 * HEAD_DIM * groups * 3,
        ),
    )(chunk_blocks, query_blocks, query_low, all_kv, all_kv, d_attended, lse, query_pos,
      own_ids, key_pos, key_alive)


def partner_perm(axis_size, mask):
    return [(index, index ^ mask) for index in range(axis_size)]


def permute_sum(parts, dims, axis):
    size = lax.axis_size(axis)
    steps = size.bit_length() - 1
    assert 1 << steps == size
    me = lax.axis_index(axis)
    pieces = list(parts)
    for step in range(steps):
        bit = (me >> step) & 1
        keep, send = [], []
        for piece, dim in zip(pieces, dims):
            half = piece.shape[dim] // 2
            keep.append(lax.dynamic_slice_in_dim(piece, bit * half, half, axis=dim))
            send.append(
                lax.dynamic_slice_in_dim(piece, (1 - bit) * half, half, axis=dim).astype(jnp.bfloat16)
            )
        got = lax.ppermute(send, axis, partner_perm(size, 1 << step))
        pieces = [mine + theirs.astype(jnp.float32) for mine, theirs in zip(keep, got)]
    pieces = [piece.astype(jnp.bfloat16) for piece in pieces]
    for step in reversed(range(steps)):
        first = ((me >> step) & 1) == 0
        got = lax.ppermute(pieces, axis, partner_perm(size, 1 << step))
        pieces = [
            jnp.concatenate(
                [jnp.where(first, mine, theirs), jnp.where(first, theirs, mine)], axis=dim
            )
            for mine, theirs, dim in zip(pieces, got, dims)
        ]
    return [piece.astype(jnp.float32) for piece in pieces]


def permute_scatter(value, axis):
    size = lax.axis_size(axis)
    steps = size.bit_length() - 1
    assert 1 << steps == size
    block = value.shape[0] // size

    def reverse(index):
        return int(format(index, f"0{steps}b")[::-1], 2) if steps else 0

    value = jnp.concatenate(
        [value[reverse(place) * block : (reverse(place) + 1) * block] for place in range(size)], axis=0
    )
    me = lax.axis_index(axis)
    for step in range(steps):
        bit = (me >> step) & 1
        half = value.shape[0] // 2
        keep = lax.dynamic_slice_in_dim(value, bit * half, half, axis=0)
        send = lax.dynamic_slice_in_dim(value, (1 - bit) * half, half, axis=0).astype(jnp.bfloat16)
        got = lax.ppermute(send, axis, partner_perm(size, 1 << step))
        value = keep.astype(jnp.float32) + got.astype(jnp.float32)
    return value


def permute_allsum(value, axis):
    size = lax.axis_size(axis)
    steps = size.bit_length() - 1
    for step in range(steps):
        value = value + lax.ppermute(value, axis, partner_perm(size, 1 << step))
    return value


def on_device(
    inputs,
    active,
    block_table,
    gain_one,
    w_query,
    w_key,
    w_value,
    w_out,
    gain_two,
    w_gate,
    w_up,
    w_down,
    cotangent,
):
    row_count = inputs.shape[0]
    local_heads = w_query.shape[1] // HEAD_DIM
    local_groups = w_key.shape[1] // HEAD_DIM
    group_size = local_heads // local_groups
    half_rows = row_count // 2
    length = row_count * lax.axis_size("dp")
    score_scale = HEAD_DIM ** (-0.5)
    key_pos = (
        block_table[:, None] * half_rows + jnp.arange(half_rows, dtype=jnp.int32)[None, :]
    ).reshape(length)
    row_start = lax.axis_index("dp") * row_count
    query_pos = lax.dynamic_slice_in_dim(key_pos, row_start, row_count)
    slot_ids = jnp.arange(length, dtype=jnp.int32)
    own_ids = row_start + jnp.arange(row_count, dtype=jnp.int32)
    cos_table, sin_table = angles_of(query_pos, HEAD_DIM)
    keep_rows = active.astype(jnp.float32)[:, None]
    source = inputs.astype(jnp.float32)
    normed_full, norm_one_back = jax.vjp(rms_norm, source, gain_one.astype(jnp.float32))
    normed = normed_full.astype(jnp.bfloat16)
    query_raw = jnp.dot(normed, w_query, preferred_element_type=jnp.float32).reshape(
        row_count, local_heads, HEAD_DIM
    )
    key_raw = jnp.dot(normed, w_key, preferred_element_type=jnp.float32).reshape(
        row_count, local_groups, HEAD_DIM
    )
    value_low = jnp.dot(normed, w_value, preferred_element_type=jnp.float32).astype(jnp.bfloat16)
    query_low = (
        rotate(query_raw, cos_table, sin_table)
        .reshape(row_count, local_heads * HEAD_DIM)
        .astype(jnp.bfloat16)
    )
    key_low = (
        rotate(key_raw, cos_table, sin_table)
        .reshape(row_count, local_groups * HEAD_DIM)
        .astype(jnp.bfloat16)
    )
    alive_low = active.astype(jnp.bfloat16)

    kv_width = local_groups * HEAD_DIM
    all_kv = lax.all_gather(
        jnp.concatenate([key_low, value_low], axis=1), "dp", axis=0, tiled=True
    )
    all_alive = lax.all_gather(alive_low, "dp", axis=0, tiled=True)
    mask_args = dict(
        chunk_blocks=block_table,
        query_blocks=lax.dynamic_slice_in_dim(block_table, 2 * lax.axis_index("dp"), 2),
        query_pos=query_pos[:, None],
        own_ids=own_ids[:, None],
        key_pos=key_pos[None, :],
        key_alive=(all_alive > 0).astype(jnp.int32)[None, :],
    )

    def allowed_of(alive_all):
        return (key_pos[None, :] <= query_pos[:, None]) & (
            (alive_all[None, :] > 0) | (slot_ids[None, :] == own_ids[:, None])
        )

    def head_scores(head_index, keys_all, allowed):
        query_part = query_low[:, head_index * HEAD_DIM : (head_index + 1) * HEAD_DIM]
        group_index = head_index // group_size
        key_part = keys_all[:, group_index * HEAD_DIM : (group_index + 1) * HEAD_DIM]
        raw_scores = right_trans(query_part, key_part) * score_scale
        return jnp.where(allowed, raw_scores, MASKED_SCORE)

    all_keys = all_kv[:, :kv_width]
    all_values = all_kv[:, kv_width:]
    allowed_fwd = allowed_of(all_alive)
    mixed_parts = []
    lse_parts = []
    for head_index in range(local_heads):
        masked = head_scores(head_index, all_keys, allowed_fwd)
        row_max = jnp.max(masked, axis=1, keepdims=True)
        shifted = jnp.exp(masked - row_max)
        row_total = jnp.sum(shifted, axis=1, keepdims=True)
        probs_low = (shifted / row_total).astype(jnp.bfloat16)
        lse_parts.append(row_max + jnp.log(row_total))
        group_index = head_index // group_size
        value_part = all_values[:, group_index * HEAD_DIM : (group_index + 1) * HEAD_DIM]
        mixed_parts.append(jnp.dot(probs_low, value_part, preferred_element_type=jnp.float32))
    attended = jnp.concatenate(mixed_parts, axis=1).astype(jnp.bfloat16)
    lse = jnp.stack(lse_parts)
    branch_part = jnp.dot(attended, w_out, preferred_element_type=jnp.float32)
    sc_rows = row_count * 5 // 8
    branch_top = lax.psum(branch_part[:sc_rows].astype(jnp.bfloat16), "tensor")
    (branch_bottom,) = permute_sum([branch_part[sc_rows:]], [0], "tensor")
    branch = jnp.concatenate([branch_top.astype(jnp.float32), branch_bottom], axis=0)
    middle = source + keep_rows * branch
    normed_two_full, norm_two_back = jax.vjp(rms_norm, middle, gain_two.astype(jnp.float32))
    normed_two = normed_two_full.astype(jnp.bfloat16)
    gate_value = jnp.dot(normed_two, w_gate, preferred_element_type=jnp.float32)
    up_value = jnp.dot(normed_two, w_up, preferred_element_type=jnp.float32)
    hidden_full, swiglu_back = jax.vjp(swiglu, gate_value, up_value)
    hidden = hidden_full.astype(jnp.bfloat16)
    down_part = jnp.dot(hidden, w_down, preferred_element_type=jnp.float32)
    grad_out = cotangent.astype(jnp.float32)

    def dp_sum(grads):
        return [lax.psum(grad.astype(jnp.bfloat16), "dp") for grad in grads]

    d_down = (keep_rows * grad_out).astype(jnp.bfloat16)
    grad_w_down = left_trans(hidden, d_down)
    d_hidden = right_trans(d_down, w_down)
    d_gate_full, d_up_full = swiglu_back(d_hidden)
    d_gate = d_gate_full.astype(jnp.bfloat16)
    d_up = d_up_full.astype(jnp.bfloat16)
    grad_w_gate = left_trans(normed_two, d_gate)
    grad_w_up = left_trans(normed_two, d_up)
    d_normed_two_part = right_trans(d_gate, w_gate) + right_trans(d_up, w_up)
    grad_w_gate, grad_w_up, grad_w_down, d_normed_two_part = lax.optimization_barrier(
        (grad_w_gate, grad_w_up, grad_w_down, d_normed_two_part)
    )
    mlp_grads = dp_sum([grad_w_gate, grad_w_up, grad_w_down])
    grad_w_gate, grad_w_up, grad_w_down = mlp_grads
    (d_normed_two,) = permute_sum([d_normed_two_part], [0], "tensor")
    down_part, d_normed_two = lax.optimization_barrier((down_part, d_normed_two))
    (down_sum,) = permute_sum([down_part], [0], "tensor")
    d_middle_norm, grad_gain_two = norm_two_back(d_normed_two)
    grad_middle = grad_out + d_middle_norm
    d_branch = (keep_rows * grad_middle).astype(jnp.bfloat16)
    grad_w_out = left_trans(attended, d_branch)
    grad_w_gate, grad_w_up, grad_w_down, grad_w_out = lax.optimization_barrier(
        (grad_w_gate, grad_w_up, grad_w_down, grad_w_out)
    )
    d_attended = right_trans(d_branch, w_out).astype(jnp.bfloat16)
    group_grads = []
    for group_index in range(local_groups):
        group_grads.append(
            attention_backward(
                query_low, all_kv, d_attended, lse, local_groups=local_groups,
                chunk=half_rows, first_group=group_index, groups=1, **mask_args,
            )
        )
    d_queries, d_key_all, d_value_all = [
        jnp.concatenate(parts, axis=1) for parts in zip(*group_grads)
    ]
    d_kv_own = permute_scatter(jnp.concatenate([d_key_all, d_value_all], axis=1), "dp")
    d_kv_own, grad_w_out = lax.optimization_barrier((d_kv_own, grad_w_out))
    d_key_own = d_kv_own[:, :kv_width]
    d_value_own = d_kv_own[:, kv_width:]
    d_queries = d_queries.reshape(row_count, local_heads, HEAD_DIM)
    d_query_low = (
        rotate(d_queries, cos_table, -sin_table)
        .reshape(row_count, local_heads * HEAD_DIM)
        .astype(jnp.bfloat16)
    )
    d_key_low = (
        rotate(d_key_own.reshape(row_count, local_groups, HEAD_DIM), cos_table, -sin_table)
        .reshape(row_count, local_groups * HEAD_DIM)
        .astype(jnp.bfloat16)
    )
    d_value_low = d_value_own.astype(jnp.bfloat16)
    grad_w_query = left_trans(normed, d_query_low)
    grad_w_key = left_trans(normed, d_key_low)
    grad_w_value = left_trans(normed, d_value_low)
    d_normed_part = (
        right_trans(d_query_low, w_query)
        + right_trans(d_key_low, w_key)
        + right_trans(d_value_low, w_value)
    )
    (
        down_sum,
        d_normed_part,
        grad_w_out,
        grad_w_query,
        grad_w_key,
        grad_w_value,
    ) = lax.optimization_barrier(
        (down_sum, d_normed_part, grad_w_out, grad_w_query, grad_w_key, grad_w_value)
    )
    grad_w_out, grad_w_query, grad_w_key, grad_w_value = dp_sum(
        [grad_w_out, grad_w_query, grad_w_key, grad_w_value]
    )
    grad_w_gate, grad_w_up, grad_w_down = [
        grad.astype(jnp.float32) for grad in (grad_w_gate, grad_w_up, grad_w_down)
    ]
    output = (middle + keep_rows * down_sum).astype(jnp.bfloat16)
    (d_normed,) = permute_sum([d_normed_part], [0], "tensor")
    d_source_norm, grad_gain_one = norm_one_back(d_normed)
    grad_input = grad_middle + d_source_norm
    grad_gain_one = permute_allsum(grad_gain_one, "dp")
    grad_gain_two = permute_allsum(grad_gain_two, "dp")
    grad_w_out, grad_w_query, grad_w_key, grad_w_value = [
        grad.astype(jnp.float32) for grad in (grad_w_out, grad_w_query, grad_w_key, grad_w_value)
    ]
    return (
        output,
        grad_input,
        grad_gain_one,
        grad_w_query,
        grad_w_key,
        grad_w_value,
        grad_w_out,
        grad_gain_two,
        grad_w_gate,
        grad_w_up,
        grad_w_down,
    )


def solution(mesh):
    placed = (
        P("dp", None),
        P("dp"),
        P(),
        P(),
        P(None, "tensor"),
        P(None, "tensor"),
        P(None, "tensor"),
        P("tensor", None),
        P(),
        P(None, "tensor"),
        P(None, "tensor"),
        P("tensor", None),
        P("dp", None),
    )
    return jax.shard_map(
        on_device,
        mesh=mesh,
        in_specs=placed,
        out_specs=(
            P("dp", None),
            P("dp", None),
            P(),
            P(None, "tensor"),
            P(None, "tensor"),
            P(None, "tensor"),
            P("tensor", None),
            P(),
            P(None, "tensor"),
            P(None, "tensor"),
            P("tensor", None),
        ),
        check_vma=False,
    )
```

```python
import functools

import jax
import jax.numpy as jnp
from jax import lax
from jax.experimental import pallas as pl
from jax.experimental.pallas import tpu as pltpu
from jax.sharding import PartitionSpec as P


HEAD_DIM = 128


EPS = 1e-05
MASKED_SCORE = -1e30


def rms_norm(values, scales):
    return values * lax.rsqrt(jnp.mean(values * values, axis=-1, keepdims=True) + EPS) * scales


def rotate(values, cos_table, sin_table):
    middle = values.shape[-1] // 2
    leading = values[..., :middle]
    trailing = values[..., middle:]
    return jnp.concatenate(
        [leading * cos_table - trailing * sin_table, trailing * cos_table + leading * sin_table],
        axis=-1,
    )


def angles_of(positions, head_size):
    frequency = 10000.0 ** (-jnp.arange(0, head_size, 2, dtype=jnp.float32) / head_size)
    angles = positions.astype(jnp.float32)[:, None] * frequency[None, :]
    return (jnp.cos(angles)[:, None, :], jnp.sin(angles)[:, None, :])


def swiglu(gate_value, up_value):
    return jax.nn.silu(gate_value) * up_value


def left_trans(left, right):
    return lax.dot_general(
        left, right, (((0,), (0,)), ((), ())), preferred_element_type=jnp.float32
    )


def right_trans(left, right):
    return lax.dot_general(
        left, right, (((1,), (1,)), ((), ())), preferred_element_type=jnp.float32
    )


def _allowed(qpos, own, kpos, kalive, start, width):
    slots = lax.broadcasted_iota(jnp.int32, (1, width), 1) + start
    return (kpos <= qpos) & ((kalive > 0) | (slots == own))


def _attn_bwd_kernel(
    chunk_ref, qblock_ref, q_ref, k_ref, v_ref, do_ref, lse_ref, qpos_ref, own_ref, kpos_ref,
    kalive_ref, dq_ref, dk_ref, dv_ref, delta_ref, dqacc_ref, *, heads, halves, chunk, chunks,
    scale,
):
    rows = q_ref.shape[0] // halves
    dk_ref[...] = jnp.zeros(dk_ref.shape, jnp.float32)
    dv_ref[...] = jnp.zeros(dv_ref.shape, jnp.float32)
    for head in range(heads):
        for half in range(halves):
            row_sl = pl.ds(half * rows, rows)
            col_sl = pl.ds(head * HEAD_DIM, HEAD_DIM)
            q = q_ref[row_sl, col_sl]
            do = do_ref[row_sl, col_sl]
            lse = lse_ref[head, row_sl, :]
            qpos = qpos_ref[row_sl, :]
            own = own_ref[row_sl, :]
            limit = qblock_ref[half]

            def probs_of(c):
                start = pl.multiple_of(c * chunk, chunk)
                k = k_ref[pl.ds(start, chunk), :]
                v = v_ref[pl.ds(start, chunk), :]
                s = lax.dot_general(
                    q, k, (((1,), (1,)), ((), ())), preferred_element_type=jnp.float32
                ) * scale
                ok = _allowed(
                    qpos, own, kpos_ref[:, pl.ds(start, chunk)],
                    kalive_ref[:, pl.ds(start, chunk)], start, chunk,
                )
                p = jnp.where(ok, jnp.exp(jnp.where(ok, s, MASKED_SCORE) - lse), 0.0)
                dp = lax.dot_general(
                    do, v, (((1,), (1,)), ((), ())), preferred_element_type=jnp.float32
                )
                return p, dp, k, start

            delta_ref[...] = jnp.zeros(delta_ref.shape, jnp.float32)

            def deltas(c, carry):
                @pl.when(chunk_ref[c] <= limit)
                def _():
                    p, dp, _, _ = probs_of(c)
                    delta_ref[...] += jnp.sum(p * dp, axis=1, keepdims=True)

                return carry

            lax.fori_loop(0, chunks, deltas, 0)
            delta = delta_ref[...]
            dqacc_ref[...] = jnp.zeros(dqacc_ref.shape, jnp.float32)

            def grads(c, carry):
                @pl.when(chunk_ref[c] <= limit)
                def _():
                    p, dp, k, start = probs_of(c)
                    ds = (p * (dp - delta)).astype(jnp.bfloat16)
                    dqacc_ref[...] += jnp.dot(ds, k, preferred_element_type=jnp.float32)
                    key_sl = pl.ds(start, chunk)
                    dk_ref[key_sl, :] += lax.dot_general(
                        ds, q, (((0,), (0,)), ((), ())), preferred_element_type=jnp.float32
                    ) * scale
                    dv_ref[key_sl, :] += lax.dot_general(
                        p.astype(jnp.bfloat16), do, (((0,), (0,)), ((), ())),
                        preferred_element_type=jnp.float32,
                    )

                return carry

            lax.fori_loop(0, chunks, grads, 0)
            dq_ref[row_sl, col_sl] = dqacc_ref[...] * scale


def _common(query_low, all_kv, local_groups):
    rows = query_low.shape[0]
    length = all_kv.shape[0]
    heads = query_low.shape[1] // HEAD_DIM // local_groups
    return rows, length, heads


def attention_backward(query_low, all_kv, d_attended, lse, chunk_blocks, query_blocks,
                       query_pos, own_ids, key_pos, key_alive, *, local_groups, chunk):
    rows, length, heads = _common(query_low, all_kv, local_groups)
    halves = 2
    chunks = length // chunk
    kernel = functools.partial(
        _attn_bwd_kernel, heads=heads, halves=halves, chunk=chunk, chunks=chunks,
        scale=HEAD_DIM ** (-0.5),
    )
    group_cols = heads * HEAD_DIM
    grid_spec = pltpu.PrefetchScalarGridSpec(
        num_scalar_prefetch=2,
        grid=(local_groups,),
        in_specs=[
            pl.BlockSpec((rows, group_cols), lambda g, *_: (0, g)),
            pl.BlockSpec((length, HEAD_DIM), lambda g, *_: (0, g)),
            pl.BlockSpec((length, HEAD_DIM), lambda g, *_: (0, local_groups + g)),
            pl.BlockSpec((rows, group_cols), lambda g, *_: (0, g)),
            pl.BlockSpec((heads, rows, 1), lambda g, *_: (g, 0, 0)),
            pl.BlockSpec((rows, 1), lambda g, *_: (0, 0)),
            pl.BlockSpec((rows, 1), lambda g, *_: (0, 0)),
            pl.BlockSpec((1, length), lambda g, *_: (0, 0)),
            pl.BlockSpec((1, length), lambda g, *_: (0, 0)),
        ],
        out_specs=[
            pl.BlockSpec((rows, group_cols), lambda g, *_: (0, g)),
            pl.BlockSpec((length, HEAD_DIM), lambda g, *_: (0, g)),
            pl.BlockSpec((length, HEAD_DIM), lambda g, *_: (0, g)),
        ],
        scratch_shapes=[
            pltpu.VMEM((rows // halves, 1), jnp.float32),
            pltpu.VMEM((rows // halves, HEAD_DIM), jnp.float32),
        ],
    )
    flops = 10 * rows * length * HEAD_DIM * heads * local_groups
    kv_width = local_groups * HEAD_DIM
    return pl.pallas_call(
        kernel,
        grid_spec=grid_spec,
        out_shape=[
            jax.ShapeDtypeStruct((rows, heads * local_groups * HEAD_DIM), jnp.float32),
            jax.ShapeDtypeStruct((length, kv_width), jnp.float32),
            jax.ShapeDtypeStruct((length, kv_width), jnp.float32),
        ],
        compiler_params=pltpu.CompilerParams(vmem_limit_bytes=48 * 1024 * 1024),
        cost_estimate=pl.CostEstimate(
            flops=flops, transcendentals=2 * rows * length * heads * local_groups,
            bytes_accessed=2 * length * 4 * HEAD_DIM * local_groups * 3,
        ),
    )(chunk_blocks, query_blocks, query_low, all_kv, all_kv, d_attended, lse, query_pos,
      own_ids, key_pos, key_alive)


def partner_perm(axis_size, mask):
    return [(index, index ^ mask) for index in range(axis_size)]


def permute_sum(parts, dims, axis):
    size = lax.axis_size(axis)
    steps = size.bit_length() - 1
    assert 1 << steps == size
    me = lax.axis_index(axis)
    pieces = list(parts)
    for step in range(steps):
        bit = (me >> step) & 1
        keep, send = [], []
        for piece, dim in zip(pieces, dims):
            half = piece.shape[dim] // 2
            keep.append(lax.dynamic_slice_in_dim(piece, bit * half, half, axis=dim))
            send.append(
                lax.dynamic_slice_in_dim(piece, (1 - bit) * half, half, axis=dim).astype(jnp.bfloat16)
            )
        got = lax.ppermute(send, axis, partner_perm(size, 1 << step))
        pieces = [mine + theirs.astype(jnp.float32) for mine, theirs in zip(keep, got)]
    pieces = [piece.astype(jnp.bfloat16) for piece in pieces]
    for step in reversed(range(steps)):
        first = ((me >> step) & 1) == 0
        got = lax.ppermute(pieces, axis, partner_perm(size, 1 << step))
        pieces = [
            jnp.concatenate(
                [jnp.where(first, mine, theirs), jnp.where(first, theirs, mine)], axis=dim
            )
            for mine, theirs, dim in zip(pieces, got, dims)
        ]
    return [piece.astype(jnp.float32) for piece in pieces]


def permute_scatter(value, axis):
    size = lax.axis_size(axis)
    steps = size.bit_length() - 1
    assert 1 << steps == size
    block = value.shape[0] // size

    def reverse(index):
        return int(format(index, f"0{steps}b")[::-1], 2) if steps else 0

    value = jnp.concatenate(
        [value[reverse(place) * block : (reverse(place) + 1) * block] for place in range(size)], axis=0
    )
    me = lax.axis_index(axis)
    for step in range(steps):
        bit = (me >> step) & 1
        half = value.shape[0] // 2
        keep = lax.dynamic_slice_in_dim(value, bit * half, half, axis=0)
        send = lax.dynamic_slice_in_dim(value, (1 - bit) * half, half, axis=0).astype(jnp.bfloat16)
        got = lax.ppermute(send, axis, partner_perm(size, 1 << step))
        value = keep.astype(jnp.float32) + got.astype(jnp.float32)
    return value


def permute_allsum(value, axis):
    size = lax.axis_size(axis)
    steps = size.bit_length() - 1
    for step in range(steps):
        value = value + lax.ppermute(value, axis, partner_perm(size, 1 << step))
    return value


def on_device(
    inputs,
    active,
    block_table,
    gain_one,
    w_query,
    w_key,
    w_value,
    w_out,
    gain_two,
    w_gate,
    w_up,
    w_down,
    cotangent,
):
    row_count = inputs.shape[0]
    local_heads = w_query.shape[1] // HEAD_DIM
    local_groups = w_key.shape[1] // HEAD_DIM
    group_size = local_heads // local_groups
    half_rows = row_count // 2
    length = row_count * lax.axis_size("dp")
    score_scale = HEAD_DIM ** (-0.5)
    key_pos = (
        block_table[:, None] * half_rows + jnp.arange(half_rows, dtype=jnp.int32)[None, :]
    ).reshape(length)
    row_start = lax.axis_index("dp") * row_count
    query_pos = lax.dynamic_slice_in_dim(key_pos, row_start, row_count)
    slot_ids = jnp.arange(length, dtype=jnp.int32)
    own_ids = row_start + jnp.arange(row_count, dtype=jnp.int32)
    cos_table, sin_table = angles_of(query_pos, HEAD_DIM)
    keep_rows = active.astype(jnp.float32)[:, None]
    source = inputs.astype(jnp.float32)
    normed_full, norm_one_back = jax.vjp(rms_norm, source, gain_one.astype(jnp.float32))
    normed = normed_full.astype(jnp.bfloat16)
    query_raw = jnp.dot(normed, w_query, preferred_element_type=jnp.float32).reshape(
        row_count, local_heads, HEAD_DIM
    )
    key_raw = jnp.dot(normed, w_key, preferred_element_type=jnp.float32).reshape(
        row_count, local_groups, HEAD_DIM
    )
    value_low = jnp.dot(normed, w_value, preferred_element_type=jnp.float32).astype(jnp.bfloat16)
    query_low = (
        rotate(query_raw, cos_table, sin_table)
        .reshape(row_count, local_heads * HEAD_DIM)
        .astype(jnp.bfloat16)
    )
    key_low = (
        rotate(key_raw, cos_table, sin_table)
        .reshape(row_count, local_groups * HEAD_DIM)
        .astype(jnp.bfloat16)
    )
    alive_low = active.astype(jnp.bfloat16)

    kv_width = local_groups * HEAD_DIM
    all_kv = lax.all_gather(
        jnp.concatenate([key_low, value_low], axis=1), "dp", axis=0, tiled=True
    )
    all_alive = lax.all_gather(alive_low, "dp", axis=0, tiled=True)
    mask_args = dict(
        chunk_blocks=block_table,
        query_blocks=lax.dynamic_slice_in_dim(block_table, 2 * lax.axis_index("dp"), 2),
        query_pos=query_pos[:, None],
        own_ids=own_ids[:, None],
        key_pos=key_pos[None, :],
        key_alive=(all_alive > 0).astype(jnp.int32)[None, :],
    )

    def allowed_of(alive_all):
        return (key_pos[None, :] <= query_pos[:, None]) & (
            (alive_all[None, :] > 0) | (slot_ids[None, :] == own_ids[:, None])
        )

    def head_scores(head_index, keys_all, allowed):
        query_part = query_low[:, head_index * HEAD_DIM : (head_index + 1) * HEAD_DIM]
        group_index = head_index // group_size
        key_part = keys_all[:, group_index * HEAD_DIM : (group_index + 1) * HEAD_DIM]
        raw_scores = right_trans(query_part, key_part) * score_scale
        return jnp.where(allowed, raw_scores, MASKED_SCORE)

    all_keys = all_kv[:, :kv_width]
    all_values = all_kv[:, kv_width:]
    allowed_fwd = allowed_of(all_alive)
    mixed_parts = []
    lse_parts = []
    for head_index in range(local_heads):
        masked = head_scores(head_index, all_keys, allowed_fwd)
        row_max = jnp.max(masked, axis=1, keepdims=True)
        shifted = jnp.exp(masked - row_max)
        row_total = jnp.sum(shifted, axis=1, keepdims=True)
        probs_low = (shifted / row_total).astype(jnp.bfloat16)
        lse_parts.append(row_max + jnp.log(row_total))
        group_index = head_index // group_size
        value_part = all_values[:, group_index * HEAD_DIM : (group_index + 1) * HEAD_DIM]
        mixed_parts.append(jnp.dot(probs_low, value_part, preferred_element_type=jnp.float32))
    attended = jnp.concatenate(mixed_parts, axis=1).astype(jnp.bfloat16)
    lse = jnp.stack(lse_parts)
    branch_part = jnp.dot(attended, w_out, preferred_element_type=jnp.float32)
    sc_rows = row_count * 5 // 8
    branch_top = lax.psum(branch_part[:sc_rows].astype(jnp.bfloat16), "tensor")
    (branch_bottom,) = permute_sum([branch_part[sc_rows:]], [0], "tensor")
    branch = jnp.concatenate([branch_top.astype(jnp.float32), branch_bottom], axis=0)
    middle = source + keep_rows * branch
    normed_two_full, norm_two_back = jax.vjp(rms_norm, middle, gain_two.astype(jnp.float32))
    normed_two = normed_two_full.astype(jnp.bfloat16)
    gate_value = jnp.dot(normed_two, w_gate, preferred_element_type=jnp.float32)
    up_value = jnp.dot(normed_two, w_up, preferred_element_type=jnp.float32)
    hidden_full, swiglu_back = jax.vjp(swiglu, gate_value, up_value)
    hidden = hidden_full.astype(jnp.bfloat16)
    down_part = jnp.dot(hidden, w_down, preferred_element_type=jnp.float32)
    grad_out = cotangent.astype(jnp.float32)

    def dp_sum(grads):
        return [lax.psum(grad.astype(jnp.bfloat16), "dp") for grad in grads]

    d_down = (keep_rows * grad_out).astype(jnp.bfloat16)
    grad_w_down = left_trans(hidden, d_down)
    d_hidden = right_trans(d_down, w_down)
    d_gate_full, d_up_full = swiglu_back(d_hidden)
    d_gate = d_gate_full.astype(jnp.bfloat16)
    d_up = d_up_full.astype(jnp.bfloat16)
    grad_w_gate = left_trans(normed_two, d_gate)
    grad_w_up = left_trans(normed_two, d_up)
    d_normed_two_part = right_trans(d_gate, w_gate) + right_trans(d_up, w_up)
    grad_w_gate, grad_w_up, grad_w_down, d_normed_two_part = lax.optimization_barrier(
        (grad_w_gate, grad_w_up, grad_w_down, d_normed_two_part)
    )
    mlp_grads = dp_sum([grad_w_gate, grad_w_up, grad_w_down])
    grad_w_gate, grad_w_up, grad_w_down = mlp_grads
    (d_normed_two,) = permute_sum([d_normed_two_part], [0], "tensor")
    down_part, d_normed_two = lax.optimization_barrier((down_part, d_normed_two))
    (down_sum,) = permute_sum([down_part], [0], "tensor")
    d_middle_norm, grad_gain_two = norm_two_back(d_normed_two)
    grad_middle = grad_out + d_middle_norm
    d_branch = (keep_rows * grad_middle).astype(jnp.bfloat16)
    grad_w_out = left_trans(attended, d_branch)
    grad_w_gate, grad_w_up, grad_w_down, grad_w_out = lax.optimization_barrier(
        (grad_w_gate, grad_w_up, grad_w_down, grad_w_out)
    )
    d_attended = right_trans(d_branch, w_out).astype(jnp.bfloat16)
    d_queries, d_key_all, d_value_all = attention_backward(
        query_low, all_kv, d_attended, lse, local_groups=local_groups, chunk=half_rows,
        **mask_args,
    )
    d_kv_own = permute_scatter(jnp.concatenate([d_key_all, d_value_all], axis=1), "dp")
    d_kv_own, grad_w_out = lax.optimization_barrier((d_kv_own, grad_w_out))
    d_key_own = d_kv_own[:, :kv_width]
    d_value_own = d_kv_own[:, kv_width:]
    d_queries = d_queries.reshape(row_count, local_heads, HEAD_DIM)
    d_query_low = (
        rotate(d_queries, cos_table, -sin_table)
        .reshape(row_count, local_heads * HEAD_DIM)
        .astype(jnp.bfloat16)
    )
    d_key_low = (
        rotate(d_key_own.reshape(row_count, local_groups, HEAD_DIM), cos_table, -sin_table)
        .reshape(row_count, local_groups * HEAD_DIM)
        .astype(jnp.bfloat16)
    )
    d_value_low = d_value_own.astype(jnp.bfloat16)
    grad_w_query = left_trans(normed, d_query_low)
    grad_w_key = left_trans(normed, d_key_low)
    grad_w_value = left_trans(normed, d_value_low)
    d_normed_part = (
        right_trans(d_query_low, w_query)
        + right_trans(d_key_low, w_key)
        + right_trans(d_value_low, w_value)
    )
    (
        down_sum,
        d_normed_part,
        grad_w_out,
        grad_w_query,
        grad_w_key,
        grad_w_value,
    ) = lax.optimization_barrier(
        (down_sum, d_normed_part, grad_w_out, grad_w_query, grad_w_key, grad_w_value)
    )
    grad_w_out, grad_w_query = dp_sum([grad_w_out, grad_w_query])
    grad_w_key, grad_w_value = permute_sum([grad_w_key, grad_w_value], [0, 0], "dp")
    grad_w_gate, grad_w_up, grad_w_down = [
        grad.astype(jnp.float32) for grad in (grad_w_gate, grad_w_up, grad_w_down)
    ]
    output = (middle + keep_rows * down_sum).astype(jnp.bfloat16)
    (d_normed,) = permute_sum([d_normed_part], [0], "tensor")
    d_source_norm, grad_gain_one = norm_one_back(d_normed)
    grad_input = grad_middle + d_source_norm
    grad_gain_one = permute_allsum(grad_gain_one, "dp")
    grad_gain_two = permute_allsum(grad_gain_two, "dp")
    grad_w_out, grad_w_query = [grad.astype(jnp.float32) for grad in (grad_w_out, grad_w_query)]
    return (
        output,
        grad_input,
        grad_gain_one,
        grad_w_query,
        grad_w_key,
        grad_w_value,
        grad_w_out,
        grad_gain_two,
        grad_w_gate,
        grad_w_up,
        grad_w_down,
    )


def solution(mesh):
    placed = (
        P("dp", None),
        P("dp"),
        P(),
        P(),
        P(None, "tensor"),
        P(None, "tensor"),
        P(None, "tensor"),
        P("tensor", None),
        P(),
        P(None, "tensor"),
        P(None, "tensor"),
        P("tensor", None),
        P("dp", None),
    )
    return jax.shard_map(
        on_device,
        mesh=mesh,
        in_specs=placed,
        out_specs=(
            P("dp", None),
            P("dp", None),
            P(),
            P(None, "tensor"),
            P(None, "tensor"),
            P(None, "tensor"),
            P("tensor", None),
            P(),
            P(None, "tensor"),
            P(None, "tensor"),
            P("tensor", None),
        ),
        check_vma=False,
    )
```

```python
import functools

import jax
import jax.numpy as jnp
from jax import lax
from jax.experimental import pallas as pl
from jax.experimental.pallas import tpu as pltpu
from jax.sharding import PartitionSpec as P


HEAD_DIM = 128


EPS = 1e-05
MASKED_SCORE = -1e30


def rms_norm(values, scales):
    return values * lax.rsqrt(jnp.mean(values * values, axis=-1, keepdims=True) + EPS) * scales


def rotate(values, cos_table, sin_table):
    middle = values.shape[-1] // 2
    leading = values[..., :middle]
    trailing = values[..., middle:]
    return jnp.concatenate(
        [leading * cos_table - trailing * sin_table, trailing * cos_table + leading * sin_table],
        axis=-1,
    )


def angles_of(positions, head_size):
    frequency = 10000.0 ** (-jnp.arange(0, head_size, 2, dtype=jnp.float32) / head_size)
    angles = positions.astype(jnp.float32)[:, None] * frequency[None, :]
    return (jnp.cos(angles)[:, None, :], jnp.sin(angles)[:, None, :])


def swiglu(gate_value, up_value):
    return jax.nn.silu(gate_value) * up_value


def left_trans(left, right):
    return lax.dot_general(
        left, right, (((0,), (0,)), ((), ())), preferred_element_type=jnp.float32
    )


def right_trans(left, right):
    return lax.dot_general(
        left, right, (((1,), (1,)), ((), ())), preferred_element_type=jnp.float32
    )


def _allowed(qpos, own, kpos, kalive, start, width):
    slots = lax.broadcasted_iota(jnp.int32, (1, width), 1) + start
    return (kpos <= qpos) & ((kalive > 0) | (slots == own))


def _attn_bwd_kernel(
    chunk_ref, qblock_ref, q_ref, k_ref, v_ref, do_ref, lse_ref, qpos_ref, own_ref, kpos_ref,
    kalive_ref, dq_ref, dk_ref, dv_ref, delta_ref, dqacc_ref, *, heads, halves, chunk, chunks,
    scale,
):
    rows = q_ref.shape[0] // halves
    dk_ref[...] = jnp.zeros(dk_ref.shape, jnp.float32)
    dv_ref[...] = jnp.zeros(dv_ref.shape, jnp.float32)
    for head in range(heads):
        for half in range(halves):
            row_sl = pl.ds(half * rows, rows)
            col_sl = pl.ds(head * HEAD_DIM, HEAD_DIM)
            q = q_ref[row_sl, col_sl]
            do = do_ref[row_sl, col_sl]
            lse = lse_ref[head, row_sl, :]
            qpos = qpos_ref[row_sl, :]
            own = own_ref[row_sl, :]
            limit = qblock_ref[half]

            def probs_of(c):
                start = pl.multiple_of(c * chunk, chunk)
                k = k_ref[pl.ds(start, chunk), :]
                v = v_ref[pl.ds(start, chunk), :]
                s = lax.dot_general(
                    q, k, (((1,), (1,)), ((), ())), preferred_element_type=jnp.float32
                ) * scale
                ok = _allowed(
                    qpos, own, kpos_ref[:, pl.ds(start, chunk)],
                    kalive_ref[:, pl.ds(start, chunk)], start, chunk,
                )
                p = jnp.where(ok, jnp.exp(jnp.where(ok, s, MASKED_SCORE) - lse), 0.0)
                dp = lax.dot_general(
                    do, v, (((1,), (1,)), ((), ())), preferred_element_type=jnp.float32
                )
                return p, dp, k, start

            delta_ref[...] = jnp.zeros(delta_ref.shape, jnp.float32)

            def deltas(c, carry):
                @pl.when(chunk_ref[c] <= limit)
                def _():
                    p, dp, _, _ = probs_of(c)
                    delta_ref[...] += jnp.sum(p * dp, axis=1, keepdims=True)

                return carry

            lax.fori_loop(0, chunks, deltas, 0)
            delta = delta_ref[...]
            dqacc_ref[...] = jnp.zeros(dqacc_ref.shape, jnp.float32)

            def grads(c, carry):
                @pl.when(chunk_ref[c] <= limit)
                def _():
                    p, dp, k, start = probs_of(c)
                    ds = (p * (dp - delta)).astype(jnp.bfloat16)
                    dqacc_ref[...] += jnp.dot(ds, k, preferred_element_type=jnp.float32)
                    key_sl = pl.ds(start, chunk)
                    dk_ref[key_sl, :] += lax.dot_general(
                        ds, q, (((0,), (0,)), ((), ())), preferred_element_type=jnp.float32
                    ) * scale
                    dv_ref[key_sl, :] += lax.dot_general(
                        p.astype(jnp.bfloat16), do, (((0,), (0,)), ((), ())),
                        preferred_element_type=jnp.float32,
                    )

                return carry

            lax.fori_loop(0, chunks, grads, 0)
            dq_ref[row_sl, col_sl] = dqacc_ref[...] * scale


def _common(query_low, all_kv, local_groups):
    rows = query_low.shape[0]
    length = all_kv.shape[0]
    heads = query_low.shape[1] // HEAD_DIM // local_groups
    return rows, length, heads


def attention_backward(query_low, all_kv, d_attended, lse, chunk_blocks, query_blocks,
                       query_pos, own_ids, key_pos, key_alive, *, local_groups, chunk):
    rows, length, heads = _common(query_low, all_kv, local_groups)
    halves = 2
    chunks = length // chunk
    kernel = functools.partial(
        _attn_bwd_kernel, heads=heads, halves=halves, chunk=chunk, chunks=chunks,
        scale=HEAD_DIM ** (-0.5),
    )
    group_cols = heads * HEAD_DIM
    grid_spec = pltpu.PrefetchScalarGridSpec(
        num_scalar_prefetch=2,
        grid=(local_groups,),
        in_specs=[
            pl.BlockSpec((rows, group_cols), lambda g, *_: (0, g)),
            pl.BlockSpec((length, HEAD_DIM), lambda g, *_: (0, g)),
            pl.BlockSpec((length, HEAD_DIM), lambda g, *_: (0, local_groups + g)),
            pl.BlockSpec((rows, group_cols), lambda g, *_: (0, g)),
            pl.BlockSpec((heads, rows, 1), lambda g, *_: (g, 0, 0)),
            pl.BlockSpec((rows, 1), lambda g, *_: (0, 0)),
            pl.BlockSpec((rows, 1), lambda g, *_: (0, 0)),
            pl.BlockSpec((1, length), lambda g, *_: (0, 0)),
            pl.BlockSpec((1, length), lambda g, *_: (0, 0)),
        ],
        out_specs=[
            pl.BlockSpec((rows, group_cols), lambda g, *_: (0, g)),
            pl.BlockSpec((length, HEAD_DIM), lambda g, *_: (0, g)),
            pl.BlockSpec((length, HEAD_DIM), lambda g, *_: (0, g)),
        ],
        scratch_shapes=[
            pltpu.VMEM((rows // halves, 1), jnp.float32),
            pltpu.VMEM((rows // halves, HEAD_DIM), jnp.float32),
        ],
    )
    flops = 10 * rows * length * HEAD_DIM * heads * local_groups
    kv_width = local_groups * HEAD_DIM
    return pl.pallas_call(
        kernel,
        grid_spec=grid_spec,
        out_shape=[
            jax.ShapeDtypeStruct((rows, heads * local_groups * HEAD_DIM), jnp.float32),
            jax.ShapeDtypeStruct((length, kv_width), jnp.float32),
            jax.ShapeDtypeStruct((length, kv_width), jnp.float32),
        ],
        compiler_params=pltpu.CompilerParams(vmem_limit_bytes=48 * 1024 * 1024),
        cost_estimate=pl.CostEstimate(
            flops=flops, transcendentals=2 * rows * length * heads * local_groups,
            bytes_accessed=2 * length * 4 * HEAD_DIM * local_groups * 3,
        ),
    )(chunk_blocks, query_blocks, query_low, all_kv, all_kv, d_attended, lse, query_pos,
      own_ids, key_pos, key_alive)


def partner_perm(axis_size, mask):
    return [(index, index ^ mask) for index in range(axis_size)]


def permute_sum(parts, dims, axis):
    size = lax.axis_size(axis)
    steps = size.bit_length() - 1
    assert 1 << steps == size
    me = lax.axis_index(axis)
    pieces = list(parts)
    for step in range(steps):
        bit = (me >> step) & 1
        keep, send = [], []
        for piece, dim in zip(pieces, dims):
            half = piece.shape[dim] // 2
            keep.append(lax.dynamic_slice_in_dim(piece, bit * half, half, axis=dim))
            send.append(
                lax.dynamic_slice_in_dim(piece, (1 - bit) * half, half, axis=dim).astype(jnp.bfloat16)
            )
        got = lax.ppermute(send, axis, partner_perm(size, 1 << step))
        pieces = [mine + theirs.astype(jnp.float32) for mine, theirs in zip(keep, got)]
    pieces = [piece.astype(jnp.bfloat16) for piece in pieces]
    for step in reversed(range(steps)):
        first = ((me >> step) & 1) == 0
        got = lax.ppermute(pieces, axis, partner_perm(size, 1 << step))
        pieces = [
            jnp.concatenate(
                [jnp.where(first, mine, theirs), jnp.where(first, theirs, mine)], axis=dim
            )
            for mine, theirs, dim in zip(pieces, got, dims)
        ]
    return [piece.astype(jnp.float32) for piece in pieces]


def permute_allsum(value, axis):
    size = lax.axis_size(axis)
    steps = size.bit_length() - 1
    for step in range(steps):
        value = value + lax.ppermute(value, axis, partner_perm(size, 1 << step))
    return value


def on_device(
    inputs,
    active,
    block_table,
    gain_one,
    w_query,
    w_key,
    w_value,
    w_out,
    gain_two,
    w_gate,
    w_up,
    w_down,
    cotangent,
):
    row_count = inputs.shape[0]
    local_heads = w_query.shape[1] // HEAD_DIM
    local_groups = w_key.shape[1] // HEAD_DIM
    group_size = local_heads // local_groups
    half_rows = row_count // 2
    length = row_count * lax.axis_size("dp")
    score_scale = HEAD_DIM ** (-0.5)
    key_pos = (
        block_table[:, None] * half_rows + jnp.arange(half_rows, dtype=jnp.int32)[None, :]
    ).reshape(length)
    row_start = lax.axis_index("dp") * row_count
    query_pos = lax.dynamic_slice_in_dim(key_pos, row_start, row_count)
    slot_ids = jnp.arange(length, dtype=jnp.int32)
    own_ids = row_start + jnp.arange(row_count, dtype=jnp.int32)
    cos_table, sin_table = angles_of(query_pos, HEAD_DIM)
    keep_rows = active.astype(jnp.float32)[:, None]
    source = inputs.astype(jnp.float32)
    normed_full, norm_one_back = jax.vjp(rms_norm, source, gain_one.astype(jnp.float32))
    normed = normed_full.astype(jnp.bfloat16)
    query_raw = jnp.dot(normed, w_query, preferred_element_type=jnp.float32).reshape(
        row_count, local_heads, HEAD_DIM
    )
    key_raw = jnp.dot(normed, w_key, preferred_element_type=jnp.float32).reshape(
        row_count, local_groups, HEAD_DIM
    )
    value_low = jnp.dot(normed, w_value, preferred_element_type=jnp.float32).astype(jnp.bfloat16)
    query_low = (
        rotate(query_raw, cos_table, sin_table)
        .reshape(row_count, local_heads * HEAD_DIM)
        .astype(jnp.bfloat16)
    )
    key_low = (
        rotate(key_raw, cos_table, sin_table)
        .reshape(row_count, local_groups * HEAD_DIM)
        .astype(jnp.bfloat16)
    )
    alive_low = active.astype(jnp.bfloat16)

    kv_width = local_groups * HEAD_DIM
    all_kv = lax.all_gather(
        jnp.concatenate([key_low, value_low], axis=1), "dp", axis=0, tiled=True
    )
    all_alive = lax.all_gather(alive_low, "dp", axis=0, tiled=True)
    mask_args = dict(
        chunk_blocks=block_table,
        query_blocks=lax.dynamic_slice_in_dim(block_table, 2 * lax.axis_index("dp"), 2),
        query_pos=query_pos[:, None],
        own_ids=own_ids[:, None],
        key_pos=key_pos[None, :],
        key_alive=(all_alive > 0).astype(jnp.int32)[None, :],
    )

    def allowed_of(alive_all):
        return (key_pos[None, :] <= query_pos[:, None]) & (
            (alive_all[None, :] > 0) | (slot_ids[None, :] == own_ids[:, None])
        )

    def head_scores(head_index, keys_all, allowed):
        query_part = query_low[:, head_index * HEAD_DIM : (head_index + 1) * HEAD_DIM]
        group_index = head_index // group_size
        key_part = keys_all[:, group_index * HEAD_DIM : (group_index + 1) * HEAD_DIM]
        raw_scores = right_trans(query_part, key_part) * score_scale
        return jnp.where(allowed, raw_scores, MASKED_SCORE)

    all_keys = all_kv[:, :kv_width]
    all_values = all_kv[:, kv_width:]
    allowed_fwd = allowed_of(all_alive)
    mixed_parts = []
    lse_parts = []
    for head_index in range(local_heads):
        masked = head_scores(head_index, all_keys, allowed_fwd)
        row_max = jnp.max(masked, axis=1, keepdims=True)
        shifted = jnp.exp(masked - row_max)
        row_total = jnp.sum(shifted, axis=1, keepdims=True)
        probs_low = (shifted / row_total).astype(jnp.bfloat16)
        lse_parts.append(row_max + jnp.log(row_total))
        group_index = head_index // group_size
        value_part = all_values[:, group_index * HEAD_DIM : (group_index + 1) * HEAD_DIM]
        mixed_parts.append(jnp.dot(probs_low, value_part, preferred_element_type=jnp.float32))
    attended = jnp.concatenate(mixed_parts, axis=1).astype(jnp.bfloat16)
    lse = jnp.stack(lse_parts)
    branch_part = jnp.dot(attended, w_out, preferred_element_type=jnp.float32)
    sc_rows = row_count * 5 // 8
    branch_top = lax.psum(branch_part[:sc_rows].astype(jnp.bfloat16), "tensor")
    (branch_bottom,) = permute_sum([branch_part[sc_rows:]], [0], "tensor")
    branch = jnp.concatenate([branch_top.astype(jnp.float32), branch_bottom], axis=0)
    middle = source + keep_rows * branch
    normed_two_full, norm_two_back = jax.vjp(rms_norm, middle, gain_two.astype(jnp.float32))
    normed_two = normed_two_full.astype(jnp.bfloat16)
    gate_value = jnp.dot(normed_two, w_gate, preferred_element_type=jnp.float32)
    up_value = jnp.dot(normed_two, w_up, preferred_element_type=jnp.float32)
    hidden_full, swiglu_back = jax.vjp(swiglu, gate_value, up_value)
    hidden = hidden_full.astype(jnp.bfloat16)
    down_part = jnp.dot(hidden, w_down, preferred_element_type=jnp.float32)
    grad_out = cotangent.astype(jnp.float32)

    def dp_sum(grads):
        return [lax.psum(grad.astype(jnp.bfloat16), "dp") for grad in grads]

    d_down = (keep_rows * grad_out).astype(jnp.bfloat16)
    grad_w_down = left_trans(hidden, d_down)
    d_hidden = right_trans(d_down, w_down)
    d_gate_full, d_up_full = swiglu_back(d_hidden)
    d_gate = d_gate_full.astype(jnp.bfloat16)
    d_up = d_up_full.astype(jnp.bfloat16)
    grad_w_gate = left_trans(normed_two, d_gate)
    grad_w_up = left_trans(normed_two, d_up)
    d_normed_two_part = right_trans(d_gate, w_gate) + right_trans(d_up, w_up)
    grad_w_gate, grad_w_up, grad_w_down, d_normed_two_part = lax.optimization_barrier(
        (grad_w_gate, grad_w_up, grad_w_down, d_normed_two_part)
    )
    mlp_grads = dp_sum([grad_w_gate, grad_w_up, grad_w_down])
    grad_w_gate, grad_w_up, grad_w_down = mlp_grads
    (d_normed_two,) = permute_sum([d_normed_two_part], [0], "tensor")
    down_part, d_normed_two = lax.optimization_barrier((down_part, d_normed_two))
    (down_sum,) = permute_sum([down_part], [0], "tensor")
    d_middle_norm, grad_gain_two = norm_two_back(d_normed_two)
    grad_middle = grad_out + d_middle_norm
    d_branch = (keep_rows * grad_middle).astype(jnp.bfloat16)
    grad_w_out = left_trans(attended, d_branch)
    grad_w_gate, grad_w_up, grad_w_down, grad_w_out = lax.optimization_barrier(
        (grad_w_gate, grad_w_up, grad_w_down, grad_w_out)
    )
    d_attended = right_trans(d_branch, w_out).astype(jnp.bfloat16)
    d_queries, d_key_all, d_value_all = attention_backward(
        query_low, all_kv, d_attended, lse, local_groups=local_groups, chunk=half_rows,
        **mask_args,
    )
    d_kv_cat = jnp.concatenate([d_key_all, d_value_all], axis=1).astype(jnp.bfloat16)
    d_kv_own = lax.psum_scatter(
        d_kv_cat,
        "dp",
        scatter_dimension=0,
        tiled=True,
    ).astype(jnp.float32)
    d_kv_own, grad_w_out = lax.optimization_barrier((d_kv_own, grad_w_out))
    d_key_own = d_kv_own[:, :kv_width]
    d_value_own = d_kv_own[:, kv_width:]
    d_queries = d_queries.reshape(row_count, local_heads, HEAD_DIM)
    d_query_low = (
        rotate(d_queries, cos_table, -sin_table)
        .reshape(row_count, local_heads * HEAD_DIM)
        .astype(jnp.bfloat16)
    )
    d_key_low = (
        rotate(d_key_own.reshape(row_count, local_groups, HEAD_DIM), cos_table, -sin_table)
        .reshape(row_count, local_groups * HEAD_DIM)
        .astype(jnp.bfloat16)
    )
    d_value_low = d_value_own.astype(jnp.bfloat16)
    grad_w_query = left_trans(normed, d_query_low)
    grad_w_key = left_trans(normed, d_key_low)
    grad_w_value = left_trans(normed, d_value_low)
    d_normed_part = (
        right_trans(d_query_low, w_query)
        + right_trans(d_key_low, w_key)
        + right_trans(d_value_low, w_value)
    )
    unit_normed = source * lax.rsqrt(jnp.mean(source * source, axis=-1, keepdims=True) + EPS)
    grad_gain_one = jnp.sum(d_normed_part * unit_normed, axis=0)
    (
        down_sum,
        d_normed_part,
        grad_gain_one,
        grad_w_out,
        grad_w_query,
        grad_w_key,
        grad_w_value,
    ) = lax.optimization_barrier(
        (down_sum, d_normed_part, grad_gain_one, grad_w_out, grad_w_query, grad_w_key, grad_w_value)
    )
    grad_w_out, grad_w_query, grad_w_key, grad_w_value = dp_sum(
        [grad_w_out, grad_w_query, grad_w_key, grad_w_value]
    )
    grad_w_gate, grad_w_up, grad_w_down = [
        grad.astype(jnp.float32) for grad in (grad_w_gate, grad_w_up, grad_w_down)
    ]
    output = (middle + keep_rows * down_sum).astype(jnp.bfloat16)
    grad_gain_one = permute_allsum(permute_allsum(grad_gain_one, "dp"), "tensor")
    (d_normed,) = permute_sum([d_normed_part], [0], "tensor")
    d_source_norm, _ = norm_one_back(d_normed)
    grad_input = grad_middle + d_source_norm
    grad_gain_two = permute_allsum(grad_gain_two, "dp")
    grad_w_out, grad_w_query, grad_w_key, grad_w_value = [
        grad.astype(jnp.float32) for grad in (grad_w_out, grad_w_query, grad_w_key, grad_w_value)
    ]
    return (
        output,
        grad_input,
        grad_gain_one,
        grad_w_query,
        grad_w_key,
        grad_w_value,
        grad_w_out,
        grad_gain_two,
        grad_w_gate,
        grad_w_up,
        grad_w_down,
    )


def solution(mesh):
    placed = (
        P("dp", None),
        P("dp"),
        P(),
        P(),
        P(None, "tensor"),
        P(None, "tensor"),
        P(None, "tensor"),
        P("tensor", None),
        P(),
        P(None, "tensor"),
        P(None, "tensor"),
        P("tensor", None),
        P("dp", None),
    )
    return jax.shard_map(
        on_device,
        mesh=mesh,
        in_specs=placed,
        out_specs=(
            P("dp", None),
            P("dp", None),
            P(),
            P(None, "tensor"),
            P(None, "tensor"),
            P(None, "tensor"),
            P("tensor", None),
            P(),
            P(None, "tensor"),
            P(None, "tensor"),
            P("tensor", None),
        ),
        check_vma=False,
    )
```

```python
import functools

import jax
import jax.numpy as jnp
from jax import lax
from jax.experimental import pallas as pl
from jax.experimental.pallas import tpu as pltpu
from jax.sharding import PartitionSpec as P


HEAD_DIM = 128


EPS = 1e-05
MASKED_SCORE = -1e30


def rms_norm(values, scales):
    return values * lax.rsqrt(jnp.mean(values * values, axis=-1, keepdims=True) + EPS) * scales


def rotate(values, cos_table, sin_table):
    middle = values.shape[-1] // 2
    leading = values[..., :middle]
    trailing = values[..., middle:]
    return jnp.concatenate(
        [leading * cos_table - trailing * sin_table, trailing * cos_table + leading * sin_table],
        axis=-1,
    )


def angles_of(positions, head_size):
    frequency = 10000.0 ** (-jnp.arange(0, head_size, 2, dtype=jnp.float32) / head_size)
    angles = positions.astype(jnp.float32)[:, None] * frequency[None, :]
    return (jnp.cos(angles)[:, None, :], jnp.sin(angles)[:, None, :])


def swiglu(gate_value, up_value):
    return jax.nn.silu(gate_value) * up_value


def left_trans(left, right):
    return lax.dot_general(
        left, right, (((0,), (0,)), ((), ())), preferred_element_type=jnp.float32
    )


def right_trans(left, right):
    return lax.dot_general(
        left, right, (((1,), (1,)), ((), ())), preferred_element_type=jnp.float32
    )


def _allowed(qpos, own, kpos, kalive, start, width):
    slots = lax.broadcasted_iota(jnp.int32, (1, width), 1) + start
    return (kpos <= qpos) & ((kalive > 0) | (slots == own))


def _attn_bwd_kernel(
    chunk_ref, qblock_ref, q_ref, k_ref, v_ref, do_ref, lse_ref, qpos_ref, own_ref, kpos_ref,
    kalive_ref, dq_ref, dk_ref, dv_ref, delta_ref, dqacc_ref, *, heads, halves, chunk, chunks,
    scale,
):
    rows = q_ref.shape[0] // halves
    dk_ref[...] = jnp.zeros(dk_ref.shape, jnp.float32)
    dv_ref[...] = jnp.zeros(dv_ref.shape, jnp.float32)
    for head in range(heads):
        for half in range(halves):
            row_sl = pl.ds(half * rows, rows)
            col_sl = pl.ds(head * HEAD_DIM, HEAD_DIM)
            q = q_ref[row_sl, col_sl]
            do = do_ref[row_sl, col_sl]
            lse = lse_ref[head, row_sl, :]
            qpos = qpos_ref[row_sl, :]
            own = own_ref[row_sl, :]
            limit = qblock_ref[half]

            def probs_of(c):
                start = pl.multiple_of(c * chunk, chunk)
                k = k_ref[pl.ds(start, chunk), :]
                v = v_ref[pl.ds(start, chunk), :]
                s = lax.dot_general(
                    q, k, (((1,), (1,)), ((), ())), preferred_element_type=jnp.float32
                ) * scale
                ok = _allowed(
                    qpos, own, kpos_ref[:, pl.ds(start, chunk)],
                    kalive_ref[:, pl.ds(start, chunk)], start, chunk,
                )
                p = jnp.where(ok, jnp.exp(jnp.where(ok, s, MASKED_SCORE) - lse), 0.0)
                dp = lax.dot_general(
                    do, v, (((1,), (1,)), ((), ())), preferred_element_type=jnp.float32
                )
                return p, dp, k, start

            delta_ref[...] = jnp.zeros(delta_ref.shape, jnp.float32)

            def deltas(c, carry):
                @pl.when(chunk_ref[c] <= limit)
                def _():
                    p, dp, _, _ = probs_of(c)
                    delta_ref[...] += jnp.sum(p * dp, axis=1, keepdims=True)

                return carry

            lax.fori_loop(0, chunks, deltas, 0)
            delta = delta_ref[...]
            dqacc_ref[...] = jnp.zeros(dqacc_ref.shape, jnp.float32)

            def grads(c, carry):
                @pl.when(chunk_ref[c] <= limit)
                def _():
                    p, dp, k, start = probs_of(c)
                    ds = (p * (dp - delta)).astype(jnp.bfloat16)
                    dqacc_ref[...] += jnp.dot(ds, k, preferred_element_type=jnp.float32)
                    key_sl = pl.ds(start, chunk)
                    dk_ref[key_sl, :] += lax.dot_general(
                        ds, q, (((0,), (0,)), ((), ())), preferred_element_type=jnp.float32
                    ) * scale
                    dv_ref[key_sl, :] += lax.dot_general(
                        p.astype(jnp.bfloat16), do, (((0,), (0,)), ((), ())),
                        preferred_element_type=jnp.float32,
                    )

                return carry

            lax.fori_loop(0, chunks, grads, 0)
            dq_ref[row_sl, col_sl] = dqacc_ref[...] * scale


def _common(query_low, all_kv, local_groups):
    rows = query_low.shape[0]
    length = all_kv.shape[0]
    heads = query_low.shape[1] // HEAD_DIM // local_groups
    return rows, length, heads


def attention_backward(query_low, all_kv, d_attended, lse, chunk_blocks, query_blocks,
                       query_pos, own_ids, key_pos, key_alive, *, local_groups, chunk):
    rows, length, heads = _common(query_low, all_kv, local_groups)
    halves = 2
    chunks = length // chunk
    kernel = functools.partial(
        _attn_bwd_kernel, heads=heads, halves=halves, chunk=chunk, chunks=chunks,
        scale=HEAD_DIM ** (-0.5),
    )
    group_cols = heads * HEAD_DIM
    grid_spec = pltpu.PrefetchScalarGridSpec(
        num_scalar_prefetch=2,
        grid=(local_groups,),
        in_specs=[
            pl.BlockSpec((rows, group_cols), lambda g, *_: (0, g)),
            pl.BlockSpec((length, HEAD_DIM), lambda g, *_: (0, g)),
            pl.BlockSpec((length, HEAD_DIM), lambda g, *_: (0, local_groups + g)),
            pl.BlockSpec((rows, group_cols), lambda g, *_: (0, g)),
            pl.BlockSpec((heads, rows, 1), lambda g, *_: (g, 0, 0)),
            pl.BlockSpec((rows, 1), lambda g, *_: (0, 0)),
            pl.BlockSpec((rows, 1), lambda g, *_: (0, 0)),
            pl.BlockSpec((1, length), lambda g, *_: (0, 0)),
            pl.BlockSpec((1, length), lambda g, *_: (0, 0)),
        ],
        out_specs=[
            pl.BlockSpec((rows, group_cols), lambda g, *_: (0, g)),
            pl.BlockSpec((length, HEAD_DIM), lambda g, *_: (0, g)),
            pl.BlockSpec((length, HEAD_DIM), lambda g, *_: (0, g)),
        ],
        scratch_shapes=[
            pltpu.VMEM((rows // halves, 1), jnp.float32),
            pltpu.VMEM((rows // halves, HEAD_DIM), jnp.float32),
        ],
    )
    flops = 10 * rows * length * HEAD_DIM * heads * local_groups
    kv_width = local_groups * HEAD_DIM
    return pl.pallas_call(
        kernel,
        grid_spec=grid_spec,
        out_shape=[
            jax.ShapeDtypeStruct((rows, heads * local_groups * HEAD_DIM), jnp.float32),
            jax.ShapeDtypeStruct((length, kv_width), jnp.float32),
            jax.ShapeDtypeStruct((length, kv_width), jnp.float32),
        ],
        compiler_params=pltpu.CompilerParams(vmem_limit_bytes=48 * 1024 * 1024),
        cost_estimate=pl.CostEstimate(
            flops=flops, transcendentals=2 * rows * length * heads * local_groups,
            bytes_accessed=2 * length * 4 * HEAD_DIM * local_groups * 3,
        ),
    )(chunk_blocks, query_blocks, query_low, all_kv, all_kv, d_attended, lse, query_pos,
      own_ids, key_pos, key_alive)


def partner_perm(axis_size, mask):
    return [(index, index ^ mask) for index in range(axis_size)]


def permute_sum(parts, dims, axis):
    size = lax.axis_size(axis)
    steps = size.bit_length() - 1
    assert 1 << steps == size
    me = lax.axis_index(axis)
    pieces = list(parts)
    for step in range(steps):
        bit = (me >> step) & 1
        keep, send = [], []
        for piece, dim in zip(pieces, dims):
            half = piece.shape[dim] // 2
            keep.append(lax.dynamic_slice_in_dim(piece, bit * half, half, axis=dim))
            send.append(
                lax.dynamic_slice_in_dim(piece, (1 - bit) * half, half, axis=dim).astype(jnp.bfloat16)
            )
        got = lax.ppermute(send, axis, partner_perm(size, 1 << step))
        pieces = [mine + theirs.astype(jnp.float32) for mine, theirs in zip(keep, got)]
    pieces = [piece.astype(jnp.bfloat16) for piece in pieces]
    for step in reversed(range(steps)):
        first = ((me >> step) & 1) == 0
        got = lax.ppermute(pieces, axis, partner_perm(size, 1 << step))
        pieces = [
            jnp.concatenate(
                [jnp.where(first, mine, theirs), jnp.where(first, theirs, mine)], axis=dim
            )
            for mine, theirs, dim in zip(pieces, got, dims)
        ]
    return [piece.astype(jnp.float32) for piece in pieces]


def permute_scatter(value, axis):
    size = lax.axis_size(axis)
    steps = size.bit_length() - 1
    assert 1 << steps == size
    block = value.shape[0] // size

    def reverse(index):
        return int(format(index, f"0{steps}b")[::-1], 2) if steps else 0

    value = jnp.concatenate(
        [value[reverse(place) * block : (reverse(place) + 1) * block] for place in range(size)], axis=0
    )
    me = lax.axis_index(axis)
    for step in range(steps):
        bit = (me >> step) & 1
        half = value.shape[0] // 2
        keep = lax.dynamic_slice_in_dim(value, bit * half, half, axis=0)
        send = lax.dynamic_slice_in_dim(value, (1 - bit) * half, half, axis=0).astype(jnp.bfloat16)
        got = lax.ppermute(send, axis, partner_perm(size, 1 << step))
        value = keep.astype(jnp.float32) + got.astype(jnp.float32)
    return value


def permute_allsum(value, axis):
    size = lax.axis_size(axis)
    steps = size.bit_length() - 1
    for step in range(steps):
        value = value + lax.ppermute(value, axis, partner_perm(size, 1 << step))
    return value


def on_device(
    inputs,
    active,
    block_table,
    gain_one,
    w_query,
    w_key,
    w_value,
    w_out,
    gain_two,
    w_gate,
    w_up,
    w_down,
    cotangent,
):
    row_count = inputs.shape[0]
    local_heads = w_query.shape[1] // HEAD_DIM
    local_groups = w_key.shape[1] // HEAD_DIM
    group_size = local_heads // local_groups
    half_rows = row_count // 2
    length = row_count * lax.axis_size("dp")
    score_scale = HEAD_DIM ** (-0.5)
    key_pos = (
        block_table[:, None] * half_rows + jnp.arange(half_rows, dtype=jnp.int32)[None, :]
    ).reshape(length)
    row_start = lax.axis_index("dp") * row_count
    query_pos = lax.dynamic_slice_in_dim(key_pos, row_start, row_count)
    slot_ids = jnp.arange(length, dtype=jnp.int32)
    own_ids = row_start + jnp.arange(row_count, dtype=jnp.int32)
    cos_table, sin_table = angles_of(query_pos, HEAD_DIM)
    keep_rows = active.astype(jnp.float32)[:, None]
    source = inputs.astype(jnp.float32)
    normed_full, norm_one_back = jax.vjp(rms_norm, source, gain_one.astype(jnp.float32))
    normed = normed_full.astype(jnp.bfloat16)
    query_raw = jnp.dot(normed, w_query, preferred_element_type=jnp.float32).reshape(
        row_count, local_heads, HEAD_DIM
    )
    key_raw = jnp.dot(normed, w_key, preferred_element_type=jnp.float32).reshape(
        row_count, local_groups, HEAD_DIM
    )
    value_low = jnp.dot(normed, w_value, preferred_element_type=jnp.float32).astype(jnp.bfloat16)
    query_low = (
        rotate(query_raw, cos_table, sin_table)
        .reshape(row_count, local_heads * HEAD_DIM)
        .astype(jnp.bfloat16)
    )
    key_low = (
        rotate(key_raw, cos_table, sin_table)
        .reshape(row_count, local_groups * HEAD_DIM)
        .astype(jnp.bfloat16)
    )
    alive_low = active.astype(jnp.bfloat16)

    kv_width = local_groups * HEAD_DIM
    all_kv = lax.all_gather(
        jnp.concatenate([key_low, value_low], axis=1), "dp", axis=0, tiled=True
    )
    all_alive = lax.all_gather(alive_low, "dp", axis=0, tiled=True)
    mask_args = dict(
        chunk_blocks=block_table,
        query_blocks=lax.dynamic_slice_in_dim(block_table, 2 * lax.axis_index("dp"), 2),
        query_pos=query_pos[:, None],
        own_ids=own_ids[:, None],
        key_pos=key_pos[None, :],
        key_alive=(all_alive > 0).astype(jnp.int32)[None, :],
    )

    def allowed_of(alive_all):
        return (key_pos[None, :] <= query_pos[:, None]) & (
            (alive_all[None, :] > 0) | (slot_ids[None, :] == own_ids[:, None])
        )

    def head_scores(head_index, keys_all, allowed):
        query_part = query_low[:, head_index * HEAD_DIM : (head_index + 1) * HEAD_DIM]
        group_index = head_index // group_size
        key_part = keys_all[:, group_index * HEAD_DIM : (group_index + 1) * HEAD_DIM]
        raw_scores = right_trans(query_part, key_part) * score_scale
        return jnp.where(allowed, raw_scores, MASKED_SCORE)

    all_keys = all_kv[:, :kv_width]
    all_values = all_kv[:, kv_width:]
    allowed_fwd = allowed_of(all_alive)
    mixed_parts = []
    lse_parts = []
    for head_index in range(local_heads):
        masked = head_scores(head_index, all_keys, allowed_fwd)
        row_max = jnp.max(masked, axis=1, keepdims=True)
        shifted = jnp.exp(masked - row_max)
        row_total = jnp.sum(shifted, axis=1, keepdims=True)
        probs_low = (shifted / row_total).astype(jnp.bfloat16)
        lse_parts.append(row_max + jnp.log(row_total))
        group_index = head_index // group_size
        value_part = all_values[:, group_index * HEAD_DIM : (group_index + 1) * HEAD_DIM]
        mixed_parts.append(jnp.dot(probs_low, value_part, preferred_element_type=jnp.float32))
    attended = jnp.concatenate(mixed_parts, axis=1).astype(jnp.bfloat16)
    lse = jnp.stack(lse_parts)
    branch_part = jnp.dot(attended, w_out, preferred_element_type=jnp.float32)
    sc_rows = row_count * 5 // 8
    branch_top = lax.psum(branch_part[:sc_rows].astype(jnp.bfloat16), "tensor")
    (branch_bottom,) = permute_sum([branch_part[sc_rows:]], [0], "tensor")
    branch = jnp.concatenate([branch_top.astype(jnp.float32), branch_bottom], axis=0)
    middle = source + keep_rows * branch
    normed_two_full, norm_two_back = jax.vjp(rms_norm, middle, gain_two.astype(jnp.float32))
    normed_two = normed_two_full.astype(jnp.bfloat16)
    gate_value = jnp.dot(normed_two, w_gate, preferred_element_type=jnp.float32)
    up_value = jnp.dot(normed_two, w_up, preferred_element_type=jnp.float32)
    hidden_full, swiglu_back = jax.vjp(swiglu, gate_value, up_value)
    hidden = hidden_full.astype(jnp.bfloat16)
    down_part = jnp.dot(hidden, w_down, preferred_element_type=jnp.float32)
    grad_out = cotangent.astype(jnp.float32)

    def dp_sum(grads):
        return [lax.psum(grad.astype(jnp.bfloat16), "dp") for grad in grads]

    d_down = (keep_rows * grad_out).astype(jnp.bfloat16)
    grad_w_down = left_trans(hidden, d_down)
    d_hidden = right_trans(d_down, w_down)
    d_gate_full, d_up_full = swiglu_back(d_hidden)
    d_gate = d_gate_full.astype(jnp.bfloat16)
    d_up = d_up_full.astype(jnp.bfloat16)
    grad_w_gate = left_trans(normed_two, d_gate)
    grad_w_up = left_trans(normed_two, d_up)
    d_normed_two_part = right_trans(d_gate, w_gate) + right_trans(d_up, w_up)
    grad_w_gate, grad_w_up, grad_w_down, d_normed_two_part = lax.optimization_barrier(
        (grad_w_gate, grad_w_up, grad_w_down, d_normed_two_part)
    )
    mlp_grads = dp_sum([grad_w_gate, grad_w_up, grad_w_down])
    grad_w_gate, grad_w_up, grad_w_down = mlp_grads
    (d_normed_two,) = permute_sum([d_normed_two_part], [0], "tensor")
    down_part, d_normed_two = lax.optimization_barrier((down_part, d_normed_two))
    (down_sum,) = permute_sum([down_part], [0], "tensor")
    d_middle_norm, grad_gain_two = norm_two_back(d_normed_two)
    grad_middle = grad_out + d_middle_norm
    d_branch = (keep_rows * grad_middle).astype(jnp.bfloat16)
    grad_w_out = left_trans(attended, d_branch)
    d_attended = right_trans(d_branch, w_out).astype(jnp.bfloat16)
    d_queries, d_key_all, d_value_all = attention_backward(
        query_low, all_kv, d_attended, lse, local_groups=local_groups, chunk=half_rows,
        **mask_args,
    )
    d_kv_own = permute_scatter(jnp.concatenate([d_key_all, d_value_all], axis=1), "dp")
    d_key_own = d_kv_own[:, :kv_width]
    d_value_own = d_kv_own[:, kv_width:]
    d_queries = d_queries.reshape(row_count, local_heads, HEAD_DIM)
    d_query_low = (
        rotate(d_queries, cos_table, -sin_table)
        .reshape(row_count, local_heads * HEAD_DIM)
        .astype(jnp.bfloat16)
    )
    d_key_low = (
        rotate(d_key_own.reshape(row_count, local_groups, HEAD_DIM), cos_table, -sin_table)
        .reshape(row_count, local_groups * HEAD_DIM)
        .astype(jnp.bfloat16)
    )
    d_value_low = d_value_own.astype(jnp.bfloat16)
    grad_w_query = left_trans(normed, d_query_low)
    grad_w_key = left_trans(normed, d_key_low)
    grad_w_value = left_trans(normed, d_value_low)
    d_normed_part = (
        right_trans(d_query_low, w_query)
        + right_trans(d_key_low, w_key)
        + right_trans(d_value_low, w_value)
    )
    unit_normed = source * lax.rsqrt(jnp.mean(source * source, axis=-1, keepdims=True) + EPS)
    grad_gain_one = jnp.sum(d_normed_part * unit_normed, axis=0)
    (
        down_sum,
        d_normed_part,
        grad_gain_one,
        grad_w_out,
        grad_w_query,
        grad_w_key,
        grad_w_value,
    ) = lax.optimization_barrier(
        (down_sum, d_normed_part, grad_gain_one, grad_w_out, grad_w_query, grad_w_key, grad_w_value)
    )
    (
        grad_w_gate,
        grad_w_up,
        grad_w_down,
        grad_w_out,
        grad_w_query,
        grad_w_key,
        grad_w_value,
    ) = lax.optimization_barrier(
        (grad_w_gate, grad_w_up, grad_w_down, grad_w_out, grad_w_query, grad_w_key, grad_w_value)
    )
    grad_w_out, grad_w_query, grad_w_key, grad_w_value = dp_sum(
        [grad_w_out, grad_w_query, grad_w_key, grad_w_value]
    )
    grad_w_gate, grad_w_up, grad_w_down = [
        grad.astype(jnp.float32) for grad in (grad_w_gate, grad_w_up, grad_w_down)
    ]
    output = (middle + keep_rows * down_sum).astype(jnp.bfloat16)
    grad_gain_one = permute_allsum(permute_allsum(grad_gain_one, "dp"), "tensor")
    (d_normed,) = permute_sum([d_normed_part], [0], "tensor")
    d_source_norm, _ = norm_one_back(d_normed)
    grad_input = grad_middle + d_source_norm
    grad_gain_two = permute_allsum(grad_gain_two, "dp")
    grad_w_out, grad_w_query, grad_w_key, grad_w_value = [
        grad.astype(jnp.float32) for grad in (grad_w_out, grad_w_query, grad_w_key, grad_w_value)
    ]
    return (
        output,
        grad_input,
        grad_gain_one,
        grad_w_query,
        grad_w_key,
        grad_w_value,
        grad_w_out,
        grad_gain_two,
        grad_w_gate,
        grad_w_up,
        grad_w_down,
    )


def solution(mesh):
    placed = (
        P("dp", None),
        P("dp"),
        P(),
        P(),
        P(None, "tensor"),
        P(None, "tensor"),
        P(None, "tensor"),
        P("tensor", None),
        P(),
        P(None, "tensor"),
        P(None, "tensor"),
        P("tensor", None),
        P("dp", None),
    )
    return jax.shard_map(
        on_device,
        mesh=mesh,
        in_specs=placed,
        out_specs=(
            P("dp", None),
            P("dp", None),
            P(),
            P(None, "tensor"),
            P(None, "tensor"),
            P(None, "tensor"),
            P("tensor", None),
            P(),
            P(None, "tensor"),
            P(None, "tensor"),
            P("tensor", None),
        ),
        check_vma=False,
    )
```

```python
import functools

import jax
import jax.numpy as jnp
from jax import lax
from jax.experimental import pallas as pl
from jax.experimental.pallas import tpu as pltpu
from jax.sharding import PartitionSpec as P


HEAD_DIM = 128


EPS = 1e-05
MASKED_SCORE = -1e30


def rms_norm(values, scales):
    return values * lax.rsqrt(jnp.mean(values * values, axis=-1, keepdims=True) + EPS) * scales


def rotate(values, cos_table, sin_table):
    middle = values.shape[-1] // 2
    leading = values[..., :middle]
    trailing = values[..., middle:]
    return jnp.concatenate(
        [leading * cos_table - trailing * sin_table, trailing * cos_table + leading * sin_table],
        axis=-1,
    )


def angles_of(positions, head_size):
    frequency = 10000.0 ** (-jnp.arange(0, head_size, 2, dtype=jnp.float32) / head_size)
    angles = positions.astype(jnp.float32)[:, None] * frequency[None, :]
    return (jnp.cos(angles)[:, None, :], jnp.sin(angles)[:, None, :])


def swiglu(gate_value, up_value):
    return jax.nn.silu(gate_value) * up_value


def left_trans(left, right):
    return lax.dot_general(
        left, right, (((0,), (0,)), ((), ())), preferred_element_type=jnp.float32
    )


def right_trans(left, right):
    return lax.dot_general(
        left, right, (((1,), (1,)), ((), ())), preferred_element_type=jnp.float32
    )


def _allowed(qpos, own, kpos, kalive, start, width):
    slots = lax.broadcasted_iota(jnp.int32, (1, width), 1) + start
    return (kpos <= qpos) & ((kalive > 0) | (slots == own))


def _attn_bwd_kernel(
    chunk_ref, qblock_ref, q_ref, k_ref, v_ref, do_ref, lse_ref, qpos_ref, own_ref, kpos_ref,
    kalive_ref, dq_ref, dk_ref, dv_ref, delta_ref, dqacc_ref, *, heads, halves, chunk, chunks,
    scale,
):
    rows = q_ref.shape[0] // halves
    dk_ref[...] = jnp.zeros(dk_ref.shape, jnp.float32)
    dv_ref[...] = jnp.zeros(dv_ref.shape, jnp.float32)
    for head in range(heads):
        for half in range(halves):
            row_sl = pl.ds(half * rows, rows)
            col_sl = pl.ds(head * HEAD_DIM, HEAD_DIM)
            q = q_ref[row_sl, col_sl]
            do = do_ref[row_sl, col_sl]
            lse = lse_ref[head, row_sl, :]
            qpos = qpos_ref[row_sl, :]
            own = own_ref[row_sl, :]
            limit = qblock_ref[half]

            def probs_of(c):
                start = pl.multiple_of(c * chunk, chunk)
                k = k_ref[pl.ds(start, chunk), :]
                v = v_ref[pl.ds(start, chunk), :]
                s = lax.dot_general(
                    q, k, (((1,), (1,)), ((), ())), preferred_element_type=jnp.float32
                ) * scale
                ok = _allowed(
                    qpos, own, kpos_ref[:, pl.ds(start, chunk)],
                    kalive_ref[:, pl.ds(start, chunk)], start, chunk,
                )
                p = jnp.where(ok, jnp.exp(jnp.where(ok, s, MASKED_SCORE) - lse), 0.0)
                dp = lax.dot_general(
                    do, v, (((1,), (1,)), ((), ())), preferred_element_type=jnp.float32
                )
                return p, dp, k, start

            delta_ref[...] = jnp.zeros(delta_ref.shape, jnp.float32)

            def deltas(c, carry):
                @pl.when(chunk_ref[c] <= limit)
                def _():
                    p, dp, _, _ = probs_of(c)
                    delta_ref[...] += jnp.sum(p * dp, axis=1, keepdims=True)

                return carry

            lax.fori_loop(0, chunks, deltas, 0)
            delta = delta_ref[...]
            dqacc_ref[...] = jnp.zeros(dqacc_ref.shape, jnp.float32)

            def grads(c, carry):
                @pl.when(chunk_ref[c] <= limit)
                def _():
                    p, dp, k, start = probs_of(c)
                    ds = (p * (dp - delta)).astype(jnp.bfloat16)
                    dqacc_ref[...] += jnp.dot(ds, k, preferred_element_type=jnp.float32)
                    key_sl = pl.ds(start, chunk)
                    dk_ref[key_sl, :] += lax.dot_general(
                        ds, q, (((0,), (0,)), ((), ())), preferred_element_type=jnp.float32
                    ) * scale
                    dv_ref[key_sl, :] += lax.dot_general(
                        p.astype(jnp.bfloat16), do, (((0,), (0,)), ((), ())),
                        preferred_element_type=jnp.float32,
                    )

                return carry

            lax.fori_loop(0, chunks, grads, 0)
            dq_ref[row_sl, col_sl] = dqacc_ref[...] * scale


def _common(query_low, all_kv, local_groups):
    rows = query_low.shape[0]
    length = all_kv.shape[0]
    heads = query_low.shape[1] // HEAD_DIM // local_groups
    return rows, length, heads


def attention_backward(query_low, all_kv, d_attended, lse, chunk_blocks, query_blocks,
                       query_pos, own_ids, key_pos, key_alive, *, local_groups, chunk):
    rows, length, heads = _common(query_low, all_kv, local_groups)
    halves = 2
    chunks = length // chunk
    kernel = functools.partial(
        _attn_bwd_kernel, heads=heads, halves=halves, chunk=chunk, chunks=chunks,
        scale=HEAD_DIM ** (-0.5),
    )
    group_cols = heads * HEAD_DIM
    grid_spec = pltpu.PrefetchScalarGridSpec(
        num_scalar_prefetch=2,
        grid=(local_groups,),
        in_specs=[
            pl.BlockSpec((rows, group_cols), lambda g, *_: (0, g)),
            pl.BlockSpec((length, HEAD_DIM), lambda g, *_: (0, g)),
            pl.BlockSpec((length, HEAD_DIM), lambda g, *_: (0, local_groups + g)),
            pl.BlockSpec((rows, group_cols), lambda g, *_: (0, g)),
            pl.BlockSpec((heads, rows, 1), lambda g, *_: (g, 0, 0)),
            pl.BlockSpec((rows, 1), lambda g, *_: (0, 0)),
            pl.BlockSpec((rows, 1), lambda g, *_: (0, 0)),
            pl.BlockSpec((1, length), lambda g, *_: (0, 0)),
            pl.BlockSpec((1, length), lambda g, *_: (0, 0)),
        ],
        out_specs=[
            pl.BlockSpec((rows, group_cols), lambda g, *_: (0, g)),
            pl.BlockSpec((length, HEAD_DIM), lambda g, *_: (0, g)),
            pl.BlockSpec((length, HEAD_DIM), lambda g, *_: (0, g)),
        ],
        scratch_shapes=[
            pltpu.VMEM((rows // halves, 1), jnp.float32),
            pltpu.VMEM((rows // halves, HEAD_DIM), jnp.float32),
        ],
    )
    flops = 10 * rows * length * HEAD_DIM * heads * local_groups
    kv_width = local_groups * HEAD_DIM
    return pl.pallas_call(
        kernel,
        grid_spec=grid_spec,
        out_shape=[
            jax.ShapeDtypeStruct((rows, heads * local_groups * HEAD_DIM), jnp.float32),
            jax.ShapeDtypeStruct((length, kv_width), jnp.float32),
            jax.ShapeDtypeStruct((length, kv_width), jnp.float32),
        ],
        compiler_params=pltpu.CompilerParams(vmem_limit_bytes=48 * 1024 * 1024),
        cost_estimate=pl.CostEstimate(
            flops=flops, transcendentals=2 * rows * length * heads * local_groups,
            bytes_accessed=2 * length * 4 * HEAD_DIM * local_groups * 3,
        ),
    )(chunk_blocks, query_blocks, query_low, all_kv, all_kv, d_attended, lse, query_pos,
      own_ids, key_pos, key_alive)


def partner_perm(axis_size, mask):
    return [(index, index ^ mask) for index in range(axis_size)]


def permute_sum(parts, dims, axis):
    size = lax.axis_size(axis)
    steps = size.bit_length() - 1
    assert 1 << steps == size
    me = lax.axis_index(axis)
    pieces = list(parts)
    for step in range(steps):
        bit = (me >> step) & 1
        keep, send = [], []
        for piece, dim in zip(pieces, dims):
            half = piece.shape[dim] // 2
            keep.append(lax.dynamic_slice_in_dim(piece, bit * half, half, axis=dim))
            send.append(
                lax.dynamic_slice_in_dim(piece, (1 - bit) * half, half, axis=dim).astype(jnp.bfloat16)
            )
        got = lax.ppermute(send, axis, partner_perm(size, 1 << step))
        pieces = [mine + theirs.astype(jnp.float32) for mine, theirs in zip(keep, got)]
    pieces = [piece.astype(jnp.bfloat16) for piece in pieces]
    for step in reversed(range(steps)):
        first = ((me >> step) & 1) == 0
        got = lax.ppermute(pieces, axis, partner_perm(size, 1 << step))
        pieces = [
            jnp.concatenate(
                [jnp.where(first, mine, theirs), jnp.where(first, theirs, mine)], axis=dim
            )
            for mine, theirs, dim in zip(pieces, got, dims)
        ]
    return [piece.astype(jnp.float32) for piece in pieces]


def permute_scatter(value, axis):
    size = lax.axis_size(axis)
    steps = size.bit_length() - 1
    assert 1 << steps == size
    block = value.shape[0] // size

    def reverse(index):
        return int(format(index, f"0{steps}b")[::-1], 2) if steps else 0

    value = jnp.concatenate(
        [value[reverse(place) * block : (reverse(place) + 1) * block] for place in range(size)], axis=0
    )
    me = lax.axis_index(axis)
    for step in range(steps):
        bit = (me >> step) & 1
        half = value.shape[0] // 2
        keep = lax.dynamic_slice_in_dim(value, bit * half, half, axis=0)
        send = lax.dynamic_slice_in_dim(value, (1 - bit) * half, half, axis=0).astype(jnp.bfloat16)
        got = lax.ppermute(send, axis, partner_perm(size, 1 << step))
        value = keep.astype(jnp.float32) + got.astype(jnp.float32)
    return value


def permute_allsum(value, axis):
    size = lax.axis_size(axis)
    steps = size.bit_length() - 1
    for step in range(steps):
        value = value + lax.ppermute(value, axis, partner_perm(size, 1 << step))
    return value


def on_device(
    inputs,
    active,
    block_table,
    gain_one,
    w_query,
    w_key,
    w_value,
    w_out,
    gain_two,
    w_gate,
    w_up,
    w_down,
    cotangent,
):
    row_count = inputs.shape[0]
    local_heads = w_query.shape[1] // HEAD_DIM
    local_groups = w_key.shape[1] // HEAD_DIM
    group_size = local_heads // local_groups
    half_rows = row_count // 2
    length = row_count * lax.axis_size("dp")
    score_scale = HEAD_DIM ** (-0.5)
    key_pos = (
        block_table[:, None] * half_rows + jnp.arange(half_rows, dtype=jnp.int32)[None, :]
    ).reshape(length)
    row_start = lax.axis_index("dp") * row_count
    query_pos = lax.dynamic_slice_in_dim(key_pos, row_start, row_count)
    slot_ids = jnp.arange(length, dtype=jnp.int32)
    own_ids = row_start + jnp.arange(row_count, dtype=jnp.int32)
    cos_table, sin_table = angles_of(query_pos, HEAD_DIM)
    keep_rows = active.astype(jnp.float32)[:, None]
    source = inputs.astype(jnp.float32)
    normed_full, norm_one_back = jax.vjp(rms_norm, source, gain_one.astype(jnp.float32))
    normed = normed_full.astype(jnp.bfloat16)
    query_raw = jnp.dot(normed, w_query, preferred_element_type=jnp.float32).reshape(
        row_count, local_heads, HEAD_DIM
    )
    key_raw = jnp.dot(normed, w_key, preferred_element_type=jnp.float32).reshape(
        row_count, local_groups, HEAD_DIM
    )
    value_low = jnp.dot(normed, w_value, preferred_element_type=jnp.float32).astype(jnp.bfloat16)
    query_low = (
        rotate(query_raw, cos_table, sin_table)
        .reshape(row_count, local_heads * HEAD_DIM)
        .astype(jnp.bfloat16)
    )
    key_low = (
        rotate(key_raw, cos_table, sin_table)
        .reshape(row_count, local_groups * HEAD_DIM)
        .astype(jnp.bfloat16)
    )
    alive_low = active.astype(jnp.bfloat16)

    kv_width = local_groups * HEAD_DIM
    all_kv = lax.all_gather(
        jnp.concatenate([key_low, value_low], axis=1), "dp", axis=0, tiled=True
    )
    all_alive = lax.all_gather(alive_low, "dp", axis=0, tiled=True)
    mask_args = dict(
        chunk_blocks=block_table,
        query_blocks=lax.dynamic_slice_in_dim(block_table, 2 * lax.axis_index("dp"), 2),
        query_pos=query_pos[:, None],
        own_ids=own_ids[:, None],
        key_pos=key_pos[None, :],
        key_alive=(all_alive > 0).astype(jnp.int32)[None, :],
    )

    def allowed_of(alive_all):
        return (key_pos[None, :] <= query_pos[:, None]) & (
            (alive_all[None, :] > 0) | (slot_ids[None, :] == own_ids[:, None])
        )

    def head_scores(head_index, keys_all, allowed):
        query_part = query_low[:, head_index * HEAD_DIM : (head_index + 1) * HEAD_DIM]
        group_index = head_index // group_size
        key_part = keys_all[:, group_index * HEAD_DIM : (group_index + 1) * HEAD_DIM]
        raw_scores = right_trans(query_part, key_part) * score_scale
        return jnp.where(allowed, raw_scores, MASKED_SCORE)

    all_keys = all_kv[:, :kv_width]
    all_values = all_kv[:, kv_width:]
    allowed_fwd = allowed_of(all_alive)
    mixed_parts = []
    lse_parts = []
    for head_index in range(local_heads):
        masked = head_scores(head_index, all_keys, allowed_fwd)
        row_max = jnp.max(masked, axis=1, keepdims=True)
        shifted = jnp.exp(masked - row_max)
        row_total = jnp.sum(shifted, axis=1, keepdims=True)
        probs_low = (shifted / row_total).astype(jnp.bfloat16)
        lse_parts.append(row_max + jnp.log(row_total))
        group_index = head_index // group_size
        value_part = all_values[:, group_index * HEAD_DIM : (group_index + 1) * HEAD_DIM]
        mixed_parts.append(jnp.dot(probs_low, value_part, preferred_element_type=jnp.float32))
    attended = jnp.concatenate(mixed_parts, axis=1).astype(jnp.bfloat16)
    lse = jnp.stack(lse_parts)
    branch_part = jnp.dot(attended, w_out, preferred_element_type=jnp.float32)
    sc_rows = row_count * 5 // 8
    branch_top = lax.psum(branch_part[:sc_rows].astype(jnp.bfloat16), "tensor")
    (branch_bottom,) = permute_sum([branch_part[sc_rows:]], [0], "tensor")
    branch = jnp.concatenate([branch_top.astype(jnp.float32), branch_bottom], axis=0)
    middle = source + keep_rows * branch
    normed_two_full, norm_two_back = jax.vjp(rms_norm, middle, gain_two.astype(jnp.float32))
    normed_two = normed_two_full.astype(jnp.bfloat16)
    gate_value = jnp.dot(normed_two, w_gate, preferred_element_type=jnp.float32)
    up_value = jnp.dot(normed_two, w_up, preferred_element_type=jnp.float32)
    hidden_full, swiglu_back = jax.vjp(swiglu, gate_value, up_value)
    hidden = hidden_full.astype(jnp.bfloat16)
    down_part = jnp.dot(hidden, w_down, preferred_element_type=jnp.float32)
    grad_out = cotangent.astype(jnp.float32)

    def dp_sum(grads):
        return [lax.psum(grad.astype(jnp.bfloat16), "dp") for grad in grads]

    d_down = (keep_rows * grad_out).astype(jnp.bfloat16)
    grad_w_down = left_trans(hidden, d_down)
    d_hidden = right_trans(d_down, w_down)
    d_gate_full, d_up_full = swiglu_back(d_hidden)
    d_gate = d_gate_full.astype(jnp.bfloat16)
    d_up = d_up_full.astype(jnp.bfloat16)
    grad_w_gate = left_trans(normed_two, d_gate)
    grad_w_up = left_trans(normed_two, d_up)
    d_normed_two_part = right_trans(d_gate, w_gate) + right_trans(d_up, w_up)
    grad_w_gate, grad_w_up, grad_w_down, d_normed_two_part = lax.optimization_barrier(
        (grad_w_gate, grad_w_up, grad_w_down, d_normed_two_part)
    )
    mlp_grads = dp_sum([grad_w_gate, grad_w_up, grad_w_down])
    grad_w_gate, grad_w_up, grad_w_down = mlp_grads
    (d_normed_two,) = permute_sum([d_normed_two_part], [0], "tensor")
    down_part, d_normed_two = lax.optimization_barrier((down_part, d_normed_two))
    (down_sum,) = permute_sum([down_part], [0], "tensor")
    d_middle_norm, grad_gain_two = norm_two_back(d_normed_two)
    grad_middle = grad_out + d_middle_norm
    d_branch = (keep_rows * grad_middle).astype(jnp.bfloat16)
    grad_w_out = left_trans(attended, d_branch)
    grad_w_gate, grad_w_up, grad_w_down, grad_w_out = lax.optimization_barrier(
        (grad_w_gate, grad_w_up, grad_w_down, grad_w_out)
    )
    d_attended = right_trans(d_branch, w_out).astype(jnp.bfloat16)
    d_queries, d_key_all, d_value_all = attention_backward(
        query_low, all_kv, d_attended, lse, local_groups=local_groups, chunk=half_rows,
        **mask_args,
    )
    d_kv_own = permute_scatter(jnp.concatenate([d_key_all, d_value_all], axis=1), "dp")
    d_kv_own, grad_w_out = lax.optimization_barrier((d_kv_own, grad_w_out))
    d_key_own = d_kv_own[:, :kv_width]
    d_value_own = d_kv_own[:, kv_width:]
    d_queries = d_queries.reshape(row_count, local_heads, HEAD_DIM)
    d_query_low = (
        rotate(d_queries, cos_table, -sin_table)
        .reshape(row_count, local_heads * HEAD_DIM)
        .astype(jnp.bfloat16)
    )
    d_key_low = (
        rotate(d_key_own.reshape(row_count, local_groups, HEAD_DIM), cos_table, -sin_table)
        .reshape(row_count, local_groups * HEAD_DIM)
        .astype(jnp.bfloat16)
    )
    d_value_low = d_value_own.astype(jnp.bfloat16)
    grad_w_query = left_trans(normed, d_query_low)
    grad_w_key = left_trans(normed, d_key_low)
    grad_w_value = left_trans(normed, d_value_low)
    d_normed_part = (
        right_trans(d_query_low, w_query)
        + right_trans(d_key_low, w_key)
        + right_trans(d_value_low, w_value)
    )
    unit_normed = source * lax.rsqrt(jnp.mean(source * source, axis=-1, keepdims=True) + EPS)
    grad_gain_one = jnp.sum(d_normed_part * unit_normed, axis=0)
    (
        down_sum,
        d_normed_part,
        grad_gain_one,
        grad_w_out,
        grad_w_query,
        grad_w_key,
        grad_w_value,
    ) = lax.optimization_barrier(
        (down_sum, d_normed_part, grad_gain_one, grad_w_out, grad_w_query, grad_w_key, grad_w_value)
    )
    grad_w_out, grad_w_query, grad_w_key, grad_w_value = dp_sum(
        [grad_w_out, grad_w_query, grad_w_key, grad_w_value]
    )
    grad_w_gate, grad_w_up, grad_w_down = [
        grad.astype(jnp.float32) for grad in (grad_w_gate, grad_w_up, grad_w_down)
    ]
    output = (middle + keep_rows * down_sum).astype(jnp.bfloat16)
    grad_gain_one = permute_allsum(permute_allsum(grad_gain_one, "dp"), "tensor")
    (d_normed,) = permute_sum([d_normed_part], [0], "tensor")
    d_source_norm, _ = norm_one_back(d_normed)
    grad_input = grad_middle + d_source_norm
    grad_gain_two = permute_allsum(grad_gain_two, "dp")
    grad_w_out, grad_w_query, grad_w_key, grad_w_value = [
        grad.astype(jnp.float32) for grad in (grad_w_out, grad_w_query, grad_w_key, grad_w_value)
    ]
    return (
        output,
        grad_input,
        grad_gain_one,
        grad_w_query,
        grad_w_key,
        grad_w_value,
        grad_w_out,
        grad_gain_two,
        grad_w_gate,
        grad_w_up,
        grad_w_down,
    )


def solution(mesh):
    placed = (
        P("dp", None),
        P("dp"),
        P(),
        P(),
        P(None, "tensor"),
        P(None, "tensor"),
        P(None, "tensor"),
        P("tensor", None),
        P(),
        P(None, "tensor"),
        P(None, "tensor"),
        P("tensor", None),
        P("dp", None),
    )
    return jax.shard_map(
        on_device,
        mesh=mesh,
        in_specs=placed,
        out_specs=(
            P("dp", None),
            P("dp", None),
            P(),
            P(None, "tensor"),
            P(None, "tensor"),
            P(None, "tensor"),
            P("tensor", None),
            P(),
            P(None, "tensor"),
            P(None, "tensor"),
            P("tensor", None),
        ),
        check_vma=False,
    )
```
